32 devices in a mesh: gx: 8 (over z, x), gy: 4 (over y, core).
Axes of the slice: x: 2, y: 2, z: 4, core: 2. Of those that a mesh axis runs over, the one named last changes fastest.
Arguments:
- right_side: float32 [8, 4, 2048], P('gx', 'gy'), may hold values from -18 to 18
- coarse_matrix: float32 [8, 4, 384, 384], P('gx', 'gy'), may hold values from -2.4 to 48, as said below
- coarse_order: int32 [8, 4], P('gx', 'gy'), may hold values from 256 to 384, as said below
- diag_blocks: bfloat16 [8, 4, 16, 128, 128], P('gx', 'gy'), may hold values from -0.7 to 8.7, as said below
- couple_blocks: bfloat16 [8, 4, 16, 2, 128, 128], P('gx', 'gy'), may hold values from -0.059814453 to 0.059814453
- block_pattern: int32 [8, 4, 16, 2], P('gx', 'gy'), may hold values from 0 to 15
- tissue_labels: int32 [8, 4, 16], P('gx', 'gy'), may hold values from 0 to 2
- precond_blocks: bfloat16 [8, 4, 16, 128, 128], P('gx', 'gy'), may hold values from -0.02 to 0.14, as said below
- coarse_basis: bfloat16 [8, 4, 2048, 384], P('gx', 'gy'), may hold values from -0.059814453 to 0.059814453
- face_map: int32 [8, 4, 4, 512], P('gx', 'gy'), may hold values from 0 to 2047, as said below
Outputs:
- adjoint: float32 [8, 4, 2048], P('gx', 'gy')
- residual: float32 [8, 4, 2048], P('gx', 'gy')
The draws below stay inside these ranges and needn't reach their ends.
Inputs may be any that keep to these rules, and one draw needn't show every extreme that they name: `coarse_matrix`: symmetric positive definite. `coarse_order`: some subdomain has order exactly 384 and some exactly 256. `diag_blocks`: each block is symmetric. `precond_blocks`: each block is symmetric. `face_map`: the entries of one face are distinct.
All inputs are finite; a program needn't handle non-finite values.
Results may differ from the reference program's by a relative error of at most 0.0065.
The reference program's roundings to bfloat16 on the way count: a program that leaves them out, or rounds other values in their place, can miss the bound.
Values sent between devices are 32-bit elements; how exact they have to be, the bound alone decides.
No kernel may reach another device: no remote copies, remote signals or barrier semaphores. Data moves between devices by JAX's collectives and lax.ppermute only.
A program may use at most 128 MiB of HBM per device.

```python
import jax
import jax.numpy as jnp
from jax import lax

NB = 16
BS = 128
KOFF = 2
CMAX = 384
CMIN = 256
FACE = 512
ITERS = 2
GRID_X = 8
GRID_Y = 4


def symmetric_noise(key, dims_full, spread, limit):
    raw = jnp.clip(jax.random.normal(key, dims_full, jnp.float32), -limit, limit) * spread
    return (raw + jnp.swapaxes(raw, -1, -2)) * 0.7071


def draw_right_side(key, part):
    ramp = 1.0 + 2.0 * jnp.arange(GRID_X, dtype=jnp.float32) / max(GRID_X - 1, 1)
    dims_full = (GRID_X, GRID_Y, NB * BS)
    values = jnp.clip(jax.random.normal(key, dims_full, jnp.float32), -6.0, 6.0)
    return values * ramp[:, None, None]


def draw_coarse_matrix(key, part):
    position = jnp.arange(GRID_X, dtype=jnp.float32) / max(GRID_X - 1, 1)
    ramp = 1.0 + 2.0 * position
    level = 0.5 * GRID_X * ramp[:, None, None, None]
    noise = symmetric_noise(key, (GRID_X, GRID_Y, CMAX, CMAX), 0.008, 4.0)
    return level * (noise + jnp.eye(CMAX, dtype=jnp.float32))


def draw_diag_blocks(key, part):
    noise = symmetric_noise(key, (GRID_X, GRID_Y, NB, BS, BS), 0.1, 4.0)
    return (noise + 8.0 * jnp.eye(BS, dtype=jnp.float32)).astype(jnp.bfloat16)


def draw_precond_blocks(key, part):
    noise = symmetric_noise(key, (GRID_X, GRID_Y, NB, BS, BS), 0.002, 4.0)
    return (noise + 0.125 * jnp.eye(BS, dtype=jnp.float32)).astype(jnp.bfloat16)


def draw_coarse_order(key, part):
    device_count = GRID_X * GRID_Y
    orders = jax.random.randint(jax.random.fold_in(key, 11), (device_count,), CMIN, CMAX + 1)
    spots = jax.random.permutation(jax.random.fold_in(key, 12), device_count)
    orders = orders.at[spots[0]].set(CMAX).at[spots[1]].set(CMIN)
    return orders.reshape(GRID_X, GRID_Y).astype(jnp.int32)


def draw_face_map(key, part):
    subkeys = jax.random.split(key, GRID_X * GRID_Y * 4)

    def pick_face(subkey):
        return jax.random.permutation(subkey, NB * BS)[:FACE]
    picks = jax.vmap(pick_face)(subkeys)
    return picks.reshape(GRID_X, GRID_Y, 4, FACE).astype(jnp.int32)


def with_ends(drawn, own_key, smallest, largest):
    longest = drawn.shape.index(max(drawn.shape))
    spots = []
    for shift in (0, 1):
        where = [jax.random.randint(jax.random.fold_in(own_key, axis), (), 0, length) for axis, length in enumerate(drawn.shape)]
        where[longest] = (where[longest] + shift) % drawn.shape[longest]
        spots.append(tuple(where))
    return drawn.at[spots[0]].set(smallest).at[spots[1]].set(largest)


def levels(own_key, shape, cuts, low, largest):
    factor_of = 1.0
    for dim, blocks in cuts:
        draws = jax.random.uniform(jax.random.fold_in(jax.random.fold_in(own_key, 6), dim), (blocks,), jnp.float32, low / len(cuts), largest / len(cuts))
        factor_of = factor_of * jnp.repeat(jnp.exp(draws), shape[dim] // blocks).reshape((-1,) + (1,) * (len(shape) - 1 - dim))
    return factor_of


def bell_draw(stream_key, dims, scale, bound, cuts=(), held_as=jnp.bfloat16):
    drawn = scale * jax.random.normal(stream_key, dims, jnp.float32)
    if cuts:
        drawn = drawn * levels(stream_key, dims, cuts, -0.22, 0.18)
    return jnp.clip(drawn, -bound, bound).astype(held_as)


def setup_inputs(seed: int = 0) -> dict:
    key_of = jax.random.split(jax.random.key(seed), 11)
    return {
        "right_side": draw_right_side(jax.random.fold_in(key_of[10], 71), 0),
        "coarse_matrix": draw_coarse_matrix(jax.random.fold_in(key_of[10], 71), 0),
        "coarse_order": draw_coarse_order(jax.random.fold_in(key_of[10], 71), 0),
        "diag_blocks": draw_diag_blocks(jax.random.fold_in(key_of[10], 71), 0),
        "couple_blocks": bell_draw(key_of[4], (GRID_X, GRID_Y, NB, KOFF, BS, BS), 0.01, 0.059814453, ((0, 8), (1, 4))),
        "block_pattern": with_ends(jax.random.randint(key_of[5], (GRID_X, GRID_Y, NB, KOFF), 0, NB), jax.random.fold_in(key_of[5], 1), 0, NB - 1).astype(jnp.int32),
        "tissue_labels": with_ends(jax.random.randint(key_of[6], (GRID_X, GRID_Y, NB), 0, 3), jax.random.fold_in(key_of[6], 1), 0, 2).astype(jnp.int32),
        "precond_blocks": draw_precond_blocks(jax.random.fold_in(key_of[10], 71), 0),
        "coarse_basis": bell_draw(key_of[8], (GRID_X, GRID_Y, NB * BS, CMAX), (0.5 / (NB * BS * CMAX * GRID_X) ** 0.25), 0.059814453, ((0, 8), (1, 4))),
        "face_map": draw_face_map(jax.random.fold_in(key_of[10], 71), 0),
    }


STIFFNESS = (1.0, 0.6, 2.0)
COUPLING = 0.5
NEWTON_STEPS = 4


def material_scale(tissue_labels):
    return jnp.where(tissue_labels == 0, STIFFNESS[0], jnp.where(tissue_labels == 1, STIFFNESS[1], STIFFNESS[2])).astype(jnp.float32)


def masked_coarse(matrix, coarse_order):
    live_cols = (jnp.arange(matrix.shape[-1]) < coarse_order).astype(jnp.float32)
    live_pairs = live_cols[:, None] * live_cols[None, :]
    return matrix * live_pairs + jnp.diag(jnp.diagonal(matrix) * (1.0 - live_cols))


def newton_inverse(matrix):
    order_size = matrix.shape[-1]
    identity = jnp.eye(order_size, dtype=jnp.float32)
    approx = jnp.diag(1.0 / jnp.diagonal(matrix))
    for sweep in range(NEWTON_STEPS):
        product = jnp.dot(matrix, approx, precision=lax.Precision.HIGHEST)
        approx = jnp.dot(approx, 2.0 * identity - product, precision=lax.Precision.HIGHEST)
    return approx


def parallel_sum(left_term, right_term):
    inverse = newton_inverse(left_term + right_term)
    middle = jnp.dot(inverse, left_term, precision=lax.Precision.HIGHEST)
    return left_term - jnp.dot(left_term, middle, precision=lax.Precision.HIGHEST)


def over_devices(function, *arrays):
    def per_row(grouped):
        return jax.vmap(function)(*grouped)
    return lax.map(per_row, arrays)


def block_apply(vector, diag_blocks, couple_blocks, block_pattern, tissue_labels):
    block_count, block_size = diag_blocks.shape[0], diag_blocks.shape[1]
    rounded = vector.astype(jnp.bfloat16).astype(jnp.float32).reshape(block_count, block_size)
    result = material_scale(tissue_labels)[:, None] * jnp.einsum("rij,rj->ri", diag_blocks.astype(jnp.float32), rounded, precision=lax.Precision.HIGHEST)
    couples = couple_blocks.astype(jnp.float32)
    gathered = rounded[block_pattern]
    result = result + jnp.einsum("rkij,rkj->ri", couples, gathered, precision=lax.Precision.HIGHEST)
    backward = jnp.einsum("rkij,ri->rkj", couples, rounded, precision=lax.Precision.HIGHEST)
    result = result + jax.ops.segment_sum(backward.reshape(-1, block_size), block_pattern.reshape(-1), num_segments=block_count)
    return result.reshape(-1)


def gather_faces(vector, face_map):
    return vector[face_map]


def add_faces(result, face_map, received):
    return result.at[face_map.reshape(-1)].add(-COUPLING * received.reshape(-1))


def local_precondition(rounded, precond_blocks, tissue_labels):
    block_count, block_size = precond_blocks.shape[0], precond_blocks.shape[1]
    product = jnp.einsum("rij,rj->ri", precond_blocks.astype(jnp.float32), rounded.astype(jnp.float32).reshape(block_count, block_size), precision=lax.Precision.HIGHEST)
    return (product / material_scale(tissue_labels)[:, None]).reshape(-1)


def project_basis(rounded, coarse_basis):
    return jnp.dot(rounded, coarse_basis, preferred_element_type=jnp.float32)


def lift_basis(coarse_basis, weights):
    return jnp.dot(coarse_basis, weights, preferred_element_type=jnp.float32)


def solve_column(compliance, summed):
    return jnp.dot(compliance, summed, precision=lax.Precision.HIGHEST)


def reference(right_side, coarse_matrix, coarse_order, diag_blocks, couple_blocks, block_pattern, tissue_labels, precond_blocks, coarse_basis, face_map):
    live_cols = (jnp.arange(CMAX)[None, None, :] < coarse_order[:, :, None]).astype(jnp.float32)
    pending = over_devices(masked_coarse, coarse_matrix, coarse_order)
    while pending.shape[0] > 1:
        pair_count = pending.shape[0] // 2
        merged = jax.vmap(jax.vmap(parallel_sum))(pending[0:2 * pair_count:2], pending[1:2 * pair_count:2])
        if pending.shape[0] % 2 == 1:
            merged = jnp.concatenate([merged, pending[-1:]], axis=0)
        pending = merged
    compliance = jax.vmap(newton_inverse)(pending[0])

    def operate(vector):
        result = over_devices(block_apply, vector, diag_blocks, couple_blocks, block_pattern, tissue_labels)
        values = over_devices(gather_faces, vector, face_map)
        empty_row = jnp.zeros_like(values[:1, :, 0])
        empty_col = jnp.zeros_like(values[:, :1, 0])
        from_west = jnp.concatenate([empty_row, values[:-1, :, 1]], axis=0)
        from_east = jnp.concatenate([values[1:, :, 0], empty_row], axis=0)
        from_south = jnp.concatenate([empty_col, values[:, :-1, 3]], axis=1)
        from_north = jnp.concatenate([values[:, 1:, 2], empty_col], axis=1)
        received = jnp.stack([from_west, from_east, from_south, from_north], axis=2)
        return over_devices(add_faces, result, face_map, received)

    def precondition(residual_now):
        rounded = residual_now.astype(jnp.bfloat16)
        local_part = over_devices(local_precondition, rounded, precond_blocks, tissue_labels)
        coarse_load = over_devices(project_basis, rounded, coarse_basis) * live_cols
        summed = jnp.sum(coarse_load, axis=0)
        solved = jax.vmap(solve_column)(compliance, summed)
        weights = (solved[None] * live_cols).astype(jnp.bfloat16)
        return local_part + over_devices(lift_basis, coarse_basis, weights)

    adjoint = jnp.zeros_like(right_side)
    residual = right_side
    precond = precondition(residual)
    precond_dot = jnp.sum(residual * precond)
    direction = precond
    for iteration in range(ITERS):
        applied = operate(direction)
        step_size = precond_dot / jnp.sum(direction * applied)
        adjoint = adjoint + step_size * direction
        residual = residual - step_size * applied
        if iteration + 1 < ITERS:
            precond = precondition(residual)
            dot_next = jnp.sum(residual * precond)
            direction = precond + (dot_next / precond_dot) * direction
            precond_dot = dot_next
    return adjoint, residual
```

```python
import jax
import jax.numpy as jnp
from jax import lax
from jax.sharding import PartitionSpec as P

ITERS = 2


STIFFNESS = (1.0, 0.6, 2.0)
COUPLING = 0.5
NEWTON_STEPS = 4


def is_power_of_two(count):
    return count > 0 and (count & (count - 1)) == 0


def butterfly_sum(value, axes):
    for axis in axes:
        count = lax.axis_size(axis)
        if not is_power_of_two(count):
            value = lax.psum(value, axis)
            continue
        stride = 1
        while stride < count:
            pairs = [(i, i ^ stride) for i in range(count)]
            value = value + lax.ppermute(value, axis, pairs)
            stride *= 2
    return value


def extended(block, sides, width):
    for axis, dim in sides:
        count = lax.axis_size(axis)
        forward = [(i, i + 1) for i in range(count - 1)]
        backward = [(target, source) for source, target in forward]
        low = lax.ppermute(
            lax.slice_in_dim(block, block.shape[dim] - width, None, axis=dim), axis, forward
        )
        high = lax.ppermute(lax.slice_in_dim(block, 0, width, axis=dim), axis, backward)
        block = jnp.concatenate([low, block, high], axis=dim)
    return block


def merged_chain(part, axis, combine):
    gathered = lax.all_gather(part, axis)

    def take(source):
        return lax.dynamic_index_in_dim(gathered, source, 0, False)

    return lax.fori_loop(
        1, lax.axis_size(axis), lambda source, state: combine(state, take(source)), take(0)
    )


def merged_tree(part, axis, combine):
    count = lax.axis_size(axis)
    if not is_power_of_two(count):
        return merged_chain(part, axis, combine)
    index = lax.axis_index(axis)
    stride = 1
    while stride < count:
        pairs = [(i, i ^ stride) for i in range(count)]
        other = lax.ppermute(part, axis, pairs)
        upper = (index & stride) != 0
        lower_term = jnp.where(upper, other, part)
        upper_term = jnp.where(upper, part, other)
        part = combine(lower_term, upper_term)
        stride *= 2
    return part


def material_scale(tissue_labels):
    return jnp.where(
        tissue_labels == 0, STIFFNESS[0], jnp.where(tissue_labels == 1, STIFFNESS[1], STIFFNESS[2])
    ).astype(jnp.float32)


def identity_mask(order_size):
    index = jnp.arange(order_size)
    return index[:, None] == index[None, :]


def diagonal_of(matrix):
    eye = identity_mask(matrix.shape[-1])
    return jnp.sum(jnp.where(eye, matrix, 0.0), axis=1)


def masked_coarse(matrix, coarse_order):
    order_size = matrix.shape[-1]
    live = jnp.arange(order_size) < coarse_order
    keep = (live[:, None] & live[None, :]) | identity_mask(order_size)
    return jnp.where(keep, matrix, 0.0)


def newton_inverse(matrix):
    order_size = matrix.shape[-1]
    eye = identity_mask(order_size)
    identity = eye.astype(jnp.float32)
    recip = 1.0 / diagonal_of(matrix)
    product = matrix * recip[None, :]
    approx = recip[:, None] * (2.0 * identity - product)
    for sweep in range(1, NEWTON_STEPS):
        product = jnp.dot(matrix, approx, precision=lax.Precision.HIGHEST)
        approx = jnp.dot(approx, 2.0 * identity - product, precision=lax.Precision.HIGHEST)
    return approx


def parallel_sum(left_term, right_term):
    inverse = newton_inverse(left_term + right_term)
    middle = jnp.dot(inverse, left_term, precision=lax.Precision.HIGHEST)
    return left_term - jnp.dot(left_term, middle, precision=lax.Precision.HIGHEST)


def block_apply(vector, diag_blocks, couple_blocks, block_pattern, tissue_labels):
    block_count, block_size = (diag_blocks.shape[0], diag_blocks.shape[1])
    rounded = vector.astype(jnp.bfloat16).reshape(block_count, block_size)
    result = material_scale(tissue_labels)[:, None] * jnp.einsum(
        "rij,rj->ri", diag_blocks, rounded, preferred_element_type=jnp.float32
    )
    gathered = rounded[block_pattern]
    result = result + jnp.einsum(
        "rkij,rkj->ri", couple_blocks, gathered, preferred_element_type=jnp.float32
    )
    backward = jnp.einsum(
        "rkij,ri->rkj", couple_blocks, rounded, preferred_element_type=jnp.float32
    )
    onehot = (block_pattern.reshape(-1)[:, None] == jnp.arange(block_count)[None, :]).astype(
        jnp.float32
    )
    result = result + jnp.einsum(
        "mc,mj->cj", onehot, backward.reshape(-1, block_size), precision=lax.Precision.HIGHEST
    )
    return result.reshape(-1)


def operate(vector, diag_blocks, couple_blocks, block_pattern, tissue_labels, face_map):
    result = block_apply(vector, diag_blocks, couple_blocks, block_pattern, tissue_labels)
    values = vector[face_map]
    across = extended(values[0:2], (("gx", 0),), 1)
    upward = extended(values[2:4], (("gy", 0),), 1)
    received = jnp.stack([across[0], across[3], upward[0], upward[3]])
    return result.at[face_map.reshape(-1)].add(-COUPLING * received.reshape(-1))


def precondition(residual, precond_blocks, tissue_labels, coarse_basis, live_cols, compliance):
    block_count, block_size = (precond_blocks.shape[0], precond_blocks.shape[1])
    rounded = residual.astype(jnp.bfloat16)
    product = jnp.einsum(
        "rij,rj->ri",
        precond_blocks,
        rounded.reshape(block_count, block_size),
        preferred_element_type=jnp.float32,
    )
    local_part = (product / material_scale(tissue_labels)[:, None]).reshape(-1)
    coarse_load = jnp.dot(rounded, coarse_basis, preferred_element_type=jnp.float32) * live_cols
    summed = butterfly_sum(coarse_load, ("gx",))
    solved = jnp.dot(compliance, summed, precision=lax.Precision.HIGHEST)
    weights = (solved * live_cols).astype(jnp.bfloat16)
    return local_part + jnp.dot(coarse_basis, weights, preferred_element_type=jnp.float32)


def global_sum(value):
    return butterfly_sum(value, ("gy", "gx"))


def body(
    right_side,
    coarse_matrix,
    coarse_order,
    diag_blocks,
    couple_blocks,
    block_pattern,
    tissue_labels,
    precond_blocks,
    coarse_basis,
    face_map,
):
    source = right_side[0, 0]
    matrix = coarse_matrix[0, 0]
    order_here = coarse_order[0, 0]
    diagonal = diag_blocks[0, 0]
    couples = couple_blocks[0, 0]
    pattern = block_pattern[0, 0]
    labels = tissue_labels[0, 0]
    inverses = precond_blocks[0, 0]
    basis = coarse_basis[0, 0]
    faces = face_map[0, 0]
    order_size = matrix.shape[-1]
    live_cols = (jnp.arange(order_size) < order_here).astype(jnp.float32)
    masked = masked_coarse(matrix, order_here)
    merged = merged_tree(masked, "gx", parallel_sum)
    compliance = newton_inverse(merged)
    adjoint = jnp.zeros_like(source)
    residual = source
    precond = precondition(residual, inverses, labels, basis, live_cols, compliance)
    precond_dot = jnp.sum(residual * precond)
    direction = precond
    for iteration in range(ITERS):
        applied = operate(direction, diagonal, couples, pattern, labels, faces)
        curvature = jnp.sum(direction * applied)
        if iteration == 0:
            both = global_sum(jnp.stack([precond_dot, curvature]))
            precond_dot, curvature = both[0], both[1]
        else:
            curvature = global_sum(curvature)
        step_size = precond_dot / curvature
        adjoint = adjoint + step_size * direction
        residual = residual - step_size * applied
        if iteration + 1 < ITERS:
            precond = precondition(residual, inverses, labels, basis, live_cols, compliance)
            dot_next = global_sum(jnp.sum(residual * precond))
            direction = precond + dot_next / precond_dot * direction
            precond_dot = dot_next
    return (adjoint[None, None], residual[None, None])


def solution(mesh):
    in_specs = (
        P("gx", "gy", None),
        P("gx", "gy", None, None),
        P("gx", "gy"),
        P("gx", "gy", None, None, None),
        P("gx", "gy", None, None, None, None),
        P("gx", "gy", None, None),
        P("gx", "gy", None),
        P("gx", "gy", None, None, None),
        P("gx", "gy", None, None),
        P("gx", "gy", None, None),
    )
    out_specs = (P("gx", "gy", None), P("gx", "gy", None))
    return jax.shard_map(body, mesh=mesh, in_specs=in_specs, out_specs=out_specs, check_vma=False)
```

```python
import jax
import jax.numpy as jnp
from jax import lax
from jax.sharding import PartitionSpec as P

ITERS = 2


STIFFNESS = (1.0, 0.6, 2.0)
COUPLING = 0.5
NEWTON_STEPS = 4


def is_power_of_two(count):
    return count > 0 and (count & (count - 1)) == 0


def butterfly_sum(value, axes):
    for axis in axes:
        count = lax.axis_size(axis)
        if not is_power_of_two(count):
            value = lax.psum(value, axis)
            continue
        stride = 1
        while stride < count:
            pairs = [(i, i ^ stride) for i in range(count)]
            value = value + lax.ppermute(value, axis, pairs)
            stride *= 2
    return value


def extended(block, sides, width):
    for axis, dim in sides:
        count = lax.axis_size(axis)
        forward = [(i, i + 1) for i in range(count - 1)]
        backward = [(target, source) for source, target in forward]
        low = lax.ppermute(
            lax.slice_in_dim(block, block.shape[dim] - width, None, axis=dim), axis, forward
        )
        high = lax.ppermute(lax.slice_in_dim(block, 0, width, axis=dim), axis, backward)
        block = jnp.concatenate([low, block, high], axis=dim)
    return block


def merged_chain(part, axis, combine):
    gathered = lax.all_gather(part, axis)

    def take(source):
        return lax.dynamic_index_in_dim(gathered, source, 0, False)

    return lax.fori_loop(
        1, lax.axis_size(axis), lambda source, state: combine(state, take(source)), take(0)
    )


def merged_tree(part, axis, combine):
    count = lax.axis_size(axis)
    if not is_power_of_two(count):
        return merged_chain(part, axis, combine)
    index = lax.axis_index(axis)
    stride = 1
    while stride < count:
        pairs = [(i, i ^ stride) for i in range(count)]
        other = lax.ppermute(part, axis, pairs)
        upper = (index & stride) != 0
        lower_term = jnp.where(upper, other, part)
        upper_term = jnp.where(upper, part, other)
        part = combine(lower_term, upper_term)
        stride *= 2
    return part


def material_scale(tissue_labels):
    return jnp.where(
        tissue_labels == 0, STIFFNESS[0], jnp.where(tissue_labels == 1, STIFFNESS[1], STIFFNESS[2])
    ).astype(jnp.float32)


def identity_mask(order_size):
    index = jnp.arange(order_size)
    return index[:, None] == index[None, :]


def diagonal_of(matrix):
    eye = identity_mask(matrix.shape[-1])
    return jnp.sum(jnp.where(eye, matrix, 0.0), axis=1)


def masked_coarse(matrix, coarse_order):
    order_size = matrix.shape[-1]
    live = jnp.arange(order_size) < coarse_order
    keep = (live[:, None] & live[None, :]) | identity_mask(order_size)
    return jnp.where(keep, matrix, 0.0)


def newton_inverse(matrix):
    order_size = matrix.shape[-1]
    eye = identity_mask(order_size)
    identity = eye.astype(jnp.float32)
    recip = 1.0 / diagonal_of(matrix)
    product = matrix * recip[None, :]
    approx = recip[:, None] * (2.0 * identity - product)
    for sweep in range(1, NEWTON_STEPS):
        product = jnp.dot(matrix, approx, precision=lax.Precision.HIGHEST)
        approx = jnp.dot(approx, 2.0 * identity - product, precision=lax.Precision.HIGHEST)
    return approx


def parallel_sum(left_term, right_term):
    inverse = newton_inverse(left_term + right_term)
    middle = jnp.dot(inverse, left_term, precision=lax.Precision.HIGHEST)
    return left_term - jnp.dot(left_term, middle, precision=lax.Precision.HIGHEST)


def block_apply(vector, diag_blocks, couple_blocks, block_pattern, tissue_labels):
    block_count, block_size = (diag_blocks.shape[0], diag_blocks.shape[1])
    rounded = vector.astype(jnp.bfloat16).reshape(block_count, block_size)
    result = material_scale(tissue_labels)[:, None] * jnp.einsum(
        "rij,rj->ri", diag_blocks, rounded, preferred_element_type=jnp.float32
    )
    gathered = rounded[block_pattern]
    result = result + jnp.einsum(
        "rkij,rkj->ri", couple_blocks, gathered, preferred_element_type=jnp.float32
    )
    backward = jnp.einsum(
        "rkij,ri->rkj", couple_blocks, rounded, preferred_element_type=jnp.float32
    )
    onehot = (block_pattern.reshape(-1)[:, None] == jnp.arange(block_count)[None, :]).astype(
        jnp.float32
    )
    result = result + jnp.einsum(
        "mc,mj->cj", onehot, backward.reshape(-1, block_size), precision=lax.Precision.HIGHEST
    )
    return result.reshape(-1)


def face_tables(face_map, block_count, block_size):
    flat = face_map.reshape(-1)
    rows = (flat[:, None] // block_size == jnp.arange(block_count)[None, :]).astype(jnp.float32)
    lanes = flat[:, None] % block_size == jnp.arange(block_size)[None, :]
    return rows, lanes


def gather_faces(vector, tables):
    rows, lanes = tables
    block_count = rows.shape[1]
    picked = jnp.dot(rows, vector.reshape(block_count, -1), precision=lax.Precision.HIGHEST)
    return jnp.sum(jnp.where(lanes, picked, 0.0), axis=1)


def scatter_faces(result, tables, contribution):
    rows, lanes = tables
    spread = jnp.where(lanes, contribution[:, None], 0.0)
    added = jnp.dot(rows.T, spread, precision=lax.Precision.HIGHEST)
    return result + added.reshape(-1)


def exchange_faces(values):
    across = extended(values[0:2], (("gx", 0),), 1)
    upward = extended(values[2:4], (("gy", 0),), 1)
    return jnp.stack([across[0], across[3], upward[0], upward[3]])


def operate(vector, received, diag_blocks, couple_blocks, block_pattern, tissue_labels, tables):
    result = block_apply(vector, diag_blocks, couple_blocks, block_pattern, tissue_labels)
    return scatter_faces(result, tables, -COUPLING * received.reshape(-1))


def precondition(residual, precond_blocks, tissue_labels, coarse_basis, live_cols, compliance):
    block_count, block_size = (precond_blocks.shape[0], precond_blocks.shape[1])
    rounded = residual.astype(jnp.bfloat16)
    product = jnp.einsum(
        "rij,rj->ri",
        precond_blocks,
        rounded.reshape(block_count, block_size),
        preferred_element_type=jnp.float32,
    )
    local_part = (product / material_scale(tissue_labels)[:, None]).reshape(-1)
    coarse_load = jnp.dot(rounded, coarse_basis, preferred_element_type=jnp.float32) * live_cols
    summed = butterfly_sum(coarse_load, ("gx",))
    solved = jnp.dot(compliance, summed, precision=lax.Precision.HIGHEST)
    weights = (solved * live_cols).astype(jnp.bfloat16)
    return local_part + jnp.dot(coarse_basis, weights, preferred_element_type=jnp.float32)


def global_sum(value):
    return butterfly_sum(value, ("gy", "gx"))


def body(
    right_side,
    coarse_matrix,
    coarse_order,
    diag_blocks,
    couple_blocks,
    block_pattern,
    tissue_labels,
    precond_blocks,
    coarse_basis,
    face_map,
):
    source = right_side[0, 0]
    matrix = coarse_matrix[0, 0]
    order_here = coarse_order[0, 0]
    diagonal = diag_blocks[0, 0]
    couples = couple_blocks[0, 0]
    pattern = block_pattern[0, 0]
    labels = tissue_labels[0, 0]
    inverses = precond_blocks[0, 0]
    basis = coarse_basis[0, 0]
    faces = face_map[0, 0]
    order_size = matrix.shape[-1]
    live_cols = (jnp.arange(order_size) < order_here).astype(jnp.float32)
    masked = masked_coarse(matrix, order_here)
    merged = merged_tree(masked, "gx", parallel_sum)
    compliance = newton_inverse(merged)
    adjoint = jnp.zeros_like(source)
    residual = source
    precond = precondition(residual, inverses, labels, basis, live_cols, compliance)
    precond_dot = jnp.sum(residual * precond)
    direction = precond
    tables = face_tables(faces, diagonal.shape[0], diagonal.shape[1])
    face_count = faces.shape[0]
    received = exchange_faces(gather_faces(direction, tables).reshape(face_count, -1))
    for iteration in range(ITERS):
        applied = operate(direction, received, diagonal, couples, pattern, labels, tables)
        curvature = jnp.sum(direction * applied)
        if iteration == 0:
            both = global_sum(jnp.stack([precond_dot, curvature]))
            precond_dot, curvature = both[0], both[1]
        else:
            curvature = global_sum(curvature)
        step_size = precond_dot / curvature
        adjoint = adjoint + step_size * direction
        residual = residual - step_size * applied
        if iteration + 1 < ITERS:
            precond = precondition(residual, inverses, labels, basis, live_cols, compliance)
            received_precond = exchange_faces(
                gather_faces(precond, tables).reshape(face_count, -1)
            )
            dot_next = global_sum(jnp.sum(residual * precond))
            ratio = dot_next / precond_dot
            direction = precond + ratio * direction
            received = received_precond + ratio * received
            precond_dot = dot_next
    return (adjoint[None, None], residual[None, None])


def solution(mesh):
    in_specs = (
        P("gx", "gy", None),
        P("gx", "gy", None, None),
        P("gx", "gy"),
        P("gx", "gy", None, None, None),
        P("gx", "gy", None, None, None, None),
        P("gx", "gy", None, None),
        P("gx", "gy", None),
        P("gx", "gy", None, None, None),
        P("gx", "gy", None, None),
        P("gx", "gy", None, None),
    )
    out_specs = (P("gx", "gy", None), P("gx", "gy", None))
    return jax.shard_map(body, mesh=mesh, in_specs=in_specs, out_specs=out_specs, check_vma=False)
```

```python
import jax
import jax.numpy as jnp
from jax import lax
from jax.sharding import PartitionSpec as P

ITERS = 2


STIFFNESS = (1.0, 0.6, 2.0)
COUPLING = 0.5
NEWTON_STEPS = 4


def is_power_of_two(count):
    return count > 0 and (count & (count - 1)) == 0


def butterfly_sum(value, axes):
    for axis in axes:
        count = lax.axis_size(axis)
        if not is_power_of_two(count):
            value = lax.psum(value, axis)
            continue
        stride = 1
        while stride < count:
            pairs = [(i, i ^ stride) for i in range(count)]
            value = value + lax.ppermute(value, axis, pairs)
            stride *= 2
    return value


def exchange_sum(value, axes):
    count = 1
    for axis in axes:
        count *= lax.axis_size(axis)
    shape = value.shape
    flat = value.reshape(1, -1)
    spread = jnp.broadcast_to(flat, (count,) + flat.shape[1:])
    name = axes if len(axes) > 1 else axes[0]
    gathered = lax.all_to_all(spread, name, 0, 0, tiled=True)
    return jnp.sum(gathered, axis=0).reshape(shape)


def extended(block, sides, width):
    for axis, dim in sides:
        count = lax.axis_size(axis)
        forward = [(i, i + 1) for i in range(count - 1)]
        backward = [(target, source) for source, target in forward]
        low = lax.ppermute(
            lax.slice_in_dim(block, block.shape[dim] - width, None, axis=dim), axis, forward
        )
        high = lax.ppermute(lax.slice_in_dim(block, 0, width, axis=dim), axis, backward)
        block = jnp.concatenate([low, block, high], axis=dim)
    return block


def merged_chain(part, axis, combine):
    gathered = lax.all_gather(part, axis)

    def take(source):
        return lax.dynamic_index_in_dim(gathered, source, 0, False)

    return lax.fori_loop(
        1, lax.axis_size(axis), lambda source, state: combine(state, take(source)), take(0)
    )


def merged_tree(part, axis, combine):
    count = lax.axis_size(axis)
    if not is_power_of_two(count):
        return merged_chain(part, axis, combine)
    index = lax.axis_index(axis)
    stride = 1
    while stride < count:
        pairs = [(i, i ^ stride) for i in range(count)]
        other = lax.ppermute(part, axis, pairs)
        upper = (index & stride) != 0
        lower_term = jnp.where(upper, other, part)
        upper_term = jnp.where(upper, part, other)
        part = combine(lower_term, upper_term)
        stride *= 2
    return part


def material_scale(tissue_labels):
    return jnp.where(
        tissue_labels == 0, STIFFNESS[0], jnp.where(tissue_labels == 1, STIFFNESS[1], STIFFNESS[2])
    ).astype(jnp.float32)


def identity_mask(order_size):
    index = jnp.arange(order_size)
    return index[:, None] == index[None, :]


def diagonal_of(matrix):
    eye = identity_mask(matrix.shape[-1])
    return jnp.sum(jnp.where(eye, matrix, 0.0), axis=1)


def masked_coarse(matrix, coarse_order):
    order_size = matrix.shape[-1]
    live = jnp.arange(order_size) < coarse_order
    keep = (live[:, None] & live[None, :]) | identity_mask(order_size)
    return jnp.where(keep, matrix, 0.0)


def newton_inverse(matrix):
    order_size = matrix.shape[-1]
    eye = identity_mask(order_size)
    identity = eye.astype(jnp.float32)
    recip = 1.0 / diagonal_of(matrix)
    product = matrix * recip[None, :]
    approx = recip[:, None] * (2.0 * identity - product)
    for sweep in range(1, NEWTON_STEPS):
        product = jnp.dot(matrix, approx, precision=lax.Precision.HIGHEST)
        approx = jnp.dot(approx, 2.0 * identity - product, precision=lax.Precision.HIGHEST)
    return approx


def parallel_sum(left_term, right_term):
    inverse = newton_inverse(left_term + right_term)
    middle = jnp.dot(inverse, left_term, precision=lax.Precision.HIGHEST)
    return left_term - jnp.dot(left_term, middle, precision=lax.Precision.HIGHEST)


def block_apply(vector, diag_blocks, couple_blocks, block_pattern, tissue_labels):
    block_count, block_size = (diag_blocks.shape[0], diag_blocks.shape[1])
    rounded = vector.astype(jnp.bfloat16).reshape(block_count, block_size)
    result = material_scale(tissue_labels)[:, None] * jnp.einsum(
        "rij,rj->ri", diag_blocks, rounded, preferred_element_type=jnp.float32
    )
    gathered = rounded[block_pattern]
    result = result + jnp.einsum(
        "rkij,rkj->ri", couple_blocks, gathered, preferred_element_type=jnp.float32
    )
    backward = jnp.einsum(
        "rkij,ri->rkj", couple_blocks, rounded, preferred_element_type=jnp.float32
    )
    onehot = (block_pattern.reshape(-1)[:, None] == jnp.arange(block_count)[None, :]).astype(
        jnp.float32
    )
    result = result + jnp.einsum(
        "mc,mj->cj", onehot, backward.reshape(-1, block_size), precision=lax.Precision.HIGHEST
    )
    return result.reshape(-1)


def face_tables(face_map, block_count, block_size):
    flat = face_map.reshape(-1)
    rows = (flat[:, None] // block_size == jnp.arange(block_count)[None, :]).astype(jnp.float32)
    lanes = flat[:, None] % block_size == jnp.arange(block_size)[None, :]
    return rows, lanes


def gather_faces(vector, tables):
    rows, lanes = tables
    block_count = rows.shape[1]
    picked = jnp.dot(rows, vector.reshape(block_count, -1), precision=lax.Precision.HIGHEST)
    return jnp.sum(jnp.where(lanes, picked, 0.0), axis=1)


def scatter_faces(result, tables, contribution):
    rows, lanes = tables
    spread = jnp.where(lanes, contribution[:, None], 0.0)
    added = jnp.dot(rows.T, spread, precision=lax.Precision.HIGHEST)
    return result + added.reshape(-1)


def exchange_faces(values):
    across = extended(values[0:2], (("gx", 0),), 1)
    upward = extended(values[2:4], (("gy", 0),), 1)
    return jnp.stack([across[0], across[3], upward[0], upward[3]])


def operate(vector, received, diag_blocks, couple_blocks, block_pattern, tissue_labels, tables):
    result = block_apply(vector, diag_blocks, couple_blocks, block_pattern, tissue_labels)
    return scatter_faces(result, tables, -COUPLING * received.reshape(-1))


def precondition(residual, precond_blocks, tissue_labels, coarse_basis, live_cols, compliance):
    block_count, block_size = (precond_blocks.shape[0], precond_blocks.shape[1])
    rounded = residual.astype(jnp.bfloat16)
    product = jnp.einsum(
        "rij,rj->ri",
        precond_blocks,
        rounded.reshape(block_count, block_size),
        preferred_element_type=jnp.float32,
    )
    local_part = (product / material_scale(tissue_labels)[:, None]).reshape(-1)
    coarse_load = jnp.dot(rounded, coarse_basis, preferred_element_type=jnp.float32) * live_cols
    summed = exchange_sum(coarse_load, ("gx",))
    solved = jnp.dot(compliance, summed, precision=lax.Precision.HIGHEST)
    weights = (solved * live_cols).astype(jnp.bfloat16)
    return local_part + jnp.dot(coarse_basis, weights, preferred_element_type=jnp.float32)


def global_sum(value):
    return exchange_sum(value, ("gx", "gy"))


def body(
    right_side,
    coarse_matrix,
    coarse_order,
    diag_blocks,
    couple_blocks,
    block_pattern,
    tissue_labels,
    precond_blocks,
    coarse_basis,
    face_map,
):
    source = right_side[0, 0]
    matrix = coarse_matrix[0, 0]
    order_here = coarse_order[0, 0]
    diagonal = diag_blocks[0, 0]
    couples = couple_blocks[0, 0]
    pattern = block_pattern[0, 0]
    labels = tissue_labels[0, 0]
    inverses = precond_blocks[0, 0]
    basis = coarse_basis[0, 0]
    faces = face_map[0, 0]
    order_size = matrix.shape[-1]
    live_cols = (jnp.arange(order_size) < order_here).astype(jnp.float32)
    masked = masked_coarse(matrix, order_here)
    merged = merged_tree(masked, "gx", parallel_sum)
    compliance = newton_inverse(merged)
    adjoint = jnp.zeros_like(source)
    residual = source
    precond = precondition(residual, inverses, labels, basis, live_cols, compliance)
    precond_dot = jnp.sum(residual * precond)
    direction = precond
    tables = face_tables(faces, diagonal.shape[0], diagonal.shape[1])
    face_count = faces.shape[0]
    received = exchange_faces(gather_faces(direction, tables).reshape(face_count, -1))
    for iteration in range(ITERS):
        applied = operate(direction, received, diagonal, couples, pattern, labels, tables)
        curvature = jnp.sum(direction * applied)
        if iteration == 0:
            both = global_sum(jnp.stack([precond_dot, curvature]))
            precond_dot, curvature = both[0], both[1]
        else:
            curvature = global_sum(curvature)
        step_size = precond_dot / curvature
        adjoint = adjoint + step_size * direction
        residual = residual - step_size * applied
        if iteration + 1 < ITERS:
            precond = precondition(residual, inverses, labels, basis, live_cols, compliance)
            received_precond = exchange_faces(
                gather_faces(precond, tables).reshape(face_count, -1)
            )
            dot_next = global_sum(jnp.sum(residual * precond))
            ratio = dot_next / precond_dot
            direction = precond + ratio * direction
            received = received_precond + ratio * received
            precond_dot = dot_next
    return (adjoint[None, None], residual[None, None])


def solution(mesh):
    in_specs = (
        P("gx", "gy", None),
        P("gx", "gy", None, None),
        P("gx", "gy"),
        P("gx", "gy", None, None, None),
        P("gx", "gy", None, None, None, None),
        P("gx", "gy", None, None),
        P("gx", "gy", None),
        P("gx", "gy", None, None, None),
        P("gx", "gy", None, None),
        P("gx", "gy", None, None),
    )
    out_specs = (P("gx", "gy", None), P("gx", "gy", None))
    return jax.shard_map(body, mesh=mesh, in_specs=in_specs, out_specs=out_specs, check_vma=False)
```

```python
import jax
import jax.numpy as jnp
from jax import lax
from jax.sharding import PartitionSpec as P

ITERS = 2


STIFFNESS = (1.0, 0.6, 2.0)
COUPLING = 0.5
NEWTON_STEPS = 4
COARSE_PRECISION = lax.Precision.HIGH


def is_power_of_two(count):
    return count > 0 and (count & (count - 1)) == 0


def butterfly_sum(value, axes):
    for axis in axes:
        count = lax.axis_size(axis)
        if not is_power_of_two(count):
            value = lax.psum(value, axis)
            continue
        stride = 1
        while stride < count:
            pairs = [(i, i ^ stride) for i in range(count)]
            value = value + lax.ppermute(value, axis, pairs)
            stride *= 2
    return value


def exchange_sum(value, axes):
    count = 1
    for axis in axes:
        count *= lax.axis_size(axis)
    shape = value.shape
    flat = value.reshape(1, -1)
    spread = jnp.broadcast_to(flat, (count,) + flat.shape[1:])
    name = axes if len(axes) > 1 else axes[0]
    gathered = lax.all_to_all(spread, name, 0, 0, tiled=True)
    return jnp.sum(gathered, axis=0).reshape(shape)


def extended(block, sides, width):
    for axis, dim in sides:
        count = lax.axis_size(axis)
        forward = [(i, i + 1) for i in range(count - 1)]
        backward = [(target, source) for source, target in forward]
        low = lax.ppermute(
            lax.slice_in_dim(block, block.shape[dim] - width, None, axis=dim), axis, forward
        )
        high = lax.ppermute(lax.slice_in_dim(block, 0, width, axis=dim), axis, backward)
        block = jnp.concatenate([low, block, high], axis=dim)
    return block


def merged_chain(part, axis, combine):
    gathered = lax.all_gather(part, axis)

    def take(source):
        return lax.dynamic_index_in_dim(gathered, source, 0, False)

    return lax.fori_loop(
        1, lax.axis_size(axis), lambda source, state: combine(state, take(source)), take(0)
    )


def merged_tree(part, axis, combine):
    count = lax.axis_size(axis)
    if not is_power_of_two(count):
        return merged_chain(part, axis, combine)
    index = lax.axis_index(axis)
    stride = 1
    while stride < count:
        pairs = [(i, i ^ stride) for i in range(count)]
        other = lax.ppermute(part, axis, pairs)
        upper = (index & stride) != 0
        lower_term = jnp.where(upper, other, part)
        upper_term = jnp.where(upper, part, other)
        part = combine(lower_term, upper_term)
        stride *= 2
    return part


def material_scale(tissue_labels):
    return jnp.where(
        tissue_labels == 0, STIFFNESS[0], jnp.where(tissue_labels == 1, STIFFNESS[1], STIFFNESS[2])
    ).astype(jnp.float32)


def identity_mask(order_size):
    index = jnp.arange(order_size)
    return index[:, None] == index[None, :]


def diagonal_of(matrix):
    eye = identity_mask(matrix.shape[-1])
    return jnp.sum(jnp.where(eye, matrix, 0.0), axis=1)


def masked_coarse(matrix, coarse_order):
    order_size = matrix.shape[-1]
    live = jnp.arange(order_size) < coarse_order
    keep = (live[:, None] & live[None, :]) | identity_mask(order_size)
    return jnp.where(keep, matrix, 0.0)


def newton_inverse(matrix):
    order_size = matrix.shape[-1]
    eye = identity_mask(order_size)
    identity = eye.astype(jnp.float32)
    recip = 1.0 / diagonal_of(matrix)
    product = matrix * recip[None, :]
    approx = recip[:, None] * (2.0 * identity - product)
    for sweep in range(1, NEWTON_STEPS):
        product = jnp.dot(matrix, approx, precision=COARSE_PRECISION)
        approx = jnp.dot(approx, 2.0 * identity - product, precision=COARSE_PRECISION)
    return approx


def parallel_sum(left_term, right_term):
    inverse = newton_inverse(left_term + right_term)
    middle = jnp.dot(inverse, left_term, precision=COARSE_PRECISION)
    return left_term - jnp.dot(left_term, middle, precision=COARSE_PRECISION)


def block_apply(vector, diag_blocks, couple_blocks, block_pattern, tissue_labels):
    block_count, block_size = (diag_blocks.shape[0], diag_blocks.shape[1])
    rounded = vector.astype(jnp.bfloat16).reshape(block_count, block_size)
    result = material_scale(tissue_labels)[:, None] * jnp.einsum(
        "rij,rj->ri", diag_blocks, rounded, preferred_element_type=jnp.float32
    )
    gathered = rounded[block_pattern]
    result = result + jnp.einsum(
        "rkij,rkj->ri", couple_blocks, gathered, preferred_element_type=jnp.float32
    )
    backward = jnp.einsum(
        "rkij,ri->rkj", couple_blocks, rounded, preferred_element_type=jnp.float32
    )
    onehot = (block_pattern.reshape(-1)[:, None] == jnp.arange(block_count)[None, :]).astype(
        jnp.float32
    )
    result = result + jnp.einsum(
        "mc,mj->cj", onehot, backward.reshape(-1, block_size), precision=lax.Precision.HIGHEST
    )
    return result.reshape(-1)


def face_tables(face_map, block_count, block_size):
    flat = face_map.reshape(-1)
    rows = (flat[:, None] // block_size == jnp.arange(block_count)[None, :]).astype(jnp.float32)
    lanes = flat[:, None] % block_size == jnp.arange(block_size)[None, :]
    return rows, lanes


def gather_faces(vector, tables):
    rows, lanes = tables
    block_count = rows.shape[1]
    picked = jnp.dot(rows, vector.reshape(block_count, -1), precision=lax.Precision.HIGHEST)
    return jnp.sum(jnp.where(lanes, picked, 0.0), axis=1)


def scatter_faces(result, tables, contribution):
    rows, lanes = tables
    spread = jnp.where(lanes, contribution[:, None], 0.0)
    added = jnp.dot(rows.T, spread, precision=lax.Precision.HIGHEST)
    return result + added.reshape(-1)


def exchange_faces(values):
    across = extended(values[0:2], (("gx", 0),), 1)
    upward = extended(values[2:4], (("gy", 0),), 1)
    return jnp.stack([across[0], across[3], upward[0], upward[3]])


def operate(vector, received, diag_blocks, couple_blocks, block_pattern, tissue_labels, tables):
    result = block_apply(vector, diag_blocks, couple_blocks, block_pattern, tissue_labels)
    return scatter_faces(result, tables, -COUPLING * received.reshape(-1))


def precondition(residual, precond_blocks, tissue_labels, coarse_basis, live_cols, compliance):
    block_count, block_size = (precond_blocks.shape[0], precond_blocks.shape[1])
    rounded = residual.astype(jnp.bfloat16)
    product = jnp.einsum(
        "rij,rj->ri",
        precond_blocks,
        rounded.reshape(block_count, block_size),
        preferred_element_type=jnp.float32,
    )
    local_part = (product / material_scale(tissue_labels)[:, None]).reshape(-1)
    coarse_load = jnp.dot(rounded, coarse_basis, preferred_element_type=jnp.float32) * live_cols
    summed = exchange_sum(coarse_load, ("gx",))
    solved = jnp.dot(compliance, summed, precision=lax.Precision.HIGHEST)
    weights = (solved * live_cols).astype(jnp.bfloat16)
    return local_part + jnp.dot(coarse_basis, weights, preferred_element_type=jnp.float32)


def global_sum(value):
    return exchange_sum(value, ("gx", "gy"))


def body(
    right_side,
    coarse_matrix,
    coarse_order,
    diag_blocks,
    couple_blocks,
    block_pattern,
    tissue_labels,
    precond_blocks,
    coarse_basis,
    face_map,
):
    source = right_side[0, 0]
    matrix = coarse_matrix[0, 0]
    order_here = coarse_order[0, 0]
    diagonal = diag_blocks[0, 0]
    couples = couple_blocks[0, 0]
    pattern = block_pattern[0, 0]
    labels = tissue_labels[0, 0]
    inverses = precond_blocks[0, 0]
    basis = coarse_basis[0, 0]
    faces = face_map[0, 0]
    order_size = matrix.shape[-1]
    live_cols = (jnp.arange(order_size) < order_here).astype(jnp.float32)
    masked = masked_coarse(matrix, order_here)
    merged = merged_tree(masked, "gx", parallel_sum)
    compliance = newton_inverse(merged)
    adjoint = jnp.zeros_like(source)
    residual = source
    precond = precondition(residual, inverses, labels, basis, live_cols, compliance)
    precond_dot = jnp.sum(residual * precond)
    direction = precond
    tables = face_tables(faces, diagonal.shape[0], diagonal.shape[1])
    face_count = faces.shape[0]
    received = exchange_faces(gather_faces(direction, tables).reshape(face_count, -1))
    for iteration in range(ITERS):
        applied = operate(direction, received, diagonal, couples, pattern, labels, tables)
        curvature = jnp.sum(direction * applied)
        if iteration == 0:
            both = global_sum(jnp.stack([precond_dot, curvature]))
            precond_dot, curvature = both[0], both[1]
        else:
            curvature = global_sum(curvature)
        step_size = precond_dot / curvature
        adjoint = adjoint + step_size * direction
        residual = residual - step_size * applied
        if iteration + 1 < ITERS:
            precond = precondition(residual, inverses, labels, basis, live_cols, compliance)
            received_precond = exchange_faces(
                gather_faces(precond, tables).reshape(face_count, -1)
            )
            dot_next = global_sum(jnp.sum(residual * precond))
            ratio = dot_next / precond_dot
            direction = precond + ratio * direction
            received = received_precond + ratio * received
            precond_dot = dot_next
    return (adjoint[None, None], residual[None, None])


def solution(mesh):
    in_specs = (
        P("gx", "gy", None),
        P("gx", "gy", None, None),
        P("gx", "gy"),
        P("gx", "gy", None, None, None),
        P("gx", "gy", None, None, None, None),
        P("gx", "gy", None, None),
        P("gx", "gy", None),
        P("gx", "gy", None, None, None),
        P("gx", "gy", None, None),
        P("gx", "gy", None, None),
    )
    out_specs = (P("gx", "gy", None), P("gx", "gy", None))
    return jax.shard_map(body, mesh=mesh, in_specs=in_specs, out_specs=out_specs, check_vma=False)
```

```python
import jax
import jax.numpy as jnp
from jax import lax
from jax.sharding import PartitionSpec as P

ITERS = 2


STIFFNESS = (1.0, 0.6, 2.0)
COUPLING = 0.5
NEWTON_STEPS = 4
EARLY_PRECISION = lax.Precision.HIGH


def is_power_of_two(count):
    return count > 0 and (count & (count - 1)) == 0


def butterfly_sum(value, axes):
    for axis in axes:
        count = lax.axis_size(axis)
        if not is_power_of_two(count):
            value = lax.psum(value, axis)
            continue
        stride = 1
        while stride < count:
            pairs = [(i, i ^ stride) for i in range(count)]
            value = value + lax.ppermute(value, axis, pairs)
            stride *= 2
    return value


def exchange_sum(value, axes):
    count = 1
    for axis in axes:
        count *= lax.axis_size(axis)
    shape = value.shape
    flat = value.reshape(1, -1)
    spread = jnp.broadcast_to(flat, (count,) + flat.shape[1:])
    name = axes if len(axes) > 1 else axes[0]
    gathered = lax.all_to_all(spread, name, 0, 0, tiled=True)
    return jnp.sum(gathered, axis=0).reshape(shape)


def extended(block, sides, width):
    for axis, dim in sides:
        count = lax.axis_size(axis)
        forward = [(i, i + 1) for i in range(count - 1)]
        backward = [(target, source) for source, target in forward]
        low = lax.ppermute(
            lax.slice_in_dim(block, block.shape[dim] - width, None, axis=dim), axis, forward
        )
        high = lax.ppermute(lax.slice_in_dim(block, 0, width, axis=dim), axis, backward)
        block = jnp.concatenate([low, block, high], axis=dim)
    return block


def merged_chain(part, axis, combine):
    gathered = lax.all_gather(part, axis)

    def take(source):
        return lax.dynamic_index_in_dim(gathered, source, 0, False)

    return lax.fori_loop(
        1, lax.axis_size(axis), lambda source, state: combine(state, take(source)), take(0)
    )


def merged_tree(part, axis, combine):
    count = lax.axis_size(axis)
    if not is_power_of_two(count):
        return merged_chain(part, axis, combine)
    index = lax.axis_index(axis)
    stride = 1
    while stride < count:
        pairs = [(i, i ^ stride) for i in range(count)]
        other = lax.ppermute(part, axis, pairs)
        upper = (index & stride) != 0
        lower_term = jnp.where(upper, other, part)
        upper_term = jnp.where(upper, part, other)
        part = combine(lower_term, upper_term)
        stride *= 2
    return part


def material_scale(tissue_labels):
    return jnp.where(
        tissue_labels == 0, STIFFNESS[0], jnp.where(tissue_labels == 1, STIFFNESS[1], STIFFNESS[2])
    ).astype(jnp.float32)


def identity_mask(order_size):
    index = jnp.arange(order_size)
    return index[:, None] == index[None, :]


def diagonal_of(matrix):
    eye = identity_mask(matrix.shape[-1])
    return jnp.sum(jnp.where(eye, matrix, 0.0), axis=1)


def masked_coarse(matrix, coarse_order):
    order_size = matrix.shape[-1]
    live = jnp.arange(order_size) < coarse_order
    keep = (live[:, None] & live[None, :]) | identity_mask(order_size)
    return jnp.where(keep, matrix, 0.0)


def newton_inverse(matrix):
    order_size = matrix.shape[-1]
    eye = identity_mask(order_size)
    identity = eye.astype(jnp.float32)
    recip = 1.0 / diagonal_of(matrix)
    product = matrix * recip[None, :]
    approx = recip[:, None] * (2.0 * identity - product)
    for sweep in range(1, NEWTON_STEPS):
        precision = lax.Precision.HIGHEST if sweep + 1 == NEWTON_STEPS else EARLY_PRECISION
        product = jnp.dot(matrix, approx, precision=precision)
        approx = jnp.dot(approx, 2.0 * identity - product, precision=precision)
    return approx


def parallel_sum(left_term, right_term):
    inverse = newton_inverse(left_term + right_term)
    middle = jnp.dot(inverse, left_term, precision=lax.Precision.HIGHEST)
    return left_term - jnp.dot(left_term, middle, precision=lax.Precision.HIGHEST)


def block_apply(vector, diag_blocks, couple_blocks, block_pattern, tissue_labels):
    block_count, block_size = (diag_blocks.shape[0], diag_blocks.shape[1])
    rounded = vector.astype(jnp.bfloat16).reshape(block_count, block_size)
    result = material_scale(tissue_labels)[:, None] * jnp.einsum(
        "rij,rj->ri", diag_blocks, rounded, preferred_element_type=jnp.float32
    )
    gathered = rounded[block_pattern]
    result = result + jnp.einsum(
        "rkij,rkj->ri", couple_blocks, gathered, preferred_element_type=jnp.float32
    )
    backward = jnp.einsum(
        "rkij,ri->rkj", couple_blocks, rounded, preferred_element_type=jnp.float32
    )
    onehot = (block_pattern.reshape(-1)[:, None] == jnp.arange(block_count)[None, :]).astype(
        jnp.float32
    )
    result = result + jnp.einsum(
        "mc,mj->cj", onehot, backward.reshape(-1, block_size), precision=lax.Precision.HIGHEST
    )
    return result.reshape(-1)


def face_tables(face_map, block_count, block_size):
    flat = face_map.reshape(-1)
    rows = (flat[:, None] // block_size == jnp.arange(block_count)[None, :]).astype(jnp.float32)
    lanes = flat[:, None] % block_size == jnp.arange(block_size)[None, :]
    return rows, lanes


def gather_faces(vector, tables):
    rows, lanes = tables
    block_count = rows.shape[1]
    picked = jnp.dot(rows, vector.reshape(block_count, -1), precision=lax.Precision.HIGHEST)
    return jnp.sum(jnp.where(lanes, picked, 0.0), axis=1)


def scatter_faces(result, tables, contribution):
    rows, lanes = tables
    spread = jnp.where(lanes, contribution[:, None], 0.0)
    added = jnp.dot(rows.T, spread, precision=lax.Precision.HIGHEST)
    return result + added.reshape(-1)


def exchange_faces(values):
    across = extended(values[0:2], (("gx", 0),), 1)
    upward = extended(values[2:4], (("gy", 0),), 1)
    return jnp.stack([across[0], across[3], upward[0], upward[3]])


def operate(vector, received, diag_blocks, couple_blocks, block_pattern, tissue_labels, tables):
    result = block_apply(vector, diag_blocks, couple_blocks, block_pattern, tissue_labels)
    return scatter_faces(result, tables, -COUPLING * received.reshape(-1))


def precondition(residual, precond_blocks, tissue_labels, coarse_basis, live_cols, compliance):
    block_count, block_size = (precond_blocks.shape[0], precond_blocks.shape[1])
    rounded = residual.astype(jnp.bfloat16)
    product = jnp.einsum(
        "rij,rj->ri",
        precond_blocks,
        rounded.reshape(block_count, block_size),
        preferred_element_type=jnp.float32,
    )
    local_part = (product / material_scale(tissue_labels)[:, None]).reshape(-1)
    coarse_load = jnp.dot(rounded, coarse_basis, preferred_element_type=jnp.float32) * live_cols
    summed = exchange_sum(coarse_load, ("gx",))
    solved = jnp.dot(compliance, summed, precision=lax.Precision.HIGHEST)
    weights = (solved * live_cols).astype(jnp.bfloat16)
    return local_part + jnp.dot(coarse_basis, weights, preferred_element_type=jnp.float32)


def global_sum(value):
    return exchange_sum(value, ("gx", "gy"))


def body(
    right_side,
    coarse_matrix,
    coarse_order,
    diag_blocks,
    couple_blocks,
    block_pattern,
    tissue_labels,
    precond_blocks,
    coarse_basis,
    face_map,
):
    source = right_side[0, 0]
    matrix = coarse_matrix[0, 0]
    order_here = coarse_order[0, 0]
    diagonal = diag_blocks[0, 0]
    couples = couple_blocks[0, 0]
    pattern = block_pattern[0, 0]
    labels = tissue_labels[0, 0]
    inverses = precond_blocks[0, 0]
    basis = coarse_basis[0, 0]
    faces = face_map[0, 0]
    order_size = matrix.shape[-1]
    live_cols = (jnp.arange(order_size) < order_here).astype(jnp.float32)
    masked = masked_coarse(matrix, order_here)
    merged = merged_tree(masked, "gx", parallel_sum)
    compliance = newton_inverse(merged)
    adjoint = jnp.zeros_like(source)
    residual = source
    precond = precondition(residual, inverses, labels, basis, live_cols, compliance)
    precond_dot = jnp.sum(residual * precond)
    direction = precond
    tables = face_tables(faces, diagonal.shape[0], diagonal.shape[1])
    face_count = faces.shape[0]
    received = exchange_faces(gather_faces(direction, tables).reshape(face_count, -1))
    for iteration in range(ITERS):
        applied = operate(direction, received, diagonal, couples, pattern, labels, tables)
        curvature = jnp.sum(direction * applied)
        if iteration == 0:
            both = global_sum(jnp.stack([precond_dot, curvature]))
            precond_dot, curvature = both[0], both[1]
        else:
            curvature = global_sum(curvature)
        step_size = precond_dot / curvature
        adjoint = adjoint + step_size * direction
        residual = residual - step_size * applied
        if iteration + 1 < ITERS:
            precond = precondition(residual, inverses, labels, basis, live_cols, compliance)
            received_precond = exchange_faces(
                gather_faces(precond, tables).reshape(face_count, -1)
            )
            dot_next = global_sum(jnp.sum(residual * precond))
            ratio = dot_next / precond_dot
            direction = precond + ratio * direction
            received = received_precond + ratio * received
            precond_dot = dot_next
    return (adjoint[None, None], residual[None, None])


def solution(mesh):
    in_specs = (
        P("gx", "gy", None),
        P("gx", "gy", None, None),
        P("gx", "gy"),
        P("gx", "gy", None, None, None),
        P("gx", "gy", None, None, None, None),
        P("gx", "gy", None, None),
        P("gx", "gy", None),
        P("gx", "gy", None, None, None),
        P("gx", "gy", None, None),
        P("gx", "gy", None, None),
    )
    out_specs = (P("gx", "gy", None), P("gx", "gy", None))
    return jax.shard_map(body, mesh=mesh, in_specs=in_specs, out_specs=out_specs, check_vma=False)
```

```python
import jax
import jax.numpy as jnp
from jax import lax
from jax.sharding import PartitionSpec as P

ITERS = 2


STIFFNESS = (1.0, 0.6, 2.0)
COUPLING = 0.5
NEWTON_STEPS = 4
EARLY_PRECISION = lax.Precision.HIGH


def is_power_of_two(count):
    return count > 0 and (count & (count - 1)) == 0


def butterfly_sum(value, axes):
    for axis in axes:
        count = lax.axis_size(axis)
        if not is_power_of_two(count):
            value = lax.psum(value, axis)
            continue
        stride = 1
        while stride < count:
            pairs = [(i, i ^ stride) for i in range(count)]
            value = value + lax.ppermute(value, axis, pairs)
            stride *= 2
    return value


def exchange_sum(value, axes):
    count = 1
    for axis in axes:
        count *= lax.axis_size(axis)
    shape = value.shape
    flat = value.reshape(1, -1)
    spread = jnp.broadcast_to(flat, (count,) + flat.shape[1:])
    name = axes if len(axes) > 1 else axes[0]
    gathered = lax.all_to_all(spread, name, 0, 0, tiled=True)
    return jnp.sum(gathered, axis=0).reshape(shape)


def extended(block, sides, width):
    for axis, dim in sides:
        count = lax.axis_size(axis)
        forward = [(i, i + 1) for i in range(count - 1)]
        backward = [(target, source) for source, target in forward]
        low = lax.ppermute(
            lax.slice_in_dim(block, block.shape[dim] - width, None, axis=dim), axis, forward
        )
        high = lax.ppermute(lax.slice_in_dim(block, 0, width, axis=dim), axis, backward)
        block = jnp.concatenate([low, block, high], axis=dim)
    return block


def merged_chain(part, axis, combine):
    gathered = lax.all_gather(part, axis)

    def take(source):
        return lax.dynamic_index_in_dim(gathered, source, 0, False)

    return lax.fori_loop(
        1, lax.axis_size(axis), lambda source, state: combine(state, take(source)), take(0)
    )


SYM_TILE = 128


def upper_pairs(order_size):
    tiles = order_size // SYM_TILE
    return [(i, j) for i in range(tiles) for j in range(i, tiles)]


def pack_symmetric(matrix):
    order_size = matrix.shape[-1]
    blocks = [
        matrix[i * SYM_TILE:(i + 1) * SYM_TILE, j * SYM_TILE:(j + 1) * SYM_TILE]
        for i, j in upper_pairs(order_size)
    ]
    return jnp.stack(blocks)


def unpack_symmetric(packed, order_size):
    tiles = order_size // SYM_TILE
    where = {pair: k for k, pair in enumerate(upper_pairs(order_size))}
    rows = []
    for i in range(tiles):
        row = []
        for j in range(tiles):
            row.append(packed[where[(i, j)]] if i <= j else packed[where[(j, i)]].T)
        rows.append(jnp.concatenate(row, axis=1))
    return jnp.concatenate(rows, axis=0)


def merged_tree(part, axis, combine):
    count = lax.axis_size(axis)
    if not is_power_of_two(count):
        return merged_chain(part, axis, combine)
    order_size = part.shape[-1]
    symmetric = order_size % SYM_TILE == 0
    index = lax.axis_index(axis)
    stride = 1
    while stride < count:
        pairs = [(i, i ^ stride) for i in range(count)]
        if symmetric:
            packed = pack_symmetric(part)
            other = unpack_symmetric(lax.ppermute(packed, axis, pairs), order_size)
            part = unpack_symmetric(packed, order_size)
        else:
            other = lax.ppermute(part, axis, pairs)
        upper = (index & stride) != 0
        lower_term = jnp.where(upper, other, part)
        upper_term = jnp.where(upper, part, other)
        part = combine(lower_term, upper_term)
        stride *= 2
    return part


def material_scale(tissue_labels):
    return jnp.where(
        tissue_labels == 0, STIFFNESS[0], jnp.where(tissue_labels == 1, STIFFNESS[1], STIFFNESS[2])
    ).astype(jnp.float32)


def identity_mask(order_size):
    index = jnp.arange(order_size)
    return index[:, None] == index[None, :]


def diagonal_of(matrix):
    eye = identity_mask(matrix.shape[-1])
    return jnp.sum(jnp.where(eye, matrix, 0.0), axis=1)


def masked_coarse(matrix, coarse_order):
    order_size = matrix.shape[-1]
    live = jnp.arange(order_size) < coarse_order
    keep = (live[:, None] & live[None, :]) | identity_mask(order_size)
    return jnp.where(keep, matrix, 0.0)


def newton_inverse(matrix):
    order_size = matrix.shape[-1]
    eye = identity_mask(order_size)
    identity = eye.astype(jnp.float32)
    recip = 1.0 / diagonal_of(matrix)
    product = matrix * recip[None, :]
    approx = recip[:, None] * (2.0 * identity - product)
    for sweep in range(1, NEWTON_STEPS):
        precision = lax.Precision.HIGHEST if sweep + 1 == NEWTON_STEPS else EARLY_PRECISION
        product = jnp.dot(matrix, approx, precision=precision)
        approx = jnp.dot(approx, 2.0 * identity - product, precision=precision)
    return approx


def parallel_sum(left_term, right_term):
    inverse = newton_inverse(left_term + right_term)
    middle = jnp.dot(inverse, left_term, precision=lax.Precision.HIGHEST)
    return left_term - jnp.dot(left_term, middle, precision=lax.Precision.HIGHEST)


def block_apply(vector, diag_blocks, couple_blocks, block_pattern, tissue_labels):
    block_count, block_size = (diag_blocks.shape[0], diag_blocks.shape[1])
    rounded = vector.astype(jnp.bfloat16).reshape(block_count, block_size)
    result = material_scale(tissue_labels)[:, None] * jnp.einsum(
        "rij,rj->ri", diag_blocks, rounded, preferred_element_type=jnp.float32
    )
    gathered = rounded[block_pattern]
    result = result + jnp.einsum(
        "rkij,rkj->ri", couple_blocks, gathered, preferred_element_type=jnp.float32
    )
    backward = jnp.einsum(
        "rkij,ri->rkj", couple_blocks, rounded, preferred_element_type=jnp.float32
    )
    onehot = (block_pattern.reshape(-1)[:, None] == jnp.arange(block_count)[None, :]).astype(
        jnp.float32
    )
    result = result + jnp.einsum(
        "mc,mj->cj", onehot, backward.reshape(-1, block_size), precision=lax.Precision.HIGHEST
    )
    return result.reshape(-1)


def face_tables(face_map, block_count, block_size):
    flat = face_map.reshape(-1)
    rows = (flat[:, None] // block_size == jnp.arange(block_count)[None, :]).astype(jnp.float32)
    lanes = flat[:, None] % block_size == jnp.arange(block_size)[None, :]
    return rows, lanes


def gather_faces(vector, tables):
    rows, lanes = tables
    block_count = rows.shape[1]
    picked = jnp.dot(rows, vector.reshape(block_count, -1), precision=lax.Precision.HIGHEST)
    return jnp.sum(jnp.where(lanes, picked, 0.0), axis=1)


def scatter_faces(result, tables, contribution):
    rows, lanes = tables
    spread = jnp.where(lanes, contribution[:, None], 0.0)
    added = jnp.dot(rows.T, spread, precision=lax.Precision.HIGHEST)
    return result + added.reshape(-1)


def exchange_faces(values):
    across = extended(values[0:2], (("gx", 0),), 1)
    upward = extended(values[2:4], (("gy", 0),), 1)
    return jnp.stack([across[0], across[3], upward[0], upward[3]])


def operate(vector, received, diag_blocks, couple_blocks, block_pattern, tissue_labels, tables):
    result = block_apply(vector, diag_blocks, couple_blocks, block_pattern, tissue_labels)
    return scatter_faces(result, tables, -COUPLING * received.reshape(-1))


def precondition(residual, precond_blocks, tissue_labels, coarse_basis, live_cols, compliance):
    block_count, block_size = (precond_blocks.shape[0], precond_blocks.shape[1])
    rounded = residual.astype(jnp.bfloat16)
    product = jnp.einsum(
        "rij,rj->ri",
        precond_blocks,
        rounded.reshape(block_count, block_size),
        preferred_element_type=jnp.float32,
    )
    local_part = (product / material_scale(tissue_labels)[:, None]).reshape(-1)
    coarse_load = jnp.dot(rounded, coarse_basis, preferred_element_type=jnp.float32) * live_cols
    summed = exchange_sum(coarse_load, ("gx",))
    solved = jnp.dot(compliance, summed, precision=lax.Precision.HIGHEST)
    weights = (solved * live_cols).astype(jnp.bfloat16)
    return local_part + jnp.dot(coarse_basis, weights, preferred_element_type=jnp.float32)


def global_sum(value):
    return exchange_sum(value, ("gx", "gy"))


def body(
    right_side,
    coarse_matrix,
    coarse_order,
    diag_blocks,
    couple_blocks,
    block_pattern,
    tissue_labels,
    precond_blocks,
    coarse_basis,
    face_map,
):
    source = right_side[0, 0]
    matrix = coarse_matrix[0, 0]
    order_here = coarse_order[0, 0]
    diagonal = diag_blocks[0, 0]
    couples = couple_blocks[0, 0]
    pattern = block_pattern[0, 0]
    labels = tissue_labels[0, 0]
    inverses = precond_blocks[0, 0]
    basis = coarse_basis[0, 0]
    faces = face_map[0, 0]
    order_size = matrix.shape[-1]
    live_cols = (jnp.arange(order_size) < order_here).astype(jnp.float32)
    masked = masked_coarse(matrix, order_here)
    merged = merged_tree(masked, "gx", parallel_sum)
    compliance = newton_inverse(merged)
    adjoint = jnp.zeros_like(source)
    residual = source
    precond = precondition(residual, inverses, labels, basis, live_cols, compliance)
    precond_dot = jnp.sum(residual * precond)
    direction = precond
    tables = face_tables(faces, diagonal.shape[0], diagonal.shape[1])
    face_count = faces.shape[0]
    received = exchange_faces(gather_faces(direction, tables).reshape(face_count, -1))
    for iteration in range(ITERS):
        applied = operate(direction, received, diagonal, couples, pattern, labels, tables)
        curvature = jnp.sum(direction * applied)
        if iteration == 0:
            both = global_sum(jnp.stack([precond_dot, curvature]))
            precond_dot, curvature = both[0], both[1]
        else:
            curvature = global_sum(curvature)
        step_size = precond_dot / curvature
        adjoint = adjoint + step_size * direction
        residual = residual - step_size * applied
        if iteration + 1 < ITERS:
            precond = precondition(residual, inverses, labels, basis, live_cols, compliance)
            received_precond = exchange_faces(
                gather_faces(precond, tables).reshape(face_count, -1)
            )
            dot_next = global_sum(jnp.sum(residual * precond))
            ratio = dot_next / precond_dot
            direction = precond + ratio * direction
            received = received_precond + ratio * received
            precond_dot = dot_next
    return (adjoint[None, None], residual[None, None])


def solution(mesh):
    in_specs = (
        P("gx", "gy", None),
        P("gx", "gy", None, None),
        P("gx", "gy"),
        P("gx", "gy", None, None, None),
        P("gx", "gy", None, None, None, None),
        P("gx", "gy", None, None),
        P("gx", "gy", None),
        P("gx", "gy", None, None, None),
        P("gx", "gy", None, None),
        P("gx", "gy", None, None),
    )
    out_specs = (P("gx", "gy", None), P("gx", "gy", None))
    return jax.shard_map(body, mesh=mesh, in_specs=in_specs, out_specs=out_specs, check_vma=False)
```

```python
import jax
import jax.numpy as jnp
from jax import lax
from jax.sharding import PartitionSpec as P

ITERS = 2


STIFFNESS = (1.0, 0.6, 2.0)
COUPLING = 0.5
NEWTON_STEPS = 4
EARLY_PRECISION = lax.Precision.HIGH


def is_power_of_two(count):
    return count > 0 and (count & (count - 1)) == 0


def butterfly_sum(value, axes):
    for axis in axes:
        count = lax.axis_size(axis)
        if not is_power_of_two(count):
            value = lax.psum(value, axis)
            continue
        stride = 1
        while stride < count:
            pairs = [(i, i ^ stride) for i in range(count)]
            value = value + lax.ppermute(value, axis, pairs)
            stride *= 2
    return value


def exchange_sum(value, axes):
    count = 1
    for axis in axes:
        count *= lax.axis_size(axis)
    shape = value.shape
    flat = value.reshape(1, -1)
    spread = jnp.broadcast_to(flat, (count,) + flat.shape[1:])
    name = axes if len(axes) > 1 else axes[0]
    gathered = lax.all_to_all(spread, name, 0, 0, tiled=True)
    return jnp.sum(gathered, axis=0).reshape(shape)


def extended(block, sides, width):
    for axis, dim in sides:
        count = lax.axis_size(axis)
        forward = [(i, i + 1) for i in range(count - 1)]
        backward = [(target, source) for source, target in forward]
        low = lax.ppermute(
            lax.slice_in_dim(block, block.shape[dim] - width, None, axis=dim), axis, forward
        )
        high = lax.ppermute(lax.slice_in_dim(block, 0, width, axis=dim), axis, backward)
        block = jnp.concatenate([low, block, high], axis=dim)
    return block


def merged_chain(part, axis, combine):
    gathered = lax.all_gather(part, axis)

    def take(source):
        return lax.dynamic_index_in_dim(gathered, source, 0, False)

    return lax.fori_loop(
        1, lax.axis_size(axis), lambda source, state: combine(state, take(source)), take(0)
    )


SYM_TILE = 128


def pack_symmetric(matrix):
    order_size = matrix.shape[-1]
    tiles = order_size // SYM_TILE
    rows = [matrix[i * SYM_TILE:(i + 1) * SYM_TILE, i * SYM_TILE:] for i in range(tiles)]
    return jnp.concatenate(rows, axis=1)


def unpack_symmetric(packed, order_size):
    tiles = order_size // SYM_TILE
    starts = []
    offset = 0
    for i in range(tiles):
        starts.append(offset - i * SYM_TILE)
        offset += order_size - i * SYM_TILE

    def tile(i, j):
        begin = starts[i] + j * SYM_TILE
        return packed[:, begin:begin + SYM_TILE]

    rows = []
    for i in range(tiles):
        row = [tile(i, j) if i <= j else tile(j, i).T for j in range(tiles)]
        rows.append(jnp.concatenate(row, axis=1))
    return jnp.concatenate(rows, axis=0)


def merged_tree(part, axis, combine):
    count = lax.axis_size(axis)
    if not is_power_of_two(count):
        return merged_chain(part, axis, combine)
    order_size = part.shape[-1]
    symmetric = order_size % SYM_TILE == 0
    index = lax.axis_index(axis)
    stride = 1
    while stride < count:
        pairs = [(i, i ^ stride) for i in range(count)]
        if symmetric:
            packed = pack_symmetric(part)
            other = unpack_symmetric(lax.ppermute(packed, axis, pairs), order_size)
            part = unpack_symmetric(packed, order_size)
        else:
            other = lax.ppermute(part, axis, pairs)
        upper = (index & stride) != 0
        lower_term = jnp.where(upper, other, part)
        upper_term = jnp.where(upper, part, other)
        part = combine(lower_term, upper_term)
        stride *= 2
    return part


def material_scale(tissue_labels):
    return jnp.where(
        tissue_labels == 0, STIFFNESS[0], jnp.where(tissue_labels == 1, STIFFNESS[1], STIFFNESS[2])
    ).astype(jnp.float32)


def identity_mask(order_size):
    index = jnp.arange(order_size)
    return index[:, None] == index[None, :]


def diagonal_of(matrix):
    eye = identity_mask(matrix.shape[-1])
    return jnp.sum(jnp.where(eye, matrix, 0.0), axis=1)


def masked_coarse(matrix, coarse_order):
    order_size = matrix.shape[-1]
    live = jnp.arange(order_size) < coarse_order
    keep = (live[:, None] & live[None, :]) | identity_mask(order_size)
    return jnp.where(keep, matrix, 0.0)


def newton_inverse(matrix):
    order_size = matrix.shape[-1]
    eye = identity_mask(order_size)
    identity = eye.astype(jnp.float32)
    recip = 1.0 / diagonal_of(matrix)
    product = matrix * recip[None, :]
    approx = recip[:, None] * (2.0 * identity - product)
    for sweep in range(1, NEWTON_STEPS):
        precision = lax.Precision.HIGHEST if sweep + 1 == NEWTON_STEPS else EARLY_PRECISION
        product = jnp.dot(matrix, approx, precision=precision)
        approx = jnp.dot(approx, 2.0 * identity - product, precision=precision)
    return approx


def parallel_sum(left_term, right_term):
    inverse = newton_inverse(left_term + right_term)
    middle = jnp.dot(inverse, left_term, precision=lax.Precision.HIGHEST)
    return left_term - jnp.dot(left_term, middle, precision=lax.Precision.HIGHEST)


def block_apply(vector, diag_blocks, couple_blocks, block_pattern, tissue_labels):
    block_count, block_size = (diag_blocks.shape[0], diag_blocks.shape[1])
    rounded = vector.astype(jnp.bfloat16).reshape(block_count, block_size)
    result = material_scale(tissue_labels)[:, None] * jnp.einsum(
        "rij,rj->ri", diag_blocks, rounded, preferred_element_type=jnp.float32
    )
    gathered = rounded[block_pattern]
    result = result + jnp.einsum(
        "rkij,rkj->ri", couple_blocks, gathered, preferred_element_type=jnp.float32
    )
    backward = jnp.einsum(
        "rkij,ri->rkj", couple_blocks, rounded, preferred_element_type=jnp.float32
    )
    onehot = (block_pattern.reshape(-1)[:, None] == jnp.arange(block_count)[None, :]).astype(
        jnp.float32
    )
    result = result + jnp.einsum(
        "mc,mj->cj", onehot, backward.reshape(-1, block_size), precision=lax.Precision.HIGHEST
    )
    return result.reshape(-1)


def face_tables(face_map, block_count, block_size):
    flat = face_map.reshape(-1)
    rows = (flat[:, None] // block_size == jnp.arange(block_count)[None, :]).astype(jnp.float32)
    lanes = flat[:, None] % block_size == jnp.arange(block_size)[None, :]
    return rows, lanes


def gather_faces(vector, tables):
    rows, lanes = tables
    block_count = rows.shape[1]
    picked = jnp.dot(rows, vector.reshape(block_count, -1), precision=lax.Precision.HIGHEST)
    return jnp.sum(jnp.where(lanes, picked, 0.0), axis=1)


def scatter_faces(result, tables, contribution):
    rows, lanes = tables
    spread = jnp.where(lanes, contribution[:, None], 0.0)
    added = jnp.dot(rows.T, spread, precision=lax.Precision.HIGHEST)
    return result + added.reshape(-1)


def exchange_faces(values):
    across = extended(values[0:2], (("gx", 0),), 1)
    upward = extended(values[2:4], (("gy", 0),), 1)
    return jnp.stack([across[0], across[3], upward[0], upward[3]])


def operate(vector, received, diag_blocks, couple_blocks, block_pattern, tissue_labels, tables):
    result = block_apply(vector, diag_blocks, couple_blocks, block_pattern, tissue_labels)
    return scatter_faces(result, tables, -COUPLING * received.reshape(-1))


def precondition(residual, precond_blocks, tissue_labels, coarse_basis, live_cols, compliance):
    block_count, block_size = (precond_blocks.shape[0], precond_blocks.shape[1])
    rounded = residual.astype(jnp.bfloat16)
    product = jnp.einsum(
        "rij,rj->ri",
        precond_blocks,
        rounded.reshape(block_count, block_size),
        preferred_element_type=jnp.float32,
    )
    local_part = (product / material_scale(tissue_labels)[:, None]).reshape(-1)
    coarse_load = jnp.dot(rounded, coarse_basis, preferred_element_type=jnp.float32) * live_cols
    summed = exchange_sum(coarse_load, ("gx",))
    solved = jnp.dot(compliance, summed, precision=lax.Precision.HIGHEST)
    weights = (solved * live_cols).astype(jnp.bfloat16)
    return local_part + jnp.dot(coarse_basis, weights, preferred_element_type=jnp.float32)


def global_sum(value):
    return exchange_sum(value, ("gx", "gy"))


def body(
    right_side,
    coarse_matrix,
    coarse_order,
    diag_blocks,
    couple_blocks,
    block_pattern,
    tissue_labels,
    precond_blocks,
    coarse_basis,
    face_map,
):
    source = right_side[0, 0]
    matrix = coarse_matrix[0, 0]
    order_here = coarse_order[0, 0]
    diagonal = diag_blocks[0, 0]
    couples = couple_blocks[0, 0]
    pattern = block_pattern[0, 0]
    labels = tissue_labels[0, 0]
    inverses = precond_blocks[0, 0]
    basis = coarse_basis[0, 0]
    faces = face_map[0, 0]
    order_size = matrix.shape[-1]
    live_cols = (jnp.arange(order_size) < order_here).astype(jnp.float32)
    masked = masked_coarse(matrix, order_here)
    merged = merged_tree(masked, "gx", parallel_sum)
    compliance = newton_inverse(merged)
    adjoint = jnp.zeros_like(source)
    residual = source
    precond = precondition(residual, inverses, labels, basis, live_cols, compliance)
    precond_dot = jnp.sum(residual * precond)
    direction = precond
    tables = face_tables(faces, diagonal.shape[0], diagonal.shape[1])
    face_count = faces.shape[0]
    received = exchange_faces(gather_faces(direction, tables).reshape(face_count, -1))
    for iteration in range(ITERS):
        applied = operate(direction, received, diagonal, couples, pattern, labels, tables)
        curvature = jnp.sum(direction * applied)
        if iteration == 0:
            both = global_sum(jnp.stack([precond_dot, curvature]))
            precond_dot, curvature = both[0], both[1]
        else:
            curvature = global_sum(curvature)
        step_size = precond_dot / curvature
        adjoint = adjoint + step_size * direction
        residual = residual - step_size * applied
        if iteration + 1 < ITERS:
            precond = precondition(residual, inverses, labels, basis, live_cols, compliance)
            received_precond = exchange_faces(
                gather_faces(precond, tables).reshape(face_count, -1)
            )
            dot_next = global_sum(jnp.sum(residual * precond))
            ratio = dot_next / precond_dot
            direction = precond + ratio * direction
            received = received_precond + ratio * received
            precond_dot = dot_next
    return (adjoint[None, None], residual[None, None])


def solution(mesh):
    in_specs = (
        P("gx", "gy", None),
        P("gx", "gy", None, None),
        P("gx", "gy"),
        P("gx", "gy", None, None, None),
        P("gx", "gy", None, None, None, None),
        P("gx", "gy", None, None),
        P("gx", "gy", None),
        P("gx", "gy", None, None, None),
        P("gx", "gy", None, None),
        P("gx", "gy", None, None),
    )
    out_specs = (P("gx", "gy", None), P("gx", "gy", None))
    return jax.shard_map(body, mesh=mesh, in_specs=in_specs, out_specs=out_specs, check_vma=False)
```

```python
import jax
import jax.numpy as jnp
from jax import lax
from jax.sharding import PartitionSpec as P

ITERS = 2


STIFFNESS = (1.0, 0.6, 2.0)
COUPLING = 0.5
NEWTON_STEPS = 4
EARLY_PRECISION = lax.Precision.HIGH


def is_power_of_two(count):
    return count > 0 and (count & (count - 1)) == 0


def butterfly_sum(value, axes):
    for axis in axes:
        count = lax.axis_size(axis)
        if not is_power_of_two(count):
            value = lax.psum(value, axis)
            continue
        stride = 1
        while stride < count:
            pairs = [(i, i ^ stride) for i in range(count)]
            value = value + lax.ppermute(value, axis, pairs)
            stride *= 2
    return value


def exchange_sum(value, axes):
    count = 1
    for axis in axes:
        count *= lax.axis_size(axis)
    shape = value.shape
    flat = value.reshape(1, -1)
    spread = jnp.broadcast_to(flat, (count,) + flat.shape[1:])
    name = axes if len(axes) > 1 else axes[0]
    gathered = lax.all_to_all(spread, name, 0, 0, tiled=True)
    return jnp.sum(gathered, axis=0).reshape(shape)


def extended(block, sides, width):
    for axis, dim in sides:
        count = lax.axis_size(axis)
        forward = [(i, i + 1) for i in range(count - 1)]
        backward = [(target, source) for source, target in forward]
        low = lax.ppermute(
            lax.slice_in_dim(block, block.shape[dim] - width, None, axis=dim), axis, forward
        )
        high = lax.ppermute(lax.slice_in_dim(block, 0, width, axis=dim), axis, backward)
        block = jnp.concatenate([low, block, high], axis=dim)
    return block


def merged_chain(part, axis, combine):
    gathered = lax.all_gather(part, axis)

    def take(source):
        return lax.dynamic_index_in_dim(gathered, source, 0, False)

    return lax.fori_loop(
        1, lax.axis_size(axis), lambda source, state: combine(state, take(source)), take(0)
    )


SYM_TILE = 128


def pack_symmetric(matrix):
    order_size = matrix.shape[-1]
    tiles = order_size // SYM_TILE
    rows = [matrix[i * SYM_TILE:(i + 1) * SYM_TILE, i * SYM_TILE:] for i in range(tiles)]
    return jnp.concatenate(rows, axis=1)


def unpack_symmetric(packed, order_size):
    tiles = order_size // SYM_TILE
    starts = []
    offset = 0
    for i in range(tiles):
        starts.append(offset - i * SYM_TILE)
        offset += order_size - i * SYM_TILE

    def tile(i, j):
        begin = starts[i] + j * SYM_TILE
        return packed[:, begin:begin + SYM_TILE]

    rows = []
    for i in range(tiles):
        row = [tile(i, j) if i <= j else tile(j, i).T for j in range(tiles)]
        rows.append(jnp.concatenate(row, axis=1))
    return jnp.concatenate(rows, axis=0)


def merged_tree(part, axis, combine):
    count = lax.axis_size(axis)
    if not is_power_of_two(count):
        return merged_chain(part, axis, combine)
    order_size = part.shape[-1]
    symmetric = order_size % SYM_TILE == 0
    index = lax.axis_index(axis)
    stride = 1
    while stride < count:
        pairs = [(i, i ^ stride) for i in range(count)]
        if symmetric:
            packed = pack_symmetric(part)
            other = unpack_symmetric(lax.ppermute(packed, axis, pairs), order_size)
            part = unpack_symmetric(packed, order_size)
        else:
            other = lax.ppermute(part, axis, pairs)
        upper = (index & stride) != 0
        lower_term = jnp.where(upper, other, part)
        upper_term = jnp.where(upper, part, other)
        part = combine(lower_term, upper_term)
        stride *= 2
    return part


def material_scale(tissue_labels):
    return jnp.where(
        tissue_labels == 0, STIFFNESS[0], jnp.where(tissue_labels == 1, STIFFNESS[1], STIFFNESS[2])
    ).astype(jnp.float32)


def identity_mask(order_size):
    index = jnp.arange(order_size)
    return index[:, None] == index[None, :]


def diagonal_of(matrix):
    eye = identity_mask(matrix.shape[-1])
    return jnp.sum(jnp.where(eye, matrix, 0.0), axis=1)


def masked_coarse(matrix, coarse_order):
    order_size = matrix.shape[-1]
    live = jnp.arange(order_size) < coarse_order
    keep = (live[:, None] & live[None, :]) | identity_mask(order_size)
    return jnp.where(keep, matrix, 0.0)


def newton_inverse(matrix):
    order_size = matrix.shape[-1]
    eye = identity_mask(order_size)
    identity = eye.astype(jnp.float32)
    recip = 1.0 / diagonal_of(matrix)
    product = matrix * recip[None, :]
    approx = recip[:, None] * (2.0 * identity - product)
    for sweep in range(1, NEWTON_STEPS):
        precision = lax.Precision.HIGHEST if sweep + 1 == NEWTON_STEPS else EARLY_PRECISION
        product = jnp.dot(matrix, approx, precision=precision)
        approx = jnp.dot(approx, 2.0 * identity - product, precision=precision)
    return approx


def parallel_sum(left_term, right_term):
    inverse = newton_inverse(left_term + right_term)
    middle = jnp.dot(inverse, left_term, precision=lax.Precision.HIGHEST)
    return left_term - jnp.dot(left_term, middle, precision=lax.Precision.HIGHEST)


def block_apply(vector, diag_blocks, couple_blocks, block_pattern, tissue_labels):
    block_count, block_size = (diag_blocks.shape[0], diag_blocks.shape[1])
    rounded = vector.astype(jnp.bfloat16).reshape(block_count, block_size)
    result = material_scale(tissue_labels)[:, None] * jnp.einsum(
        "rij,rj->ri", diag_blocks, rounded, preferred_element_type=jnp.float32
    )
    gathered = rounded[block_pattern]
    result = result + jnp.einsum(
        "rkij,rkj->ri", couple_blocks, gathered, preferred_element_type=jnp.float32
    )
    backward = jnp.einsum(
        "rkij,ri->rkj", couple_blocks, rounded, preferred_element_type=jnp.float32
    )
    onehot = (block_pattern.reshape(-1)[:, None] == jnp.arange(block_count)[None, :]).astype(
        jnp.float32
    )
    result = result + jnp.einsum(
        "mc,mj->cj", onehot, backward.reshape(-1, block_size), precision=lax.Precision.HIGHEST
    )
    return result.reshape(-1)


def face_tables(face_map, block_count, block_size):
    flat = face_map.reshape(-1)
    rows = (flat[:, None] // block_size == jnp.arange(block_count)[None, :]).astype(jnp.float32)
    lanes = flat[:, None] % block_size == jnp.arange(block_size)[None, :]
    return rows, lanes


def gather_faces(vector, tables):
    rows, lanes = tables
    block_count = rows.shape[1]
    picked = jnp.dot(rows, vector.reshape(block_count, -1), precision=lax.Precision.HIGHEST)
    return jnp.sum(jnp.where(lanes, picked, 0.0), axis=1)


def scatter_faces(result, tables, contribution):
    rows, lanes = tables
    spread = jnp.where(lanes, contribution[:, None], 0.0)
    added = jnp.dot(rows.T, spread, precision=lax.Precision.HIGHEST)
    return result + added.reshape(-1)


def exchange_faces(values):
    across = extended(values[0:2], (("gx", 0),), 1)
    upward = extended(values[2:4], (("gy", 0),), 1)
    return jnp.stack([across[0], across[3], upward[0], upward[3]])


def operate(vector, received, diag_blocks, couple_blocks, block_pattern, tissue_labels, tables):
    result = block_apply(vector, diag_blocks, couple_blocks, block_pattern, tissue_labels)
    contribution = -COUPLING * received.reshape(-1)
    return result, scatter_faces(result, tables, contribution), contribution


def precondition(residual, precond_blocks, tissue_labels, coarse_basis, live_cols, compliance):
    block_count, block_size = (precond_blocks.shape[0], precond_blocks.shape[1])
    rounded = residual.astype(jnp.bfloat16)
    product = jnp.einsum(
        "rij,rj->ri",
        precond_blocks,
        rounded.reshape(block_count, block_size),
        preferred_element_type=jnp.float32,
    )
    local_part = (product / material_scale(tissue_labels)[:, None]).reshape(-1)
    coarse_load = jnp.dot(rounded, coarse_basis, preferred_element_type=jnp.float32) * live_cols
    summed = exchange_sum(coarse_load, ("gx",))
    solved = jnp.dot(compliance, summed, precision=lax.Precision.HIGHEST)
    weights = (solved * live_cols).astype(jnp.bfloat16)
    return local_part + jnp.dot(coarse_basis, weights, preferred_element_type=jnp.float32)


def global_sum(value):
    return exchange_sum(value, ("gx", "gy"))


def body(
    right_side,
    coarse_matrix,
    coarse_order,
    diag_blocks,
    couple_blocks,
    block_pattern,
    tissue_labels,
    precond_blocks,
    coarse_basis,
    face_map,
):
    source = right_side[0, 0]
    matrix = coarse_matrix[0, 0]
    order_here = coarse_order[0, 0]
    diagonal = diag_blocks[0, 0]
    couples = couple_blocks[0, 0]
    pattern = block_pattern[0, 0]
    labels = tissue_labels[0, 0]
    inverses = precond_blocks[0, 0]
    basis = coarse_basis[0, 0]
    faces = face_map[0, 0]
    order_size = matrix.shape[-1]
    live_cols = (jnp.arange(order_size) < order_here).astype(jnp.float32)
    masked = masked_coarse(matrix, order_here)
    merged = merged_tree(masked, "gx", parallel_sum)
    compliance = newton_inverse(merged)
    adjoint = jnp.zeros_like(source)
    residual = source
    precond = precondition(residual, inverses, labels, basis, live_cols, compliance)
    direction = precond
    tables = face_tables(faces, diagonal.shape[0], diagonal.shape[1])
    face_count = faces.shape[0]
    faces_now = gather_faces(direction, tables)
    received = exchange_faces(faces_now.reshape(face_count, -1))
    for iteration in range(ITERS):
        local_image, applied, contribution = operate(
            direction, received, diagonal, couples, pattern, labels, tables
        )
        products = [direction * local_image, contribution * faces_now]
        if iteration == 0:
            products = [residual * precond] + products
        parts = global_sum(jnp.sum(jnp.stack(products), axis=1))
        if iteration == 0:
            precond_dot = parts[0]
        curvature = parts[-2] + parts[-1]
        step_size = precond_dot / curvature
        adjoint = adjoint + step_size * direction
        residual = residual - step_size * applied
        if iteration + 1 < ITERS:
            precond = precondition(residual, inverses, labels, basis, live_cols, compliance)
            faces_precond = gather_faces(precond, tables)
            received_precond = exchange_faces(faces_precond.reshape(face_count, -1))
            dot_next = global_sum(jnp.sum(residual * precond))
            ratio = dot_next / precond_dot
            direction = precond + ratio * direction
            faces_now = faces_precond + ratio * faces_now
            received = received_precond + ratio * received
            precond_dot = dot_next
    return (adjoint[None, None], residual[None, None])


def solution(mesh):
    in_specs = (
        P("gx", "gy", None),
        P("gx", "gy", None, None),
        P("gx", "gy"),
        P("gx", "gy", None, None, None),
        P("gx", "gy", None, None, None, None),
        P("gx", "gy", None, None),
        P("gx", "gy", None),
        P("gx", "gy", None, None, None),
        P("gx", "gy", None, None),
        P("gx", "gy", None, None),
    )
    out_specs = (P("gx", "gy", None), P("gx", "gy", None))
    return jax.shard_map(body, mesh=mesh, in_specs=in_specs, out_specs=out_specs, check_vma=False)
```

```python
import jax
import jax.numpy as jnp
from jax import lax
from jax.sharding import PartitionSpec as P

ITERS = 2


STIFFNESS = (1.0, 0.6, 2.0)
COUPLING = 0.5
NEWTON_STEPS = 4
EARLY_PRECISION = lax.Precision.HIGH


def is_power_of_two(count):
    return count > 0 and (count & (count - 1)) == 0


def butterfly_sum(value, axes):
    for axis in axes:
        count = lax.axis_size(axis)
        if not is_power_of_two(count):
            value = lax.psum(value, axis)
            continue
        stride = 1
        while stride < count:
            pairs = [(i, i ^ stride) for i in range(count)]
            value = value + lax.ppermute(value, axis, pairs)
            stride *= 2
    return value


def exchange_sum(value, axes):
    count = 1
    for axis in axes:
        count *= lax.axis_size(axis)
    shape = value.shape
    flat = value.reshape(1, -1)
    spread = jnp.broadcast_to(flat, (count,) + flat.shape[1:])
    name = axes if len(axes) > 1 else axes[0]
    gathered = lax.all_to_all(spread, name, 0, 0, tiled=True)
    return jnp.sum(gathered, axis=0).reshape(shape)


def extended(block, sides, width):
    for axis, dim in sides:
        count = lax.axis_size(axis)
        forward = [(i, i + 1) for i in range(count - 1)]
        backward = [(target, source) for source, target in forward]
        low = lax.ppermute(
            lax.slice_in_dim(block, block.shape[dim] - width, None, axis=dim), axis, forward
        )
        high = lax.ppermute(lax.slice_in_dim(block, 0, width, axis=dim), axis, backward)
        block = jnp.concatenate([low, block, high], axis=dim)
    return block


def merged_chain(part, axis, combine):
    gathered = lax.all_gather(part, axis)

    def take(source):
        return lax.dynamic_index_in_dim(gathered, source, 0, False)

    return lax.fori_loop(
        1, lax.axis_size(axis), lambda source, state: combine(state, take(source)), take(0)
    )


SYM_TILE = 128


def pack_symmetric(matrix):
    order_size = matrix.shape[-1]
    tiles = order_size // SYM_TILE
    rows = [matrix[i * SYM_TILE:(i + 1) * SYM_TILE, i * SYM_TILE:] for i in range(tiles)]
    return jnp.concatenate(rows, axis=1)


def unpack_symmetric(packed, order_size):
    tiles = order_size // SYM_TILE
    starts = []
    offset = 0
    for i in range(tiles):
        starts.append(offset - i * SYM_TILE)
        offset += order_size - i * SYM_TILE

    def tile(i, j):
        begin = starts[i] + j * SYM_TILE
        return packed[:, begin:begin + SYM_TILE]

    rows = []
    for i in range(tiles):
        row = [tile(i, j) if i <= j else tile(j, i).T for j in range(tiles)]
        rows.append(jnp.concatenate(row, axis=1))
    return jnp.concatenate(rows, axis=0)


def merged_tree(part, axis, combine, side_axis):
    count = lax.axis_size(axis)
    if not is_power_of_two(count):
        return merged_chain(part, axis, combine)
    order_size = part.shape[-1]
    symmetric = order_size % SYM_TILE == 0
    strides = []
    stride = 1
    while stride < count:
        strides.append(stride)
        stride *= 2
    side_count = lax.axis_size(side_axis)
    orders = [strides, strides[1:] + strides[:1]]
    index = lax.axis_index(axis)
    side = lax.axis_index(side_axis)
    for level in range(len(strides)):
        pairs = []
        for i in range(count):
            for j in range(side_count):
                partner = i ^ orders[j % 2][level]
                pairs.append((i * side_count + j, partner * side_count + j))
        level_stride = jnp.where(side % 2 == 0, orders[0][level], orders[1][level])
        if symmetric:
            packed = pack_symmetric(part)
            moved = lax.ppermute(packed, (axis, side_axis), pairs)
            other = unpack_symmetric(moved, order_size)
            part = unpack_symmetric(packed, order_size)
        else:
            other = lax.ppermute(part, (axis, side_axis), pairs)
        upper = (index & level_stride) != 0
        lower_term = jnp.where(upper, other, part)
        upper_term = jnp.where(upper, part, other)
        part = combine(lower_term, upper_term)
    return part


def material_scale(tissue_labels):
    return jnp.where(
        tissue_labels == 0, STIFFNESS[0], jnp.where(tissue_labels == 1, STIFFNESS[1], STIFFNESS[2])
    ).astype(jnp.float32)


def identity_mask(order_size):
    index = jnp.arange(order_size)
    return index[:, None] == index[None, :]


def diagonal_of(matrix):
    eye = identity_mask(matrix.shape[-1])
    return jnp.sum(jnp.where(eye, matrix, 0.0), axis=1)


def masked_coarse(matrix, coarse_order):
    order_size = matrix.shape[-1]
    live = jnp.arange(order_size) < coarse_order
    keep = (live[:, None] & live[None, :]) | identity_mask(order_size)
    return jnp.where(keep, matrix, 0.0)


def newton_inverse(matrix):
    order_size = matrix.shape[-1]
    eye = identity_mask(order_size)
    identity = eye.astype(jnp.float32)
    recip = 1.0 / diagonal_of(matrix)
    product = matrix * recip[None, :]
    approx = recip[:, None] * (2.0 * identity - product)
    for sweep in range(1, NEWTON_STEPS):
        precision = lax.Precision.HIGHEST if sweep + 1 == NEWTON_STEPS else EARLY_PRECISION
        product = jnp.dot(matrix, approx, precision=precision)
        approx = jnp.dot(approx, 2.0 * identity - product, precision=precision)
    return approx


def parallel_sum(left_term, right_term):
    inverse = newton_inverse(left_term + right_term)
    middle = jnp.dot(inverse, left_term, precision=lax.Precision.HIGHEST)
    return left_term - jnp.dot(left_term, middle, precision=lax.Precision.HIGHEST)


def block_apply(vector, diag_blocks, couple_blocks, block_pattern, tissue_labels):
    block_count, block_size = (diag_blocks.shape[0], diag_blocks.shape[1])
    rounded = vector.astype(jnp.bfloat16).reshape(block_count, block_size)
    result = material_scale(tissue_labels)[:, None] * jnp.einsum(
        "rij,rj->ri", diag_blocks, rounded, preferred_element_type=jnp.float32
    )
    gathered = rounded[block_pattern]
    result = result + jnp.einsum(
        "rkij,rkj->ri", couple_blocks, gathered, preferred_element_type=jnp.float32
    )
    backward = jnp.einsum(
        "rkij,ri->rkj", couple_blocks, rounded, preferred_element_type=jnp.float32
    )
    onehot = (block_pattern.reshape(-1)[:, None] == jnp.arange(block_count)[None, :]).astype(
        jnp.float32
    )
    result = result + jnp.einsum(
        "mc,mj->cj", onehot, backward.reshape(-1, block_size), precision=lax.Precision.HIGHEST
    )
    return result.reshape(-1)


def face_tables(face_map, block_count, block_size):
    flat = face_map.reshape(-1)
    rows = (flat[:, None] // block_size == jnp.arange(block_count)[None, :]).astype(jnp.float32)
    lanes = flat[:, None] % block_size == jnp.arange(block_size)[None, :]
    return rows, lanes


def gather_faces(vector, tables):
    rows, lanes = tables
    block_count = rows.shape[1]
    picked = jnp.dot(rows, vector.reshape(block_count, -1), precision=lax.Precision.HIGHEST)
    return jnp.sum(jnp.where(lanes, picked, 0.0), axis=1)


def scatter_faces(result, tables, contribution):
    rows, lanes = tables
    spread = jnp.where(lanes, contribution[:, None], 0.0)
    added = jnp.dot(rows.T, spread, precision=lax.Precision.HIGHEST)
    return result + added.reshape(-1)


def exchange_faces(values):
    across = extended(values[0:2], (("gx", 0),), 1)
    upward = extended(values[2:4], (("gy", 0),), 1)
    return jnp.stack([across[0], across[3], upward[0], upward[3]])


def operate(vector, received, diag_blocks, couple_blocks, block_pattern, tissue_labels, tables):
    result = block_apply(vector, diag_blocks, couple_blocks, block_pattern, tissue_labels)
    contribution = -COUPLING * received.reshape(-1)
    return result, scatter_faces(result, tables, contribution), contribution


def precondition(residual, precond_blocks, tissue_labels, coarse_basis, live_cols, compliance):
    block_count, block_size = (precond_blocks.shape[0], precond_blocks.shape[1])
    rounded = residual.astype(jnp.bfloat16)
    product = jnp.einsum(
        "rij,rj->ri",
        precond_blocks,
        rounded.reshape(block_count, block_size),
        preferred_element_type=jnp.float32,
    )
    local_part = (product / material_scale(tissue_labels)[:, None]).reshape(-1)
    coarse_load = jnp.dot(rounded, coarse_basis, preferred_element_type=jnp.float32) * live_cols
    summed = exchange_sum(coarse_load, ("gx",))
    solved = jnp.dot(compliance, summed, precision=lax.Precision.HIGHEST)
    weights = (solved * live_cols).astype(jnp.bfloat16)
    return local_part + jnp.dot(coarse_basis, weights, preferred_element_type=jnp.float32)


def global_sum(value):
    return exchange_sum(value, ("gx", "gy"))


def body(
    right_side,
    coarse_matrix,
    coarse_order,
    diag_blocks,
    couple_blocks,
    block_pattern,
    tissue_labels,
    precond_blocks,
    coarse_basis,
    face_map,
):
    source = right_side[0, 0]
    matrix = coarse_matrix[0, 0]
    order_here = coarse_order[0, 0]
    diagonal = diag_blocks[0, 0]
    couples = couple_blocks[0, 0]
    pattern = block_pattern[0, 0]
    labels = tissue_labels[0, 0]
    inverses = precond_blocks[0, 0]
    basis = coarse_basis[0, 0]
    faces = face_map[0, 0]
    order_size = matrix.shape[-1]
    live_cols = (jnp.arange(order_size) < order_here).astype(jnp.float32)
    masked = masked_coarse(matrix, order_here)
    merged = merged_tree(masked, "gx", parallel_sum, "gy")
    compliance = newton_inverse(merged)
    adjoint = jnp.zeros_like(source)
    residual = source
    precond = precondition(residual, inverses, labels, basis, live_cols, compliance)
    direction = precond
    tables = face_tables(faces, diagonal.shape[0], diagonal.shape[1])
    face_count = faces.shape[0]
    faces_now = gather_faces(direction, tables)
    received = exchange_faces(faces_now.reshape(face_count, -1))
    for iteration in range(ITERS):
        local_image, applied, contribution = operate(
            direction, received, diagonal, couples, pattern, labels, tables
        )
        products = [direction * local_image, contribution * faces_now]
        if iteration == 0:
            products = [residual * precond] + products
        parts = global_sum(jnp.sum(jnp.stack(products), axis=1))
        if iteration == 0:
            precond_dot = parts[0]
        curvature = parts[-2] + parts[-1]
        step_size = precond_dot / curvature
        adjoint = adjoint + step_size * direction
        residual = residual - step_size * applied
        if iteration + 1 < ITERS:
            precond = precondition(residual, inverses, labels, basis, live_cols, compliance)
            faces_precond = gather_faces(precond, tables)
            received_precond = exchange_faces(faces_precond.reshape(face_count, -1))
            dot_next = global_sum(jnp.sum(residual * precond))
            ratio = dot_next / precond_dot
            direction = precond + ratio * direction
            faces_now = faces_precond + ratio * faces_now
            received = received_precond + ratio * received
            precond_dot = dot_next
    return (adjoint[None, None], residual[None, None])


def solution(mesh):
    in_specs = (
        P("gx", "gy", None),
        P("gx", "gy", None, None),
        P("gx", "gy"),
        P("gx", "gy", None, None, None),
        P("gx", "gy", None, None, None, None),
        P("gx", "gy", None, None),
        P("gx", "gy", None),
        P("gx", "gy", None, None, None),
        P("gx", "gy", None, None),
        P("gx", "gy", None, None),
    )
    out_specs = (P("gx", "gy", None), P("gx", "gy", None))
    return jax.shard_map(body, mesh=mesh, in_specs=in_specs, out_specs=out_specs, check_vma=False)
```

```python
import jax
import jax.numpy as jnp
from jax import lax
from jax.sharding import PartitionSpec as P

ITERS = 2


STIFFNESS = (1.0, 0.6, 2.0)
COUPLING = 0.5
NEWTON_STEPS = 4
EARLY_PRECISION = lax.Precision.HIGH


def is_power_of_two(count):
    return count > 0 and (count & (count - 1)) == 0


def butterfly_sum(value, axes):
    for axis in axes:
        count = lax.axis_size(axis)
        if not is_power_of_two(count):
            value = lax.psum(value, axis)
            continue
        stride = 1
        while stride < count:
            pairs = [(i, i ^ stride) for i in range(count)]
            value = value + lax.ppermute(value, axis, pairs)
            stride *= 2
    return value


def exchange_sum(value, axes):
    count = 1
    for axis in axes:
        count *= lax.axis_size(axis)
    shape = value.shape
    flat = value.reshape(1, -1)
    spread = jnp.broadcast_to(flat, (count,) + flat.shape[1:])
    name = axes if len(axes) > 1 else axes[0]
    gathered = lax.all_to_all(spread, name, 0, 0, tiled=True)
    return jnp.sum(gathered, axis=0).reshape(shape)


def extended(block, sides, width):
    for axis, dim in sides:
        count = lax.axis_size(axis)
        forward = [(i, i + 1) for i in range(count - 1)]
        backward = [(target, source) for source, target in forward]
        low = lax.ppermute(
            lax.slice_in_dim(block, block.shape[dim] - width, None, axis=dim), axis, forward
        )
        high = lax.ppermute(lax.slice_in_dim(block, 0, width, axis=dim), axis, backward)
        block = jnp.concatenate([low, block, high], axis=dim)
    return block


def merged_chain(part, axis, combine):
    gathered = lax.all_gather(part, axis)

    def take(source):
        return lax.dynamic_index_in_dim(gathered, source, 0, False)

    return lax.fori_loop(
        1, lax.axis_size(axis), lambda source, state: combine(state, take(source)), take(0)
    )


SYM_TILE = 128


def pack_symmetric(matrix):
    order_size = matrix.shape[-1]
    tiles = order_size // SYM_TILE
    rows = [matrix[i * SYM_TILE:(i + 1) * SYM_TILE, i * SYM_TILE:] for i in range(tiles)]
    return jnp.concatenate(rows, axis=1)


def unpack_symmetric(packed, order_size):
    tiles = order_size // SYM_TILE
    starts = []
    offset = 0
    for i in range(tiles):
        starts.append(offset - i * SYM_TILE)
        offset += order_size - i * SYM_TILE

    def tile(i, j):
        begin = starts[i] + j * SYM_TILE
        return packed[:, begin:begin + SYM_TILE]

    rows = []
    for i in range(tiles):
        row = [tile(i, j) if i <= j else tile(j, i).T for j in range(tiles)]
        rows.append(jnp.concatenate(row, axis=1))
    return jnp.concatenate(rows, axis=0)


def merged_tree(part, axis, combine, side_axis):
    count = lax.axis_size(axis)
    if not is_power_of_two(count):
        return merged_chain(part, axis, combine)
    order_size = part.shape[-1]
    symmetric = order_size % SYM_TILE == 0
    strides = []
    stride = 1
    while stride < count:
        strides.append(stride)
        stride *= 2
    side_count = lax.axis_size(side_axis)
    if len(strides) >= 3:
        middle = strides[1:-1]
        orders = [[strides[0], strides[-1]] + middle, [strides[-1], strides[0]] + middle]
    else:
        orders = [strides, strides[::-1]]
    index = lax.axis_index(axis)
    side = lax.axis_index(side_axis)
    for level in range(len(strides)):
        pairs = []
        for i in range(count):
            for j in range(side_count):
                partner = i ^ orders[j % 2][level]
                pairs.append((i * side_count + j, partner * side_count + j))
        level_stride = jnp.where(side % 2 == 0, orders[0][level], orders[1][level])
        if symmetric:
            packed = pack_symmetric(part)
            moved = lax.ppermute(packed, (axis, side_axis), pairs)
            other = unpack_symmetric(moved, order_size)
            part = unpack_symmetric(packed, order_size)
        else:
            other = lax.ppermute(part, (axis, side_axis), pairs)
        upper = (index & level_stride) != 0
        lower_term = jnp.where(upper, other, part)
        upper_term = jnp.where(upper, part, other)
        part = combine(lower_term, upper_term)
    return part


def material_scale(tissue_labels):
    return jnp.where(
        tissue_labels == 0, STIFFNESS[0], jnp.where(tissue_labels == 1, STIFFNESS[1], STIFFNESS[2])
    ).astype(jnp.float32)


def identity_mask(order_size):
    index = jnp.arange(order_size)
    return index[:, None] == index[None, :]


def diagonal_of(matrix):
    eye = identity_mask(matrix.shape[-1])
    return jnp.sum(jnp.where(eye, matrix, 0.0), axis=1)


def masked_coarse(matrix, coarse_order):
    order_size = matrix.shape[-1]
    live = jnp.arange(order_size) < coarse_order
    keep = (live[:, None] & live[None, :]) | identity_mask(order_size)
    return jnp.where(keep, matrix, 0.0)


def newton_inverse(matrix):
    order_size = matrix.shape[-1]
    eye = identity_mask(order_size)
    identity = eye.astype(jnp.float32)
    recip = 1.0 / diagonal_of(matrix)
    product = matrix * recip[None, :]
    approx = recip[:, None] * (2.0 * identity - product)
    for sweep in range(1, NEWTON_STEPS):
        precision = lax.Precision.HIGHEST if sweep + 1 == NEWTON_STEPS else EARLY_PRECISION
        product = jnp.dot(matrix, approx, precision=precision)
        approx = jnp.dot(approx, 2.0 * identity - product, precision=precision)
    return approx


def parallel_sum(left_term, right_term):
    inverse = newton_inverse(left_term + right_term)
    middle = jnp.dot(inverse, left_term, precision=lax.Precision.HIGHEST)
    return left_term - jnp.dot(left_term, middle, precision=lax.Precision.HIGHEST)


def block_apply(vector, diag_blocks, couple_blocks, block_pattern, tissue_labels):
    block_count, block_size = (diag_blocks.shape[0], diag_blocks.shape[1])
    rounded = vector.astype(jnp.bfloat16).reshape(block_count, block_size)
    result = material_scale(tissue_labels)[:, None] * jnp.einsum(
        "rij,rj->ri", diag_blocks, rounded, preferred_element_type=jnp.float32
    )
    gathered = rounded[block_pattern]
    result = result + jnp.einsum(
        "rkij,rkj->ri", couple_blocks, gathered, preferred_element_type=jnp.float32
    )
    backward = jnp.einsum(
        "rkij,ri->rkj", couple_blocks, rounded, preferred_element_type=jnp.float32
    )
    onehot = (block_pattern.reshape(-1)[:, None] == jnp.arange(block_count)[None, :]).astype(
        jnp.float32
    )
    result = result + jnp.einsum(
        "mc,mj->cj", onehot, backward.reshape(-1, block_size), precision=lax.Precision.HIGHEST
    )
    return result.reshape(-1)


def face_tables(face_map, block_count, block_size):
    flat = face_map.reshape(-1)
    rows = (flat[:, None] // block_size == jnp.arange(block_count)[None, :]).astype(jnp.float32)
    lanes = flat[:, None] % block_size == jnp.arange(block_size)[None, :]
    return rows, lanes


def gather_faces(vector, tables):
    rows, lanes = tables
    block_count = rows.shape[1]
    picked = jnp.dot(rows, vector.reshape(block_count, -1), precision=lax.Precision.HIGHEST)
    return jnp.sum(jnp.where(lanes, picked, 0.0), axis=1)


def scatter_faces(result, tables, contribution):
    rows, lanes = tables
    spread = jnp.where(lanes, contribution[:, None], 0.0)
    added = jnp.dot(rows.T, spread, precision=lax.Precision.HIGHEST)
    return result + added.reshape(-1)


def exchange_faces(values):
    across = extended(values[0:2], (("gx", 0),), 1)
    upward = extended(values[2:4], (("gy", 0),), 1)
    return jnp.stack([across[0], across[3], upward[0], upward[3]])


def operate(vector, received, diag_blocks, couple_blocks, block_pattern, tissue_labels, tables):
    result = block_apply(vector, diag_blocks, couple_blocks, block_pattern, tissue_labels)
    contribution = -COUPLING * received.reshape(-1)
    return result, scatter_faces(result, tables, contribution), contribution


def precondition(residual, precond_blocks, tissue_labels, coarse_basis, live_cols, compliance):
    block_count, block_size = (precond_blocks.shape[0], precond_blocks.shape[1])
    rounded = residual.astype(jnp.bfloat16)
    product = jnp.einsum(
        "rij,rj->ri",
        precond_blocks,
        rounded.reshape(block_count, block_size),
        preferred_element_type=jnp.float32,
    )
    local_part = (product / material_scale(tissue_labels)[:, None]).reshape(-1)
    coarse_load = jnp.dot(rounded, coarse_basis, preferred_element_type=jnp.float32) * live_cols
    summed = exchange_sum(coarse_load, ("gx",))
    solved = jnp.dot(compliance, summed, precision=lax.Precision.HIGHEST)
    weights = (solved * live_cols).astype(jnp.bfloat16)
    return local_part + jnp.dot(coarse_basis, weights, preferred_element_type=jnp.float32)


def global_sum(value):
    return exchange_sum(value, ("gx", "gy"))


def body(
    right_side,
    coarse_matrix,
    coarse_order,
    diag_blocks,
    couple_blocks,
    block_pattern,
    tissue_labels,
    precond_blocks,
    coarse_basis,
    face_map,
):
    source = right_side[0, 0]
    matrix = coarse_matrix[0, 0]
    order_here = coarse_order[0, 0]
    diagonal = diag_blocks[0, 0]
    couples = couple_blocks[0, 0]
    pattern = block_pattern[0, 0]
    labels = tissue_labels[0, 0]
    inverses = precond_blocks[0, 0]
    basis = coarse_basis[0, 0]
    faces = face_map[0, 0]
    order_size = matrix.shape[-1]
    live_cols = (jnp.arange(order_size) < order_here).astype(jnp.float32)
    masked = masked_coarse(matrix, order_here)
    merged = merged_tree(masked, "gx", parallel_sum, "gy")
    compliance = newton_inverse(merged)
    adjoint = jnp.zeros_like(source)
    residual = source
    precond = precondition(residual, inverses, labels, basis, live_cols, compliance)
    direction = precond
    tables = face_tables(faces, diagonal.shape[0], diagonal.shape[1])
    face_count = faces.shape[0]
    faces_now = gather_faces(direction, tables)
    received = exchange_faces(faces_now.reshape(face_count, -1))
    for iteration in range(ITERS):
        local_image, applied, contribution = operate(
            direction, received, diagonal, couples, pattern, labels, tables
        )
        products = [direction * local_image, contribution * faces_now]
        if iteration == 0:
            products = [residual * precond] + products
        parts = global_sum(jnp.sum(jnp.stack(products), axis=1))
        if iteration == 0:
            precond_dot = parts[0]
        curvature = parts[-2] + parts[-1]
        step_size = precond_dot / curvature
        adjoint = adjoint + step_size * direction
        residual = residual - step_size * applied
        if iteration + 1 < ITERS:
            precond = precondition(residual, inverses, labels, basis, live_cols, compliance)
            faces_precond = gather_faces(precond, tables)
            received_precond = exchange_faces(faces_precond.reshape(face_count, -1))
            dot_next = global_sum(jnp.sum(residual * precond))
            ratio = dot_next / precond_dot
            direction = precond + ratio * direction
            faces_now = faces_precond + ratio * faces_now
            received = received_precond + ratio * received
            precond_dot = dot_next
    return (adjoint[None, None], residual[None, None])


def solution(mesh):
    in_specs = (
        P("gx", "gy", None),
        P("gx", "gy", None, None),
        P("gx", "gy"),
        P("gx", "gy", None, None, None),
        P("gx", "gy", None, None, None, None),
        P("gx", "gy", None, None),
        P("gx", "gy", None),
        P("gx", "gy", None, None, None),
        P("gx", "gy", None, None),
        P("gx", "gy", None, None),
    )
    out_specs = (P("gx", "gy", None), P("gx", "gy", None))
    return jax.shard_map(body, mesh=mesh, in_specs=in_specs, out_specs=out_specs, check_vma=False)
```

```python
import jax
import jax.numpy as jnp
from jax import lax
from jax.sharding import PartitionSpec as P

ITERS = 2


STIFFNESS = (1.0, 0.6, 2.0)
COUPLING = 0.5
NEWTON_STEPS = 4
EARLY_PRECISION = lax.Precision.HIGH


def is_power_of_two(count):
    return count > 0 and (count & (count - 1)) == 0


def butterfly_sum(value, axes):
    for axis in axes:
        count = lax.axis_size(axis)
        if not is_power_of_two(count):
            value = lax.psum(value, axis)
            continue
        stride = 1
        while stride < count:
            pairs = [(i, i ^ stride) for i in range(count)]
            value = value + lax.ppermute(value, axis, pairs)
            stride *= 2
    return value


def exchange_sum(value, axes):
    count = 1
    for axis in axes:
        count *= lax.axis_size(axis)
    shape = value.shape
    flat = value.reshape(1, -1)
    spread = jnp.broadcast_to(flat, (count,) + flat.shape[1:])
    name = axes if len(axes) > 1 else axes[0]
    gathered = lax.all_to_all(spread, name, 0, 0, tiled=True)
    return jnp.sum(gathered, axis=0).reshape(shape)


def extended(block, sides, width):
    for axis, dim in sides:
        count = lax.axis_size(axis)
        forward = [(i, i + 1) for i in range(count - 1)]
        backward = [(target, source) for source, target in forward]
        low = lax.ppermute(
            lax.slice_in_dim(block, block.shape[dim] - width, None, axis=dim), axis, forward
        )
        high = lax.ppermute(lax.slice_in_dim(block, 0, width, axis=dim), axis, backward)
        block = jnp.concatenate([low, block, high], axis=dim)
    return block


def merged_chain(part, axis, combine):
    gathered = lax.all_gather(part, axis)

    def take(source):
        return lax.dynamic_index_in_dim(gathered, source, 0, False)

    return lax.fori_loop(
        1, lax.axis_size(axis), lambda source, state: combine(state, take(source)), take(0)
    )


SYM_TILE = 128


def pack_symmetric(matrix):
    order_size = matrix.shape[-1]
    tiles = order_size // SYM_TILE
    rows = [matrix[i * SYM_TILE:(i + 1) * SYM_TILE, i * SYM_TILE:] for i in range(tiles)]
    return jnp.concatenate(rows, axis=1)


def unpack_symmetric(packed, order_size):
    tiles = order_size // SYM_TILE
    starts = []
    offset = 0
    for i in range(tiles):
        starts.append(offset - i * SYM_TILE)
        offset += order_size - i * SYM_TILE

    def tile(i, j):
        begin = starts[i] + j * SYM_TILE
        return packed[:, begin:begin + SYM_TILE]

    rows = []
    for i in range(tiles):
        row = [tile(i, j) if i <= j else tile(j, i).T for j in range(tiles)]
        rows.append(jnp.concatenate(row, axis=1))
    return jnp.concatenate(rows, axis=0)


def merged_tree(part, axis, combine, side_axis):
    count = lax.axis_size(axis)
    if not is_power_of_two(count):
        return merged_chain(part, axis, combine)
    order_size = part.shape[-1]
    symmetric = order_size % SYM_TILE == 0
    strides = []
    stride = 1
    while stride < count:
        strides.append(stride)
        stride *= 2
    side_count = lax.axis_size(side_axis)
    if len(strides) >= 3:
        middle = strides[1:-1]
        orders = [[strides[0], strides[-1]] + middle, [strides[-1], strides[0]] + middle]
    else:
        orders = [strides, strides[::-1]]
    index = lax.axis_index(axis)
    side = lax.axis_index(side_axis)
    for level in range(len(strides)):
        pairs = []
        for i in range(count):
            for j in range(side_count):
                partner = i ^ orders[j % 2][level]
                pairs.append((i * side_count + j, partner * side_count + j))
        level_stride = jnp.where(side % 2 == 0, orders[0][level], orders[1][level])
        if symmetric:
            packed = pack_symmetric(part)
            moved = lax.ppermute(packed, (axis, side_axis), pairs)
            other = unpack_symmetric(moved, order_size)
            part = unpack_symmetric(packed, order_size)
        else:
            other = lax.ppermute(part, (axis, side_axis), pairs)
        upper = (index & level_stride) != 0
        lower_term = jnp.where(upper, other, part)
        upper_term = jnp.where(upper, part, other)
        part = combine(lower_term, upper_term)
    return part


def material_scale(tissue_labels):
    return jnp.where(
        tissue_labels == 0, STIFFNESS[0], jnp.where(tissue_labels == 1, STIFFNESS[1], STIFFNESS[2])
    ).astype(jnp.float32)


def identity_mask(order_size):
    index = jnp.arange(order_size)
    return index[:, None] == index[None, :]


def diagonal_of(matrix):
    eye = identity_mask(matrix.shape[-1])
    return jnp.sum(jnp.where(eye, matrix, 0.0), axis=1)


def masked_coarse(matrix, coarse_order):
    order_size = matrix.shape[-1]
    live = jnp.arange(order_size) < coarse_order
    keep = (live[:, None] & live[None, :]) | identity_mask(order_size)
    return jnp.where(keep, matrix, 0.0)


def newton_inverse(matrix):
    order_size = matrix.shape[-1]
    eye = identity_mask(order_size)
    identity = eye.astype(jnp.float32)
    recip = 1.0 / diagonal_of(matrix)
    product = matrix * recip[None, :]
    approx = recip[:, None] * (2.0 * identity - product)
    for sweep in range(1, NEWTON_STEPS):
        precision = lax.Precision.HIGHEST if sweep + 1 == NEWTON_STEPS else EARLY_PRECISION
        product = jnp.dot(matrix, approx, precision=precision)
        approx = jnp.dot(approx, 2.0 * identity - product, precision=precision)
    return approx


def parallel_sum(left_term, right_term):
    inverse = newton_inverse(left_term + right_term)
    middle = jnp.dot(inverse, left_term, precision=lax.Precision.HIGHEST)
    return left_term - jnp.dot(left_term, middle, precision=lax.Precision.HIGHEST)


def block_apply(vector, diag_blocks, couple_blocks, block_pattern, tissue_labels):
    block_count, block_size = (diag_blocks.shape[0], diag_blocks.shape[1])
    rounded = vector.astype(jnp.bfloat16).reshape(block_count, block_size)
    result = material_scale(tissue_labels)[:, None] * jnp.einsum(
        "rij,rj->ri", diag_blocks, rounded, preferred_element_type=jnp.float32
    )
    gathered = rounded[block_pattern]
    result = result + jnp.einsum(
        "rkij,rkj->ri", couple_blocks, gathered, preferred_element_type=jnp.float32
    )
    backward = jnp.einsum(
        "rkij,ri->rkj", couple_blocks, rounded, preferred_element_type=jnp.float32
    )
    onehot = (block_pattern.reshape(-1)[:, None] == jnp.arange(block_count)[None, :]).astype(
        jnp.float32
    )
    result = result + jnp.einsum(
        "mc,mj->cj", onehot, backward.reshape(-1, block_size), precision=lax.Precision.HIGHEST
    )
    return result.reshape(-1)


def face_tables(face_map, block_count, block_size):
    flat = face_map.reshape(-1)
    rows = (flat[:, None] // block_size == jnp.arange(block_count)[None, :]).astype(jnp.float32)
    lanes = flat[:, None] % block_size == jnp.arange(block_size)[None, :]
    return rows, lanes


def gather_faces(vector, tables):
    rows, lanes = tables
    block_count = rows.shape[1]
    picked = jnp.dot(rows, vector.reshape(block_count, -1), precision=lax.Precision.HIGHEST)
    return jnp.sum(jnp.where(lanes, picked, 0.0), axis=1)


def scatter_faces(result, tables, contribution):
    rows, lanes = tables
    spread = jnp.where(lanes, contribution[:, None], 0.0)
    added = jnp.dot(rows.T, spread, precision=lax.Precision.HIGHEST)
    return result + added.reshape(-1)


def exchange_faces(values):
    across = extended(values[0:2], (("gx", 0),), 1)
    upward = extended(values[2:4], (("gy", 0),), 1)
    return jnp.stack([across[0], across[3], upward[0], upward[3]])


def sum_and_exchange_faces(partial, values):
    rows, cols = lax.axis_size("gx"), lax.axis_size("gy")
    row, col = lax.axis_index("gx"), lax.axis_index("gy")
    slots = jnp.arange(rows * cols)
    row_step = jnp.array([-1, 1, 0, 0])
    col_step = jnp.array([0, 0, -1, 1])
    near_row, near_col = row + row_step, col + col_step
    inside = (near_row >= 0) & (near_row < rows) & (near_col >= 0) & (near_col < cols)
    near = near_row * cols + near_col
    hits = (slots[:, None] == near[None, :]) & inside[None, :]
    outgoing = jnp.sum(jnp.where(hits[:, :, None], values[None], 0.0), axis=1)
    payload = jnp.concatenate(
        [jnp.broadcast_to(partial.reshape(1, 1), (rows * cols, 1)), outgoing], axis=1
    )
    got = lax.all_to_all(payload, ("gx", "gy"), 0, 0, tiled=True)
    incoming = jnp.sum(jnp.where(hits[:, :, None], got[:, None, 1:], 0.0), axis=0)
    return jnp.sum(got[:, 0]), incoming


def operate(vector, received, diag_blocks, couple_blocks, block_pattern, tissue_labels, tables):
    result = block_apply(vector, diag_blocks, couple_blocks, block_pattern, tissue_labels)
    contribution = -COUPLING * received.reshape(-1)
    return result, scatter_faces(result, tables, contribution), contribution


def precondition(residual, precond_blocks, tissue_labels, coarse_basis, live_cols, compliance):
    block_count, block_size = (precond_blocks.shape[0], precond_blocks.shape[1])
    rounded = residual.astype(jnp.bfloat16)
    product = jnp.einsum(
        "rij,rj->ri",
        precond_blocks,
        rounded.reshape(block_count, block_size),
        preferred_element_type=jnp.float32,
    )
    local_part = (product / material_scale(tissue_labels)[:, None]).reshape(-1)
    coarse_load = jnp.dot(rounded, coarse_basis, preferred_element_type=jnp.float32) * live_cols
    summed = exchange_sum(coarse_load, ("gx",))
    solved = jnp.dot(compliance, summed, precision=lax.Precision.HIGHEST)
    weights = (solved * live_cols).astype(jnp.bfloat16)
    return local_part + jnp.dot(coarse_basis, weights, preferred_element_type=jnp.float32)


def global_sum(value):
    return exchange_sum(value, ("gx", "gy"))


def body(
    right_side,
    coarse_matrix,
    coarse_order,
    diag_blocks,
    couple_blocks,
    block_pattern,
    tissue_labels,
    precond_blocks,
    coarse_basis,
    face_map,
):
    source = right_side[0, 0]
    matrix = coarse_matrix[0, 0]
    order_here = coarse_order[0, 0]
    diagonal = diag_blocks[0, 0]
    couples = couple_blocks[0, 0]
    pattern = block_pattern[0, 0]
    labels = tissue_labels[0, 0]
    inverses = precond_blocks[0, 0]
    basis = coarse_basis[0, 0]
    faces = face_map[0, 0]
    order_size = matrix.shape[-1]
    live_cols = (jnp.arange(order_size) < order_here).astype(jnp.float32)
    masked = masked_coarse(matrix, order_here)
    merged = merged_tree(masked, "gx", parallel_sum, "gy")
    compliance = newton_inverse(merged)
    adjoint = jnp.zeros_like(source)
    residual = source
    precond = precondition(residual, inverses, labels, basis, live_cols, compliance)
    direction = precond
    tables = face_tables(faces, diagonal.shape[0], diagonal.shape[1])
    face_count = faces.shape[0]
    faces_now = gather_faces(direction, tables)
    received = exchange_faces(faces_now.reshape(face_count, -1))
    for iteration in range(ITERS):
        local_image, applied, contribution = operate(
            direction, received, diagonal, couples, pattern, labels, tables
        )
        products = [direction * local_image, contribution * faces_now]
        if iteration == 0:
            products = [residual * precond] + products
        parts = global_sum(jnp.sum(jnp.stack(products), axis=1))
        if iteration == 0:
            precond_dot = parts[0]
        curvature = parts[-2] + parts[-1]
        step_size = precond_dot / curvature
        adjoint = adjoint + step_size * direction
        residual = residual - step_size * applied
        if iteration + 1 < ITERS:
            precond = precondition(residual, inverses, labels, basis, live_cols, compliance)
            faces_precond = gather_faces(precond, tables)
            dot_next, received_precond = sum_and_exchange_faces(
                jnp.sum(residual * precond), faces_precond.reshape(face_count, -1)
            )
            ratio = dot_next / precond_dot
            direction = precond + ratio * direction
            faces_now = faces_precond + ratio * faces_now
            received = received_precond + ratio * received
            precond_dot = dot_next
    return (adjoint[None, None], residual[None, None])


def solution(mesh):
    in_specs = (
        P("gx", "gy", None),
        P("gx", "gy", None, None),
        P("gx", "gy"),
        P("gx", "gy", None, None, None),
        P("gx", "gy", None, None, None, None),
        P("gx", "gy", None, None),
        P("gx", "gy", None),
        P("gx", "gy", None, None, None),
        P("gx", "gy", None, None),
        P("gx", "gy", None, None),
    )
    out_specs = (P("gx", "gy", None), P("gx", "gy", None))
    return jax.shard_map(body, mesh=mesh, in_specs=in_specs, out_specs=out_specs, check_vma=False)
```

```python
import jax
import jax.numpy as jnp
from jax import lax
from jax.sharding import PartitionSpec as P

ITERS = 2


STIFFNESS = (1.0, 0.6, 2.0)
COUPLING = 0.5
NEWTON_STEPS = 4
EARLY_PRECISION = lax.Precision.HIGH


def is_power_of_two(count):
    return count > 0 and (count & (count - 1)) == 0


def butterfly_sum(value, axes):
    for axis in axes:
        count = lax.axis_size(axis)
        if not is_power_of_two(count):
            value = lax.psum(value, axis)
            continue
        stride = 1
        while stride < count:
            pairs = [(i, i ^ stride) for i in range(count)]
            value = value + lax.ppermute(value, axis, pairs)
            stride *= 2
    return value


def exchange_sum(value, axes):
    count = 1
    for axis in axes:
        count *= lax.axis_size(axis)
    shape = value.shape
    flat = value.reshape(1, -1)
    spread = jnp.broadcast_to(flat, (count,) + flat.shape[1:])
    name = axes if len(axes) > 1 else axes[0]
    gathered = lax.all_to_all(spread, name, 0, 0, tiled=True)
    return jnp.sum(gathered, axis=0).reshape(shape)


def extended(block, sides, width):
    for axis, dim in sides:
        count = lax.axis_size(axis)
        forward = [(i, i + 1) for i in range(count - 1)]
        backward = [(target, source) for source, target in forward]
        low = lax.ppermute(
            lax.slice_in_dim(block, block.shape[dim] - width, None, axis=dim), axis, forward
        )
        high = lax.ppermute(lax.slice_in_dim(block, 0, width, axis=dim), axis, backward)
        block = jnp.concatenate([low, block, high], axis=dim)
    return block


def merged_chain(part, axis, combine):
    gathered = lax.all_gather(part, axis)

    def take(source):
        return lax.dynamic_index_in_dim(gathered, source, 0, False)

    return lax.fori_loop(
        1, lax.axis_size(axis), lambda source, state: combine(state, take(source)), take(0)
    )


SYM_TILE = 128


def pack_symmetric(matrix):
    order_size = matrix.shape[-1]
    tiles = order_size // SYM_TILE
    rows = [matrix[i * SYM_TILE:(i + 1) * SYM_TILE, i * SYM_TILE:] for i in range(tiles)]
    return jnp.concatenate(rows, axis=1)


def unpack_symmetric(packed, order_size):
    tiles = order_size // SYM_TILE
    starts = []
    offset = 0
    for i in range(tiles):
        starts.append(offset - i * SYM_TILE)
        offset += order_size - i * SYM_TILE

    def tile(i, j):
        begin = starts[i] + j * SYM_TILE
        return packed[:, begin:begin + SYM_TILE]

    rows = []
    for i in range(tiles):
        row = [tile(i, j) if i <= j else tile(j, i).T for j in range(tiles)]
        rows.append(jnp.concatenate(row, axis=1))
    return jnp.concatenate(rows, axis=0)


def merged_tree(part, axis, combine, side_axis):
    count = lax.axis_size(axis)
    if not is_power_of_two(count):
        return merged_chain(part, axis, combine)
    order_size = part.shape[-1]
    symmetric = order_size % SYM_TILE == 0
    strides = []
    stride = 1
    while stride < count:
        strides.append(stride)
        stride *= 2
    side_count = lax.axis_size(side_axis)
    if len(strides) >= 3:
        middle = strides[1:-1]
        orders = [[strides[0], strides[-1]] + middle, [strides[-1], strides[0]] + middle]
    else:
        orders = [strides, strides[::-1]]
    index = lax.axis_index(axis)
    side = lax.axis_index(side_axis)
    for level in range(len(strides)):
        pairs = []
        for i in range(count):
            for j in range(side_count):
                partner = i ^ orders[j % 2][level]
                pairs.append((i * side_count + j, partner * side_count + j))
        level_stride = jnp.where(side % 2 == 0, orders[0][level], orders[1][level])
        if symmetric:
            packed = pack_symmetric(part)
            moved = lax.ppermute(packed, (axis, side_axis), pairs)
            other = unpack_symmetric(moved, order_size)
            part = unpack_symmetric(packed, order_size)
        else:
            other = lax.ppermute(part, (axis, side_axis), pairs)
        upper = (index & level_stride) != 0
        lower_term = jnp.where(upper, other, part)
        upper_term = jnp.where(upper, part, other)
        part = combine(lower_term, upper_term)
    return part


def material_scale(tissue_labels):
    return jnp.where(
        tissue_labels == 0, STIFFNESS[0], jnp.where(tissue_labels == 1, STIFFNESS[1], STIFFNESS[2])
    ).astype(jnp.float32)


def identity_mask(order_size):
    index = jnp.arange(order_size)
    return index[:, None] == index[None, :]


def diagonal_of(matrix):
    eye = identity_mask(matrix.shape[-1])
    return jnp.sum(jnp.where(eye, matrix, 0.0), axis=1)


def masked_coarse(matrix, coarse_order):
    order_size = matrix.shape[-1]
    live = jnp.arange(order_size) < coarse_order
    keep = (live[:, None] & live[None, :]) | identity_mask(order_size)
    return jnp.where(keep, matrix, 0.0)


def newton_partial(matrix):
    order_size = matrix.shape[-1]
    eye = identity_mask(order_size)
    identity = eye.astype(jnp.float32)
    recip = 1.0 / diagonal_of(matrix)
    product = matrix * recip[None, :]
    approx = recip[:, None] * (2.0 * identity - product)
    for sweep in range(1, NEWTON_STEPS - 1):
        product = jnp.dot(matrix, approx, precision=EARLY_PRECISION)
        approx = jnp.dot(approx, 2.0 * identity - product, precision=EARLY_PRECISION)
    return approx


def newton_last(matrix, approx):
    identity = identity_mask(matrix.shape[-1]).astype(jnp.float32)
    product = jnp.dot(matrix, approx, precision=lax.Precision.HIGHEST)
    return jnp.dot(approx, 2.0 * identity - product, precision=lax.Precision.HIGHEST)


def newton_inverse(matrix):
    return newton_last(matrix, newton_partial(matrix))


def newton_last_apply(matrix, approx, vector):
    inner = jnp.dot(approx, vector, precision=lax.Precision.HIGHEST)
    inner = 2.0 * vector - jnp.dot(matrix, inner, precision=lax.Precision.HIGHEST)
    return jnp.dot(approx, inner, precision=lax.Precision.HIGHEST)


def parallel_sum(left_term, right_term):
    inverse = newton_inverse(left_term + right_term)
    middle = jnp.dot(inverse, left_term, precision=lax.Precision.HIGHEST)
    return left_term - jnp.dot(left_term, middle, precision=lax.Precision.HIGHEST)


def block_apply(vector, diag_blocks, couple_blocks, block_pattern, tissue_labels):
    block_count, block_size = (diag_blocks.shape[0], diag_blocks.shape[1])
    rounded = vector.astype(jnp.bfloat16).reshape(block_count, block_size)
    result = material_scale(tissue_labels)[:, None] * jnp.einsum(
        "rij,rj->ri", diag_blocks, rounded, preferred_element_type=jnp.float32
    )
    gathered = rounded[block_pattern]
    result = result + jnp.einsum(
        "rkij,rkj->ri", couple_blocks, gathered, preferred_element_type=jnp.float32
    )
    backward = jnp.einsum(
        "rkij,ri->rkj", couple_blocks, rounded, preferred_element_type=jnp.float32
    )
    onehot = (block_pattern.reshape(-1)[:, None] == jnp.arange(block_count)[None, :]).astype(
        jnp.float32
    )
    result = result + jnp.einsum(
        "mc,mj->cj", onehot, backward.reshape(-1, block_size), precision=lax.Precision.HIGHEST
    )
    return result.reshape(-1)


def face_tables(face_map, block_count, block_size):
    flat = face_map.reshape(-1)
    rows = (flat[:, None] // block_size == jnp.arange(block_count)[None, :]).astype(jnp.float32)
    lanes = flat[:, None] % block_size == jnp.arange(block_size)[None, :]
    return rows, lanes


def gather_faces(vector, tables):
    rows, lanes = tables
    block_count = rows.shape[1]
    picked = jnp.dot(rows, vector.reshape(block_count, -1), precision=lax.Precision.HIGHEST)
    return jnp.sum(jnp.where(lanes, picked, 0.0), axis=1)


def scatter_faces(result, tables, contribution):
    rows, lanes = tables
    spread = jnp.where(lanes, contribution[:, None], 0.0)
    added = jnp.dot(rows.T, spread, precision=lax.Precision.HIGHEST)
    return result + added.reshape(-1)


def exchange_faces(values):
    across = extended(values[0:2], (("gx", 0),), 1)
    upward = extended(values[2:4], (("gy", 0),), 1)
    return jnp.stack([across[0], across[3], upward[0], upward[3]])


def sum_and_exchange_faces(partial, values):
    rows, cols = lax.axis_size("gx"), lax.axis_size("gy")
    row, col = lax.axis_index("gx"), lax.axis_index("gy")
    slots = jnp.arange(rows * cols)
    row_step = jnp.array([-1, 1, 0, 0])
    col_step = jnp.array([0, 0, -1, 1])
    near_row, near_col = row + row_step, col + col_step
    inside = (near_row >= 0) & (near_row < rows) & (near_col >= 0) & (near_col < cols)
    near = near_row * cols + near_col
    hits = (slots[:, None] == near[None, :]) & inside[None, :]
    outgoing = jnp.sum(jnp.where(hits[:, :, None], values[None], 0.0), axis=1)
    payload = jnp.concatenate(
        [jnp.broadcast_to(partial.reshape(1, 1), (rows * cols, 1)), outgoing], axis=1
    )
    got = lax.all_to_all(payload, ("gx", "gy"), 0, 0, tiled=True)
    incoming = jnp.sum(jnp.where(hits[:, :, None], got[:, None, 1:], 0.0), axis=0)
    return jnp.sum(got[:, 0]), incoming


def operate(vector, received, diag_blocks, couple_blocks, block_pattern, tissue_labels, tables):
    result = block_apply(vector, diag_blocks, couple_blocks, block_pattern, tissue_labels)
    contribution = -COUPLING * received.reshape(-1)
    return result, scatter_faces(result, tables, contribution), contribution


def precondition(residual, precond_blocks, tissue_labels, coarse_basis, live_cols, solve):
    block_count, block_size = (precond_blocks.shape[0], precond_blocks.shape[1])
    rounded = residual.astype(jnp.bfloat16)
    product = jnp.einsum(
        "rij,rj->ri",
        precond_blocks,
        rounded.reshape(block_count, block_size),
        preferred_element_type=jnp.float32,
    )
    local_part = (product / material_scale(tissue_labels)[:, None]).reshape(-1)
    coarse_load = jnp.dot(rounded, coarse_basis, preferred_element_type=jnp.float32) * live_cols
    summed = exchange_sum(coarse_load, ("gx",))
    solved = solve(summed)
    weights = (solved * live_cols).astype(jnp.bfloat16)
    return local_part + jnp.dot(coarse_basis, weights, preferred_element_type=jnp.float32)


def global_sum(value):
    return exchange_sum(value, ("gx", "gy"))


def body(
    right_side,
    coarse_matrix,
    coarse_order,
    diag_blocks,
    couple_blocks,
    block_pattern,
    tissue_labels,
    precond_blocks,
    coarse_basis,
    face_map,
):
    source = right_side[0, 0]
    matrix = coarse_matrix[0, 0]
    order_here = coarse_order[0, 0]
    diagonal = diag_blocks[0, 0]
    couples = couple_blocks[0, 0]
    pattern = block_pattern[0, 0]
    labels = tissue_labels[0, 0]
    inverses = precond_blocks[0, 0]
    basis = coarse_basis[0, 0]
    faces = face_map[0, 0]
    order_size = matrix.shape[-1]
    live_cols = (jnp.arange(order_size) < order_here).astype(jnp.float32)
    masked = masked_coarse(matrix, order_here)
    merged = merged_tree(masked, "gx", parallel_sum, "gy")
    partial = newton_partial(merged)
    compliance = newton_last(merged, partial)
    adjoint = jnp.zeros_like(source)
    residual = source
    precond = precondition(
        residual, inverses, labels, basis, live_cols,
        lambda summed: newton_last_apply(merged, partial, summed),
    )
    direction = precond
    tables = face_tables(faces, diagonal.shape[0], diagonal.shape[1])
    face_count = faces.shape[0]
    faces_now = gather_faces(direction, tables)
    received = exchange_faces(faces_now.reshape(face_count, -1))
    for iteration in range(ITERS):
        local_image, applied, contribution = operate(
            direction, received, diagonal, couples, pattern, labels, tables
        )
        applied = lax.optimization_barrier(applied)
        products = [direction * local_image, contribution * faces_now]
        if iteration == 0:
            products = [residual * precond] + products
        parts = global_sum(jnp.sum(jnp.stack(products), axis=1))
        if iteration == 0:
            precond_dot = parts[0]
        curvature = parts[-2] + parts[-1]
        step_size = precond_dot / curvature
        adjoint = adjoint + step_size * direction
        residual = residual - step_size * applied
        if iteration + 1 < ITERS:
            precond = precondition(
                residual, inverses, labels, basis, live_cols,
                lambda summed: jnp.dot(compliance, summed, precision=lax.Precision.HIGHEST),
            )
            faces_precond = gather_faces(precond, tables)
            dot_next, received_precond = sum_and_exchange_faces(
                jnp.sum(residual * precond), faces_precond.reshape(face_count, -1)
            )
            ratio = dot_next / precond_dot
            direction = precond + ratio * direction
            faces_now = faces_precond + ratio * faces_now
            received = received_precond + ratio * received
            precond_dot = dot_next
    return (adjoint[None, None], residual[None, None])


def solution(mesh):
    in_specs = (
        P("gx", "gy", None),
        P("gx", "gy", None, None),
        P("gx", "gy"),
        P("gx", "gy", None, None, None),
        P("gx", "gy", None, None, None, None),
        P("gx", "gy", None, None),
        P("gx", "gy", None),
        P("gx", "gy", None, None, None),
        P("gx", "gy", None, None),
        P("gx", "gy", None, None),
    )
    out_specs = (P("gx", "gy", None), P("gx", "gy", None))
    return jax.shard_map(body, mesh=mesh, in_specs=in_specs, out_specs=out_specs, check_vma=False)
```

```python
import jax
import jax.numpy as jnp
from jax import lax
from jax.sharding import PartitionSpec as P

ITERS = 2


STIFFNESS = (1.0, 0.6, 2.0)
COUPLING = 0.5
NEWTON_STEPS = 4
EARLY_PRECISION = lax.Precision.HIGH


def is_power_of_two(count):
    return count > 0 and (count & (count - 1)) == 0


def butterfly_sum(value, axes):
    for axis in axes:
        count = lax.axis_size(axis)
        if not is_power_of_two(count):
            value = lax.psum(value, axis)
            continue
        stride = 1
        while stride < count:
            pairs = [(i, i ^ stride) for i in range(count)]
            value = value + lax.ppermute(value, axis, pairs)
            stride *= 2
    return value


def exchange_sum(value, axes):
    count = 1
    for axis in axes:
        count *= lax.axis_size(axis)
    shape = value.shape
    flat = value.reshape(1, -1)
    spread = jnp.broadcast_to(flat, (count,) + flat.shape[1:])
    name = axes if len(axes) > 1 else axes[0]
    gathered = lax.all_to_all(spread, name, 0, 0, tiled=True)
    return jnp.sum(gathered, axis=0).reshape(shape)


def extended(block, sides, width):
    for axis, dim in sides:
        count = lax.axis_size(axis)
        forward = [(i, i + 1) for i in range(count - 1)]
        backward = [(target, source) for source, target in forward]
        low = lax.ppermute(
            lax.slice_in_dim(block, block.shape[dim] - width, None, axis=dim), axis, forward
        )
        high = lax.ppermute(lax.slice_in_dim(block, 0, width, axis=dim), axis, backward)
        block = jnp.concatenate([low, block, high], axis=dim)
    return block


def merged_chain(part, axis, combine):
    gathered = lax.all_gather(part, axis)

    def take(source):
        return lax.dynamic_index_in_dim(gathered, source, 0, False)

    return lax.fori_loop(
        1, lax.axis_size(axis), lambda source, state: combine(state, take(source)), take(0)
    )


SYM_TILE = 128


def pack_symmetric(matrix):
    order_size = matrix.shape[-1]
    tiles = order_size // SYM_TILE
    rows = [matrix[i * SYM_TILE:(i + 1) * SYM_TILE, i * SYM_TILE:] for i in range(tiles)]
    return jnp.concatenate(rows, axis=1)


def unpack_symmetric(packed, order_size):
    tiles = order_size // SYM_TILE
    starts = []
    offset = 0
    for i in range(tiles):
        starts.append(offset - i * SYM_TILE)
        offset += order_size - i * SYM_TILE

    def tile(i, j):
        begin = starts[i] + j * SYM_TILE
        return packed[:, begin:begin + SYM_TILE]

    rows = []
    for i in range(tiles):
        row = [tile(i, j) if i <= j else tile(j, i).T for j in range(tiles)]
        rows.append(jnp.concatenate(row, axis=1))
    return jnp.concatenate(rows, axis=0)


def merged_tree(part, axis, combine, side_axis):
    count = lax.axis_size(axis)
    if not is_power_of_two(count):
        return merged_chain(part, axis, combine)
    order_size = part.shape[-1]
    symmetric = order_size % SYM_TILE == 0
    strides = []
    stride = 1
    while stride < count:
        strides.append(stride)
        stride *= 2
    side_count = lax.axis_size(side_axis)
    if len(strides) >= 3:
        middle = strides[1:-1]
        orders = [[strides[0], strides[-1]] + middle, [strides[-1], strides[0]] + middle]
    else:
        orders = [strides, strides[::-1]]
    index = lax.axis_index(axis)
    side = lax.axis_index(side_axis)
    for level in range(len(strides)):
        pairs = []
        for i in range(count):
            for j in range(side_count):
                partner = i ^ orders[j % 2][level]
                pairs.append((i * side_count + j, partner * side_count + j))
        level_stride = jnp.where(side % 2 == 0, orders[0][level], orders[1][level])
        if symmetric:
            packed = pack_symmetric(part)
            moved = lax.ppermute(packed, (axis, side_axis), pairs)
            other = unpack_symmetric(moved, order_size)
            part = unpack_symmetric(packed, order_size)
        else:
            other = lax.ppermute(part, (axis, side_axis), pairs)
        upper = (index & level_stride) != 0
        lower_term = jnp.where(upper, other, part)
        upper_term = jnp.where(upper, part, other)
        part = combine(lower_term, upper_term)
    return part


def material_scale(tissue_labels):
    return jnp.where(
        tissue_labels == 0, STIFFNESS[0], jnp.where(tissue_labels == 1, STIFFNESS[1], STIFFNESS[2])
    ).astype(jnp.float32)


def identity_mask(order_size):
    index = jnp.arange(order_size)
    return index[:, None] == index[None, :]


def diagonal_of(matrix):
    eye = identity_mask(matrix.shape[-1])
    return jnp.sum(jnp.where(eye, matrix, 0.0), axis=1)


def masked_coarse(matrix, coarse_order):
    order_size = matrix.shape[-1]
    live = jnp.arange(order_size) < coarse_order
    keep = (live[:, None] & live[None, :]) | identity_mask(order_size)
    return jnp.where(keep, matrix, 0.0)


def newton_inverse(matrix):
    order_size = matrix.shape[-1]
    eye = identity_mask(order_size)
    identity = eye.astype(jnp.float32)
    recip = 1.0 / diagonal_of(matrix)
    product = matrix * recip[None, :]
    approx = recip[:, None] * (2.0 * identity - product)
    for sweep in range(1, NEWTON_STEPS):
        precision = lax.Precision.HIGHEST if sweep + 1 == NEWTON_STEPS else EARLY_PRECISION
        product = jnp.dot(matrix, approx, precision=precision)
        approx = jnp.dot(approx, 2.0 * identity - product, precision=precision)
    return approx


def parallel_sum(left_term, right_term):
    inverse = newton_inverse(left_term + right_term)
    middle = jnp.dot(inverse, left_term, precision=lax.Precision.HIGHEST)
    return left_term - jnp.dot(left_term, middle, precision=lax.Precision.HIGHEST)


def block_apply(vector, diag_blocks, couple_blocks, block_pattern, tissue_labels):
    block_count, block_size = (diag_blocks.shape[0], diag_blocks.shape[1])
    rounded = vector.astype(jnp.bfloat16).reshape(block_count, block_size)
    result = material_scale(tissue_labels)[:, None] * jnp.einsum(
        "rij,rj->ri", diag_blocks, rounded, preferred_element_type=jnp.float32
    )
    gathered = rounded[block_pattern]
    result = result + jnp.einsum(
        "rkij,rkj->ri", couple_blocks, gathered, preferred_element_type=jnp.float32
    )
    backward = jnp.einsum(
        "rkij,ri->rkj", couple_blocks, rounded, preferred_element_type=jnp.float32
    )
    onehot = (block_pattern.reshape(-1)[:, None] == jnp.arange(block_count)[None, :]).astype(
        jnp.float32
    )
    result = result + jnp.einsum(
        "mc,mj->cj", onehot, backward.reshape(-1, block_size), precision=lax.Precision.HIGHEST
    )
    return result.reshape(-1)


def face_tables(face_map, block_count, block_size):
    flat = face_map.reshape(-1)
    rows = (flat[:, None] // block_size == jnp.arange(block_count)[None, :]).astype(jnp.float32)
    lanes = flat[:, None] % block_size == jnp.arange(block_size)[None, :]
    return rows, lanes


def gather_faces(vector, tables):
    rows, lanes = tables
    block_count = rows.shape[1]
    picked = jnp.dot(rows, vector.reshape(block_count, -1), precision=lax.Precision.HIGHEST)
    return jnp.sum(jnp.where(lanes, picked, 0.0), axis=1)


def scatter_faces(result, tables, contribution):
    rows, lanes = tables
    spread = jnp.where(lanes, contribution[:, None], 0.0)
    added = jnp.dot(rows.T, spread, precision=lax.Precision.HIGHEST)
    return result + added.reshape(-1)


def exchange_faces(values):
    across = extended(values[0:2], (("gx", 0),), 1)
    upward = extended(values[2:4], (("gy", 0),), 1)
    return jnp.stack([across[0], across[3], upward[0], upward[3]])


def sum_and_exchange_faces(partial, values):
    rows, cols = lax.axis_size("gx"), lax.axis_size("gy")
    row, col = lax.axis_index("gx"), lax.axis_index("gy")
    slots = jnp.arange(rows * cols)
    row_step = jnp.array([-1, 1, 0, 0])
    col_step = jnp.array([0, 0, -1, 1])
    near_row, near_col = row + row_step, col + col_step
    inside = (near_row >= 0) & (near_row < rows) & (near_col >= 0) & (near_col < cols)
    near = near_row * cols + near_col
    hits = (slots[:, None] == near[None, :]) & inside[None, :]
    outgoing = jnp.sum(jnp.where(hits[:, :, None], values[None], 0.0), axis=1)
    payload = jnp.concatenate(
        [jnp.broadcast_to(partial.reshape(1, 1), (rows * cols, 1)), outgoing], axis=1
    )
    got = lax.all_to_all(payload, ("gx", "gy"), 0, 0, tiled=True)
    incoming = jnp.sum(jnp.where(hits[:, :, None], got[:, None, 1:], 0.0), axis=0)
    return jnp.sum(got[:, 0]), incoming


def operate(vector, received, diag_blocks, couple_blocks, block_pattern, tissue_labels, tables):
    result = block_apply(vector, diag_blocks, couple_blocks, block_pattern, tissue_labels)
    contribution = -COUPLING * received.reshape(-1)
    return result, scatter_faces(result, tables, contribution), contribution


def precondition(residual, precond_blocks, tissue_labels, coarse_basis, live_cols, compliance):
    block_count, block_size = (precond_blocks.shape[0], precond_blocks.shape[1])
    rounded = residual.astype(jnp.bfloat16)
    product = jnp.einsum(
        "rij,rj->ri",
        precond_blocks,
        rounded.reshape(block_count, block_size),
        preferred_element_type=jnp.float32,
    )
    local_part = (product / material_scale(tissue_labels)[:, None]).reshape(-1)
    coarse_load = jnp.dot(rounded, coarse_basis, preferred_element_type=jnp.float32) * live_cols
    summed = exchange_sum(coarse_load, ("gx",))
    solved = jnp.dot(compliance, summed, precision=lax.Precision.HIGHEST)
    weights = (solved * live_cols).astype(jnp.bfloat16)
    return local_part + jnp.dot(coarse_basis, weights, preferred_element_type=jnp.float32)


def global_sum(value):
    return exchange_sum(value, ("gx", "gy"))


def body(
    right_side,
    coarse_matrix,
    coarse_order,
    diag_blocks,
    couple_blocks,
    block_pattern,
    tissue_labels,
    precond_blocks,
    coarse_basis,
    face_map,
):
    source = right_side[0, 0]
    matrix = coarse_matrix[0, 0]
    order_here = coarse_order[0, 0]
    diagonal = diag_blocks[0, 0]
    couples = couple_blocks[0, 0]
    pattern = block_pattern[0, 0]
    labels = tissue_labels[0, 0]
    inverses = precond_blocks[0, 0]
    basis = coarse_basis[0, 0]
    faces = face_map[0, 0]
    order_size = matrix.shape[-1]
    live_cols = (jnp.arange(order_size) < order_here).astype(jnp.float32)
    masked = masked_coarse(matrix, order_here)
    merged = merged_tree(masked, "gx", parallel_sum, "gy")
    compliance = newton_inverse(merged)
    adjoint = jnp.zeros_like(source)
    residual = source
    precond = precondition(residual, inverses, labels, basis, live_cols, compliance)
    direction = precond
    tables = face_tables(faces, diagonal.shape[0], diagonal.shape[1])
    face_count = faces.shape[0]
    faces_now = gather_faces(direction, tables)
    received = exchange_faces(faces_now.reshape(face_count, -1))
    for iteration in range(ITERS):
        local_image, applied, contribution = operate(
            direction, received, diagonal, couples, pattern, labels, tables
        )
        applied = lax.optimization_barrier(applied)
        products = [direction * local_image, contribution * faces_now]
        if iteration == 0:
            products = [residual * precond] + products
        parts = global_sum(jnp.sum(jnp.stack(products), axis=1))
        if iteration == 0:
            precond_dot = parts[0]
        curvature = parts[-2] + parts[-1]
        step_size = precond_dot / curvature
        adjoint = adjoint + step_size * direction
        residual = residual - step_size * applied
        if iteration + 1 < ITERS:
            precond = precondition(residual, inverses, labels, basis, live_cols, compliance)
            faces_precond = gather_faces(precond, tables)
            dot_next, received_precond = sum_and_exchange_faces(
                jnp.sum(residual * precond), faces_precond.reshape(face_count, -1)
            )
            ratio = dot_next / precond_dot
            direction = precond + ratio * direction
            faces_now = faces_precond + ratio * faces_now
            received = received_precond + ratio * received
            precond_dot = dot_next
    return (adjoint[None, None], residual[None, None])


def solution(mesh):
    in_specs = (
        P("gx", "gy", None),
        P("gx", "gy", None, None),
        P("gx", "gy"),
        P("gx", "gy", None, None, None),
        P("gx", "gy", None, None, None, None),
        P("gx", "gy", None, None),
        P("gx", "gy", None),
        P("gx", "gy", None, None, None),
        P("gx", "gy", None, None),
        P("gx", "gy", None, None),
    )
    out_specs = (P("gx", "gy", None), P("gx", "gy", None))
    return jax.shard_map(body, mesh=mesh, in_specs=in_specs, out_specs=out_specs, check_vma=False)
```

```python
import jax
import jax.numpy as jnp
from jax import lax
from jax.sharding import PartitionSpec as P

ITERS = 2


STIFFNESS = (1.0, 0.6, 2.0)
COUPLING = 0.5
NEWTON_STEPS = 4
EARLY_PRECISION = lax.Precision.HIGH


def is_power_of_two(count):
    return count > 0 and (count & (count - 1)) == 0


def butterfly_sum(value, axes):
    for axis in axes:
        count = lax.axis_size(axis)
        if not is_power_of_two(count):
            value = lax.psum(value, axis)
            continue
        stride = 1
        while stride < count:
            pairs = [(i, i ^ stride) for i in range(count)]
            value = value + lax.ppermute(value, axis, pairs)
            stride *= 2
    return value


def exchange_sum(value, axes):
    count = 1
    for axis in axes:
        count *= lax.axis_size(axis)
    shape = value.shape
    flat = value.reshape(1, -1)
    spread = jnp.broadcast_to(flat, (count,) + flat.shape[1:])
    name = axes if len(axes) > 1 else axes[0]
    gathered = lax.all_to_all(spread, name, 0, 0, tiled=True)
    return jnp.sum(gathered, axis=0).reshape(shape)


def reduce_to_slots(products, axes):
    count = 1
    for axis in axes:
        count *= lax.axis_size(axis)
    ones = jnp.ones((count, products.shape[-1]), jnp.float32)
    spread = jnp.dot(ones, products.T, precision=lax.Precision.HIGHEST)
    name = axes if len(axes) > 1 else axes[0]
    gathered = lax.all_to_all(spread, name, 0, 0, tiled=True)
    return jnp.sum(gathered, axis=0)


def extended(block, sides, width):
    for axis, dim in sides:
        count = lax.axis_size(axis)
        forward = [(i, i + 1) for i in range(count - 1)]
        backward = [(target, source) for source, target in forward]
        low = lax.ppermute(
            lax.slice_in_dim(block, block.shape[dim] - width, None, axis=dim), axis, forward
        )
        high = lax.ppermute(lax.slice_in_dim(block, 0, width, axis=dim), axis, backward)
        block = jnp.concatenate([low, block, high], axis=dim)
    return block


def merged_chain(part, axis, combine):
    gathered = lax.all_gather(part, axis)

    def take(source):
        return lax.dynamic_index_in_dim(gathered, source, 0, False)

    return lax.fori_loop(
        1, lax.axis_size(axis), lambda source, state: combine(state, take(source)), take(0)
    )


SYM_TILE = 128


def pack_symmetric(matrix):
    order_size = matrix.shape[-1]
    tiles = order_size // SYM_TILE
    rows = [matrix[i * SYM_TILE:(i + 1) * SYM_TILE, i * SYM_TILE:] for i in range(tiles)]
    return jnp.concatenate(rows, axis=1)


def unpack_symmetric(packed, order_size):
    tiles = order_size // SYM_TILE
    starts = []
    offset = 0
    for i in range(tiles):
        starts.append(offset - i * SYM_TILE)
        offset += order_size - i * SYM_TILE

    def tile(i, j):
        begin = starts[i] + j * SYM_TILE
        return packed[:, begin:begin + SYM_TILE]

    rows = []
    for i in range(tiles):
        row = [tile(i, j) if i <= j else tile(j, i).T for j in range(tiles)]
        rows.append(jnp.concatenate(row, axis=1))
    return jnp.concatenate(rows, axis=0)


def merged_tree(part, axis, combine, side_axis):
    count = lax.axis_size(axis)
    if not is_power_of_two(count):
        return merged_chain(part, axis, combine)
    order_size = part.shape[-1]
    symmetric = order_size % SYM_TILE == 0
    strides = []
    stride = 1
    while stride < count:
        strides.append(stride)
        stride *= 2
    side_count = lax.axis_size(side_axis)
    if len(strides) >= 3:
        middle = strides[1:-1]
        orders = [[strides[0], strides[-1]] + middle, [strides[-1], strides[0]] + middle]
    else:
        orders = [strides, strides[::-1]]
    index = lax.axis_index(axis)
    side = lax.axis_index(side_axis)
    for level in range(len(strides)):
        pairs = []
        for i in range(count):
            for j in range(side_count):
                partner = i ^ orders[j % 2][level]
                pairs.append((i * side_count + j, partner * side_count + j))
        level_stride = jnp.where(side % 2 == 0, orders[0][level], orders[1][level])
        if symmetric:
            packed = pack_symmetric(part)
            moved = lax.ppermute(packed, (axis, side_axis), pairs)
            other = unpack_symmetric(moved, order_size)
            part = unpack_symmetric(packed, order_size)
        else:
            other = lax.ppermute(part, (axis, side_axis), pairs)
        upper = (index & level_stride) != 0
        lower_term = jnp.where(upper, other, part)
        upper_term = jnp.where(upper, part, other)
        part = combine(lower_term, upper_term)
    return part


def material_scale(tissue_labels):
    return jnp.where(
        tissue_labels == 0, STIFFNESS[0], jnp.where(tissue_labels == 1, STIFFNESS[1], STIFFNESS[2])
    ).astype(jnp.float32)


def identity_mask(order_size):
    index = jnp.arange(order_size)
    return index[:, None] == index[None, :]


def diagonal_of(matrix):
    eye = identity_mask(matrix.shape[-1])
    return jnp.sum(jnp.where(eye, matrix, 0.0), axis=1)


def masked_coarse(matrix, coarse_order):
    order_size = matrix.shape[-1]
    live = jnp.arange(order_size) < coarse_order
    keep = (live[:, None] & live[None, :]) | identity_mask(order_size)
    return jnp.where(keep, matrix, 0.0)


def newton_inverse(matrix):
    order_size = matrix.shape[-1]
    eye = identity_mask(order_size)
    identity = eye.astype(jnp.float32)
    recip = 1.0 / diagonal_of(matrix)
    product = matrix * recip[None, :]
    approx = recip[:, None] * (2.0 * identity - product)
    for sweep in range(1, NEWTON_STEPS):
        precision = lax.Precision.HIGHEST if sweep + 1 == NEWTON_STEPS else EARLY_PRECISION
        product = jnp.dot(matrix, approx, precision=precision)
        approx = jnp.dot(approx, 2.0 * identity - product, precision=precision)
    return approx


def parallel_sum(left_term, right_term):
    inverse = newton_inverse(left_term + right_term)
    middle = jnp.dot(inverse, left_term, precision=lax.Precision.HIGHEST)
    return left_term - jnp.dot(left_term, middle, precision=lax.Precision.HIGHEST)


def block_apply(vector, diag_blocks, couple_blocks, block_pattern, tissue_labels):
    block_count, block_size = (diag_blocks.shape[0], diag_blocks.shape[1])
    rounded = vector.astype(jnp.bfloat16).reshape(block_count, block_size)
    result = material_scale(tissue_labels)[:, None] * jnp.einsum(
        "rij,rj->ri", diag_blocks, rounded, preferred_element_type=jnp.float32
    )
    gathered = rounded[block_pattern]
    result = result + jnp.einsum(
        "rkij,rkj->ri", couple_blocks, gathered, preferred_element_type=jnp.float32
    )
    backward = jnp.einsum(
        "rkij,ri->rkj", couple_blocks, rounded, preferred_element_type=jnp.float32
    )
    onehot = (block_pattern.reshape(-1)[:, None] == jnp.arange(block_count)[None, :]).astype(
        jnp.float32
    )
    result = result + jnp.einsum(
        "mc,mj->cj", onehot, backward.reshape(-1, block_size), precision=lax.Precision.HIGHEST
    )
    return result.reshape(-1)


def face_tables(face_map, block_count, block_size):
    flat = face_map.reshape(-1)
    rows = (flat[:, None] // block_size == jnp.arange(block_count)[None, :]).astype(jnp.float32)
    lanes = flat[:, None] % block_size == jnp.arange(block_size)[None, :]
    return rows, lanes


def gather_faces(vector, tables):
    rows, lanes = tables
    block_count = rows.shape[1]
    picked = jnp.dot(rows, vector.reshape(block_count, -1), precision=lax.Precision.HIGHEST)
    return jnp.sum(jnp.where(lanes, picked, 0.0), axis=1)


def scatter_faces(result, tables, contribution):
    rows, lanes = tables
    spread = jnp.where(lanes, contribution[:, None], 0.0)
    added = jnp.dot(rows.T, spread, precision=lax.Precision.HIGHEST)
    return result + added.reshape(-1)


def exchange_faces(values):
    across = extended(values[0:2], (("gx", 0),), 1)
    upward = extended(values[2:4], (("gy", 0),), 1)
    return jnp.stack([across[0], across[3], upward[0], upward[3]])


def sum_and_exchange_faces(partial, values):
    rows, cols = lax.axis_size("gx"), lax.axis_size("gy")
    row, col = lax.axis_index("gx"), lax.axis_index("gy")
    slots = jnp.arange(rows * cols)
    row_step = jnp.array([-1, 1, 0, 0])
    col_step = jnp.array([0, 0, -1, 1])
    near_row, near_col = row + row_step, col + col_step
    inside = (near_row >= 0) & (near_row < rows) & (near_col >= 0) & (near_col < cols)
    near = near_row * cols + near_col
    hits = (slots[:, None] == near[None, :]) & inside[None, :]
    outgoing = jnp.sum(jnp.where(hits[:, :, None], values[None], 0.0), axis=1)
    payload = jnp.concatenate(
        [jnp.broadcast_to(partial.reshape(1, 1), (rows * cols, 1)), outgoing], axis=1
    )
    got = lax.all_to_all(payload, ("gx", "gy"), 0, 0, tiled=True)
    incoming = jnp.sum(jnp.where(hits[:, :, None], got[:, None, 1:], 0.0), axis=0)
    return jnp.sum(got[:, 0]), incoming


def operate(vector, received, diag_blocks, couple_blocks, block_pattern, tissue_labels, tables):
    result = block_apply(vector, diag_blocks, couple_blocks, block_pattern, tissue_labels)
    contribution = -COUPLING * received.reshape(-1)
    return result, scatter_faces(result, tables, contribution), contribution


def precondition(residual, precond_blocks, tissue_labels, coarse_basis, live_cols, compliance):
    block_count, block_size = (precond_blocks.shape[0], precond_blocks.shape[1])
    rounded = residual.astype(jnp.bfloat16)
    product = jnp.einsum(
        "rij,rj->ri",
        precond_blocks,
        rounded.reshape(block_count, block_size),
        preferred_element_type=jnp.float32,
    )
    local_part = (product / material_scale(tissue_labels)[:, None]).reshape(-1)
    coarse_load = jnp.dot(rounded, coarse_basis, preferred_element_type=jnp.float32) * live_cols
    summed = exchange_sum(coarse_load, ("gx",))
    solved = jnp.dot(compliance, summed, precision=lax.Precision.HIGHEST)
    weights = (solved * live_cols).astype(jnp.bfloat16)
    return local_part + jnp.dot(coarse_basis, weights, preferred_element_type=jnp.float32)


def global_sum(value):
    return exchange_sum(value, ("gx", "gy"))


def body(
    right_side,
    coarse_matrix,
    coarse_order,
    diag_blocks,
    couple_blocks,
    block_pattern,
    tissue_labels,
    precond_blocks,
    coarse_basis,
    face_map,
):
    source = right_side[0, 0]
    matrix = coarse_matrix[0, 0]
    order_here = coarse_order[0, 0]
    diagonal = diag_blocks[0, 0]
    couples = couple_blocks[0, 0]
    pattern = block_pattern[0, 0]
    labels = tissue_labels[0, 0]
    inverses = precond_blocks[0, 0]
    basis = coarse_basis[0, 0]
    faces = face_map[0, 0]
    order_size = matrix.shape[-1]
    live_cols = (jnp.arange(order_size) < order_here).astype(jnp.float32)
    masked = masked_coarse(matrix, order_here)
    merged = merged_tree(masked, "gx", parallel_sum, "gy")
    compliance = newton_inverse(merged)
    adjoint = jnp.zeros_like(source)
    residual = source
    precond = precondition(residual, inverses, labels, basis, live_cols, compliance)
    direction = precond
    tables = face_tables(faces, diagonal.shape[0], diagonal.shape[1])
    face_count = faces.shape[0]
    faces_now = gather_faces(direction, tables)
    received = exchange_faces(faces_now.reshape(face_count, -1))
    for iteration in range(ITERS):
        local_image, applied, contribution = operate(
            direction, received, diagonal, couples, pattern, labels, tables
        )
        applied = lax.optimization_barrier(applied)
        products = [direction * local_image, contribution * faces_now]
        if iteration == 0:
            products = [residual * precond] + products
        parts = reduce_to_slots(jnp.stack(products), ("gx", "gy"))
        if iteration == 0:
            precond_dot = parts[0]
        curvature = parts[-2] + parts[-1]
        step_size = precond_dot / curvature
        adjoint = adjoint + step_size * direction
        residual = residual - step_size * applied
        if iteration + 1 < ITERS:
            precond = precondition(residual, inverses, labels, basis, live_cols, compliance)
            faces_precond = gather_faces(precond, tables)
            dot_next, received_precond = sum_and_exchange_faces(
                jnp.sum(residual * precond), faces_precond.reshape(face_count, -1)
            )
            ratio = dot_next / precond_dot
            direction = precond + ratio * direction
            faces_now = faces_precond + ratio * faces_now
            received = received_precond + ratio * received
            precond_dot = dot_next
    return (adjoint[None, None], residual[None, None])


def solution(mesh):
    in_specs = (
        P("gx", "gy", None),
        P("gx", "gy", None, None),
        P("gx", "gy"),
        P("gx", "gy", None, None, None),
        P("gx", "gy", None, None, None, None),
        P("gx", "gy", None, None),
        P("gx", "gy", None),
        P("gx", "gy", None, None, None),
        P("gx", "gy", None, None),
        P("gx", "gy", None, None),
    )
    out_specs = (P("gx", "gy", None), P("gx", "gy", None))
    return jax.shard_map(body, mesh=mesh, in_specs=in_specs, out_specs=out_specs, check_vma=False)
```

```python
import jax
import jax.numpy as jnp
from jax import lax
from jax.sharding import PartitionSpec as P

ITERS = 2


STIFFNESS = (1.0, 0.6, 2.0)
COUPLING = 0.5
NEWTON_STEPS = 4
EARLY_PRECISION = lax.Precision.HIGH


def is_power_of_two(count):
    return count > 0 and (count & (count - 1)) == 0


def butterfly_sum(value, axes):
    for axis in axes:
        count = lax.axis_size(axis)
        if not is_power_of_two(count):
            value = lax.psum(value, axis)
            continue
        stride = 1
        while stride < count:
            pairs = [(i, i ^ stride) for i in range(count)]
            value = value + lax.ppermute(value, axis, pairs)
            stride *= 2
    return value


def exchange_sum(value, axes):
    count = 1
    for axis in axes:
        count *= lax.axis_size(axis)
    shape = value.shape
    flat = value.reshape(1, -1)
    spread = jnp.broadcast_to(flat, (count,) + flat.shape[1:])
    name = axes if len(axes) > 1 else axes[0]
    gathered = lax.all_to_all(spread, name, 0, 0, tiled=True)
    return jnp.sum(gathered, axis=0).reshape(shape)


def extended(block, sides, width):
    for axis, dim in sides:
        count = lax.axis_size(axis)
        forward = [(i, i + 1) for i in range(count - 1)]
        backward = [(target, source) for source, target in forward]
        low = lax.ppermute(
            lax.slice_in_dim(block, block.shape[dim] - width, None, axis=dim), axis, forward
        )
        high = lax.ppermute(lax.slice_in_dim(block, 0, width, axis=dim), axis, backward)
        block = jnp.concatenate([low, block, high], axis=dim)
    return block


def merged_chain(part, axis, combine):
    gathered = lax.all_gather(part, axis)

    def take(source):
        return lax.dynamic_index_in_dim(gathered, source, 0, False)

    return lax.fori_loop(
        1, lax.axis_size(axis), lambda source, state: combine(state, take(source)), take(0)
    )


SYM_TILE = 128


def pack_symmetric(matrix):
    order_size = matrix.shape[-1]
    tiles = order_size // SYM_TILE
    rows = [matrix[i * SYM_TILE:(i + 1) * SYM_TILE, i * SYM_TILE:] for i in range(tiles)]
    return jnp.concatenate(rows, axis=1)


def unpack_symmetric(packed, order_size):
    tiles = order_size // SYM_TILE
    starts = []
    offset = 0
    for i in range(tiles):
        starts.append(offset - i * SYM_TILE)
        offset += order_size - i * SYM_TILE

    def tile(i, j):
        begin = starts[i] + j * SYM_TILE
        return packed[:, begin:begin + SYM_TILE]

    rows = []
    for i in range(tiles):
        row = [tile(i, j) if i <= j else tile(j, i).T for j in range(tiles)]
        rows.append(jnp.concatenate(row, axis=1))
    return jnp.concatenate(rows, axis=0)


def merged_tree(part, axis, combine, side_axis, order_here):
    count = lax.axis_size(axis)
    if not is_power_of_two(count):
        return merged_chain(masked_coarse(part, order_here), axis, combine)
    order_size = part.shape[-1]
    symmetric = order_size % SYM_TILE == 0
    strides = []
    stride = 1
    while stride < count:
        strides.append(stride)
        stride *= 2
    side_count = lax.axis_size(side_axis)
    if len(strides) >= 3:
        middle = strides[1:-1]
        orders = [[strides[0], strides[-1]] + middle, [strides[-1], strides[0]] + middle]
    else:
        orders = [strides, strides[::-1]]
    index = lax.axis_index(axis)
    side = lax.axis_index(side_axis)
    for level in range(len(strides)):
        pairs = []
        for i in range(count):
            for j in range(side_count):
                partner = i ^ orders[j % 2][level]
                pairs.append((i * side_count + j, partner * side_count + j))
        level_stride = jnp.where(side % 2 == 0, orders[0][level], orders[1][level])
        if symmetric:
            packed = pack_symmetric(part)
            moved = lax.ppermute(packed, (axis, side_axis), pairs)
            other = unpack_symmetric(moved, order_size)
            part = unpack_symmetric(packed, order_size)
        else:
            other = lax.ppermute(part, (axis, side_axis), pairs)
        if level == 0:
            order_value = order_here.astype(jnp.float32).reshape(1)
            other_order = lax.ppermute(order_value, (axis, side_axis), pairs)
            other = masked_coarse(other, other_order[0].astype(jnp.int32))
            part = masked_coarse(part, order_here)
        upper = (index & level_stride) != 0
        lower_term = jnp.where(upper, other, part)
        upper_term = jnp.where(upper, part, other)
        part = combine(lower_term, upper_term)
    return part


def material_scale(tissue_labels):
    return jnp.where(
        tissue_labels == 0, STIFFNESS[0], jnp.where(tissue_labels == 1, STIFFNESS[1], STIFFNESS[2])
    ).astype(jnp.float32)


def identity_mask(order_size):
    index = jnp.arange(order_size)
    return index[:, None] == index[None, :]


def diagonal_of(matrix):
    eye = identity_mask(matrix.shape[-1])
    return jnp.sum(jnp.where(eye, matrix, 0.0), axis=1)


def masked_coarse(matrix, coarse_order):
    order_size = matrix.shape[-1]
    live = jnp.arange(order_size) < coarse_order
    keep = (live[:, None] & live[None, :]) | identity_mask(order_size)
    return jnp.where(keep, matrix, 0.0)


def newton_inverse(matrix):
    order_size = matrix.shape[-1]
    eye = identity_mask(order_size)
    identity = eye.astype(jnp.float32)
    recip = 1.0 / diagonal_of(matrix)
    product = matrix * recip[None, :]
    approx = recip[:, None] * (2.0 * identity - product)
    for sweep in range(1, NEWTON_STEPS):
        precision = lax.Precision.HIGHEST if sweep + 1 == NEWTON_STEPS else EARLY_PRECISION
        product = jnp.dot(matrix, approx, precision=precision)
        approx = jnp.dot(approx, 2.0 * identity - product, precision=precision)
    return approx


def parallel_sum(left_term, right_term):
    inverse = newton_inverse(left_term + right_term)
    middle = jnp.dot(inverse, left_term, precision=lax.Precision.HIGHEST)
    return left_term - jnp.dot(left_term, middle, precision=lax.Precision.HIGHEST)


def block_apply(vector, diag_blocks, couple_blocks, block_pattern, tissue_labels):
    block_count, block_size = (diag_blocks.shape[0], diag_blocks.shape[1])
    rounded = vector.astype(jnp.bfloat16).reshape(block_count, block_size)
    result = material_scale(tissue_labels)[:, None] * jnp.einsum(
        "rij,rj->ri", diag_blocks, rounded, preferred_element_type=jnp.float32
    )
    gathered = rounded[block_pattern]
    result = result + jnp.einsum(
        "rkij,rkj->ri", couple_blocks, gathered, preferred_element_type=jnp.float32
    )
    backward = jnp.einsum(
        "rkij,ri->rkj", couple_blocks, rounded, preferred_element_type=jnp.float32
    )
    onehot = (block_pattern.reshape(-1)[:, None] == jnp.arange(block_count)[None, :]).astype(
        jnp.float32
    )
    result = result + jnp.einsum(
        "mc,mj->cj", onehot, backward.reshape(-1, block_size), precision=lax.Precision.HIGHEST
    )
    return result.reshape(-1)


def face_tables(face_map, block_count, block_size):
    flat = face_map.reshape(-1)
    rows = (flat[:, None] // block_size == jnp.arange(block_count)[None, :]).astype(jnp.float32)
    lanes = flat[:, None] % block_size == jnp.arange(block_size)[None, :]
    return rows, lanes


def gather_faces(vector, tables):
    rows, lanes = tables
    block_count = rows.shape[1]
    picked = jnp.dot(rows, vector.reshape(block_count, -1), precision=lax.Precision.HIGHEST)
    return jnp.sum(jnp.where(lanes, picked, 0.0), axis=1)


def scatter_faces(result, tables, contribution):
    rows, lanes = tables
    spread = jnp.where(lanes, contribution[:, None], 0.0)
    added = jnp.dot(rows.T, spread, precision=lax.Precision.HIGHEST)
    return result + added.reshape(-1)


def exchange_faces(values):
    across = extended(values[0:2], (("gx", 0),), 1)
    upward = extended(values[2:4], (("gy", 0),), 1)
    return jnp.stack([across[0], across[3], upward[0], upward[3]])


def sum_and_exchange_faces(partial, values):
    rows, cols = lax.axis_size("gx"), lax.axis_size("gy")
    row, col = lax.axis_index("gx"), lax.axis_index("gy")
    slots = jnp.arange(rows * cols)
    row_step = jnp.array([-1, 1, 0, 0])
    col_step = jnp.array([0, 0, -1, 1])
    near_row, near_col = row + row_step, col + col_step
    inside = (near_row >= 0) & (near_row < rows) & (near_col >= 0) & (near_col < cols)
    near = near_row * cols + near_col
    hits = (slots[:, None] == near[None, :]) & inside[None, :]
    outgoing = jnp.sum(jnp.where(hits[:, :, None], values[None], 0.0), axis=1)
    payload = jnp.concatenate(
        [jnp.broadcast_to(partial.reshape(1, 1), (rows * cols, 1)), outgoing], axis=1
    )
    got = lax.all_to_all(payload, ("gx", "gy"), 0, 0, tiled=True)
    incoming = jnp.sum(jnp.where(hits[:, :, None], got[:, None, 1:], 0.0), axis=0)
    return jnp.sum(got[:, 0]), incoming


def operate(vector, received, diag_blocks, couple_blocks, block_pattern, tissue_labels, tables):
    result = block_apply(vector, diag_blocks, couple_blocks, block_pattern, tissue_labels)
    contribution = -COUPLING * received.reshape(-1)
    return result, scatter_faces(result, tables, contribution), contribution


def precondition(residual, precond_blocks, tissue_labels, coarse_basis, live_cols, compliance):
    block_count, block_size = (precond_blocks.shape[0], precond_blocks.shape[1])
    rounded = residual.astype(jnp.bfloat16)
    product = jnp.einsum(
        "rij,rj->ri",
        precond_blocks,
        rounded.reshape(block_count, block_size),
        preferred_element_type=jnp.float32,
    )
    local_part = (product / material_scale(tissue_labels)[:, None]).reshape(-1)
    coarse_load = jnp.dot(rounded, coarse_basis, preferred_element_type=jnp.float32) * live_cols
    summed = exchange_sum(coarse_load, ("gx",))
    solved = jnp.dot(compliance, summed, precision=lax.Precision.HIGHEST)
    weights = (solved * live_cols).astype(jnp.bfloat16)
    return local_part + jnp.dot(coarse_basis, weights, preferred_element_type=jnp.float32)


def global_sum(value):
    return exchange_sum(value, ("gx", "gy"))


def body(
    right_side,
    coarse_matrix,
    coarse_order,
    diag_blocks,
    couple_blocks,
    block_pattern,
    tissue_labels,
    precond_blocks,
    coarse_basis,
    face_map,
):
    source = right_side[0, 0]
    matrix = coarse_matrix[0, 0]
    order_here = coarse_order[0, 0]
    diagonal = diag_blocks[0, 0]
    couples = couple_blocks[0, 0]
    pattern = block_pattern[0, 0]
    labels = tissue_labels[0, 0]
    inverses = precond_blocks[0, 0]
    basis = coarse_basis[0, 0]
    faces = face_map[0, 0]
    order_size = matrix.shape[-1]
    live_cols = (jnp.arange(order_size) < order_here).astype(jnp.float32)
    merged = merged_tree(matrix, "gx", parallel_sum, "gy", order_here)
    compliance = newton_inverse(merged)
    adjoint = jnp.zeros_like(source)
    residual = source
    precond = precondition(residual, inverses, labels, basis, live_cols, compliance)
    direction = precond
    tables = face_tables(faces, diagonal.shape[0], diagonal.shape[1])
    face_count = faces.shape[0]
    faces_now = gather_faces(direction, tables)
    received = exchange_faces(faces_now.reshape(face_count, -1))
    for iteration in range(ITERS):
        local_image, applied, contribution = operate(
            direction, received, diagonal, couples, pattern, labels, tables
        )
        applied = lax.optimization_barrier(applied)
        products = [direction * local_image, contribution * faces_now]
        if iteration == 0:
            products = [residual * precond] + products
        parts = global_sum(jnp.sum(jnp.stack(products), axis=1))
        if iteration == 0:
            precond_dot = parts[0]
        curvature = parts[-2] + parts[-1]
        step_size = precond_dot / curvature
        adjoint = adjoint + step_size * direction
        residual = residual - step_size * applied
        if iteration + 1 < ITERS:
            precond = precondition(residual, inverses, labels, basis, live_cols, compliance)
            faces_precond = gather_faces(precond, tables)
            dot_next, received_precond = sum_and_exchange_faces(
                jnp.sum(residual * precond), faces_precond.reshape(face_count, -1)
            )
            ratio = dot_next / precond_dot
            direction = precond + ratio * direction
            faces_now = faces_precond + ratio * faces_now
            received = received_precond + ratio * received
            precond_dot = dot_next
    return (adjoint[None, None], residual[None, None])


def solution(mesh):
    in_specs = (
        P("gx", "gy", None),
        P("gx", "gy", None, None),
        P("gx", "gy"),
        P("gx", "gy", None, None, None),
        P("gx", "gy", None, None, None, None),
        P("gx", "gy", None, None),
        P("gx", "gy", None),
        P("gx", "gy", None, None, None),
        P("gx", "gy", None, None),
        P("gx", "gy", None, None),
    )
    out_specs = (P("gx", "gy", None), P("gx", "gy", None))
    return jax.shard_map(body, mesh=mesh, in_specs=in_specs, out_specs=out_specs, check_vma=False)
```

```python
import jax
import jax.numpy as jnp
from jax import lax
from jax.sharding import PartitionSpec as P

ITERS = 2


STIFFNESS = (1.0, 0.6, 2.0)
COUPLING = 0.5
NEWTON_STEPS = 4
EARLY_PRECISION = lax.Precision.HIGH


def is_power_of_two(count):
    return count > 0 and (count & (count - 1)) == 0


def butterfly_sum(value, axes):
    for axis in axes:
        count = lax.axis_size(axis)
        if not is_power_of_two(count):
            value = lax.psum(value, axis)
            continue
        stride = 1
        while stride < count:
            pairs = [(i, i ^ stride) for i in range(count)]
            value = value + lax.ppermute(value, axis, pairs)
            stride *= 2
    return value


def exchange_sum(value, axes):
    count = 1
    for axis in axes:
        count *= lax.axis_size(axis)
    shape = value.shape
    flat = value.reshape(1, -1)
    spread = jnp.broadcast_to(flat, (count,) + flat.shape[1:])
    name = axes if len(axes) > 1 else axes[0]
    gathered = lax.all_to_all(spread, name, 0, 0, tiled=True)
    return jnp.sum(gathered, axis=0).reshape(shape)


def extended(block, sides, width):
    for axis, dim in sides:
        count = lax.axis_size(axis)
        forward = [(i, i + 1) for i in range(count - 1)]
        backward = [(target, source) for source, target in forward]
        low = lax.ppermute(
            lax.slice_in_dim(block, block.shape[dim] - width, None, axis=dim), axis, forward
        )
        high = lax.ppermute(lax.slice_in_dim(block, 0, width, axis=dim), axis, backward)
        block = jnp.concatenate([low, block, high], axis=dim)
    return block


def merged_chain(part, axis, combine):
    gathered = lax.all_gather(part, axis)

    def take(source):
        return lax.dynamic_index_in_dim(gathered, source, 0, False)

    return lax.fori_loop(
        1, lax.axis_size(axis), lambda source, state: combine(state, take(source)), take(0)
    )


SYM_TILE = 128


def pack_symmetric(matrix):
    order_size = matrix.shape[-1]
    tiles = order_size // SYM_TILE
    rows = [matrix[i * SYM_TILE:(i + 1) * SYM_TILE, i * SYM_TILE:] for i in range(tiles)]
    return jnp.concatenate(rows, axis=1)


def unpack_symmetric(packed, order_size):
    tiles = order_size // SYM_TILE
    starts = []
    offset = 0
    for i in range(tiles):
        starts.append(offset - i * SYM_TILE)
        offset += order_size - i * SYM_TILE

    def tile(i, j):
        begin = starts[i] + j * SYM_TILE
        return packed[:, begin:begin + SYM_TILE]

    rows = []
    for i in range(tiles):
        row = [tile(i, j) if i <= j else tile(j, i).T for j in range(tiles)]
        rows.append(jnp.concatenate(row, axis=1))
    return jnp.concatenate(rows, axis=0)


def merged_tree(part, axis, combine, side_axis):
    count = lax.axis_size(axis)
    if not is_power_of_two(count):
        return merged_chain(part, axis, combine)
    order_size = part.shape[-1]
    symmetric = order_size % SYM_TILE == 0
    strides = []
    stride = 1
    while stride < count:
        strides.append(stride)
        stride *= 2
    side_count = lax.axis_size(side_axis)
    if len(strides) >= 3:
        middle = strides[1:-1]
        orders = [[strides[0], strides[-1]] + middle, [strides[-1], strides[0]] + middle]
    else:
        orders = [strides, strides[::-1]]
    index = lax.axis_index(axis)
    side = lax.axis_index(side_axis)
    for level in range(len(strides)):
        pairs = []
        for i in range(count):
            for j in range(side_count):
                partner = i ^ orders[j % 2][level]
                pairs.append((i * side_count + j, partner * side_count + j))
        level_stride = jnp.where(side % 2 == 0, orders[0][level], orders[1][level])
        if symmetric:
            packed = pack_symmetric(part)
            moved = lax.ppermute(packed, (axis, side_axis), pairs)
            other = unpack_symmetric(moved, order_size)
            part = unpack_symmetric(packed, order_size)
        else:
            other = lax.ppermute(part, (axis, side_axis), pairs)
        upper = (index & level_stride) != 0
        lower_term = jnp.where(upper, other, part)
        upper_term = jnp.where(upper, part, other)
        part = combine(lower_term, upper_term)
    return part


def material_scale(tissue_labels):
    return jnp.where(
        tissue_labels == 0, STIFFNESS[0], jnp.where(tissue_labels == 1, STIFFNESS[1], STIFFNESS[2])
    ).astype(jnp.float32)


def identity_mask(order_size):
    index = jnp.arange(order_size)
    return index[:, None] == index[None, :]


def diagonal_of(matrix):
    eye = identity_mask(matrix.shape[-1])
    return jnp.sum(jnp.where(eye, matrix, 0.0), axis=1)


def masked_coarse(matrix, coarse_order):
    order_size = matrix.shape[-1]
    live = jnp.arange(order_size) < coarse_order
    keep = (live[:, None] & live[None, :]) | identity_mask(order_size)
    return jnp.where(keep, matrix, 0.0)


def newton_inverse(matrix):
    order_size = matrix.shape[-1]
    eye = identity_mask(order_size)
    identity = eye.astype(jnp.float32)
    recip = 1.0 / diagonal_of(matrix)
    product = matrix * recip[None, :]
    approx = recip[:, None] * (2.0 * identity - product)
    for sweep in range(1, NEWTON_STEPS):
        if sweep + 1 == NEWTON_STEPS:
            precision = lax.Precision.HIGHEST
        elif sweep == 1:
            precision = lax.Precision.DEFAULT
        else:
            precision = EARLY_PRECISION
        product = jnp.dot(matrix, approx, precision=precision)
        approx = jnp.dot(approx, 2.0 * identity - product, precision=precision)
    return approx


def parallel_sum(left_term, right_term):
    inverse = newton_inverse(left_term + right_term)
    middle = jnp.dot(inverse, left_term, precision=lax.Precision.HIGHEST)
    return left_term - jnp.dot(left_term, middle, precision=lax.Precision.HIGHEST)


def block_apply(vector, diag_blocks, couple_blocks, block_pattern, tissue_labels):
    block_count, block_size = (diag_blocks.shape[0], diag_blocks.shape[1])
    rounded = vector.astype(jnp.bfloat16).reshape(block_count, block_size)
    result = material_scale(tissue_labels)[:, None] * jnp.einsum(
        "rij,rj->ri", diag_blocks, rounded, preferred_element_type=jnp.float32
    )
    gathered = rounded[block_pattern]
    result = result + jnp.einsum(
        "rkij,rkj->ri", couple_blocks, gathered, preferred_element_type=jnp.float32
    )
    backward = jnp.einsum(
        "rkij,ri->rkj", couple_blocks, rounded, preferred_element_type=jnp.float32
    )
    onehot = (block_pattern.reshape(-1)[:, None] == jnp.arange(block_count)[None, :]).astype(
        jnp.float32
    )
    result = result + jnp.einsum(
        "mc,mj->cj", onehot, backward.reshape(-1, block_size), precision=lax.Precision.HIGHEST
    )
    return result.reshape(-1)


def face_tables(face_map, block_count, block_size):
    flat = face_map.reshape(-1)
    rows = (flat[:, None] // block_size == jnp.arange(block_count)[None, :]).astype(jnp.float32)
    lanes = flat[:, None] % block_size == jnp.arange(block_size)[None, :]
    return rows, lanes


def gather_faces(vector, tables):
    rows, lanes = tables
    block_count = rows.shape[1]
    picked = jnp.dot(rows, vector.reshape(block_count, -1), precision=lax.Precision.HIGHEST)
    return jnp.sum(jnp.where(lanes, picked, 0.0), axis=1)


def scatter_faces(result, tables, contribution):
    rows, lanes = tables
    spread = jnp.where(lanes, contribution[:, None], 0.0)
    added = jnp.dot(rows.T, spread, precision=lax.Precision.HIGHEST)
    return result + added.reshape(-1)


def exchange_faces(values):
    across = extended(values[0:2], (("gx", 0),), 1)
    upward = extended(values[2:4], (("gy", 0),), 1)
    return jnp.stack([across[0], across[3], upward[0], upward[3]])


def sum_and_exchange_faces(partial, values):
    rows, cols = lax.axis_size("gx"), lax.axis_size("gy")
    row, col = lax.axis_index("gx"), lax.axis_index("gy")
    slots = jnp.arange(rows * cols)
    row_step = jnp.array([-1, 1, 0, 0])
    col_step = jnp.array([0, 0, -1, 1])
    near_row, near_col = row + row_step, col + col_step
    inside = (near_row >= 0) & (near_row < rows) & (near_col >= 0) & (near_col < cols)
    near = near_row * cols + near_col
    hits = (slots[:, None] == near[None, :]) & inside[None, :]
    outgoing = jnp.sum(jnp.where(hits[:, :, None], values[None], 0.0), axis=1)
    payload = jnp.concatenate(
        [jnp.broadcast_to(partial.reshape(1, 1), (rows * cols, 1)), outgoing], axis=1
    )
    got = lax.all_to_all(payload, ("gx", "gy"), 0, 0, tiled=True)
    incoming = jnp.sum(jnp.where(hits[:, :, None], got[:, None, 1:], 0.0), axis=0)
    return jnp.sum(got[:, 0]), incoming


def operate(vector, received, diag_blocks, couple_blocks, block_pattern, tissue_labels, tables):
    result = block_apply(vector, diag_blocks, couple_blocks, block_pattern, tissue_labels)
    contribution = -COUPLING * received.reshape(-1)
    return result, scatter_faces(result, tables, contribution), contribution


def precondition(residual, precond_blocks, tissue_labels, coarse_basis, live_cols, compliance):
    block_count, block_size = (precond_blocks.shape[0], precond_blocks.shape[1])
    rounded = residual.astype(jnp.bfloat16)
    product = jnp.einsum(
        "rij,rj->ri",
        precond_blocks,
        rounded.reshape(block_count, block_size),
        preferred_element_type=jnp.float32,
    )
    local_part = (product / material_scale(tissue_labels)[:, None]).reshape(-1)
    coarse_load = jnp.dot(rounded, coarse_basis, preferred_element_type=jnp.float32) * live_cols
    summed = exchange_sum(coarse_load, ("gx",))
    solved = jnp.dot(compliance, summed, precision=lax.Precision.HIGHEST)
    weights = (solved * live_cols).astype(jnp.bfloat16)
    return local_part + jnp.dot(coarse_basis, weights, preferred_element_type=jnp.float32)


def global_sum(value):
    return exchange_sum(value, ("gx", "gy"))


def body(
    right_side,
    coarse_matrix,
    coarse_order,
    diag_blocks,
    couple_blocks,
    block_pattern,
    tissue_labels,
    precond_blocks,
    coarse_basis,
    face_map,
):
    source = right_side[0, 0]
    matrix = coarse_matrix[0, 0]
    order_here = coarse_order[0, 0]
    diagonal = diag_blocks[0, 0]
    couples = couple_blocks[0, 0]
    pattern = block_pattern[0, 0]
    labels = tissue_labels[0, 0]
    inverses = precond_blocks[0, 0]
    basis = coarse_basis[0, 0]
    faces = face_map[0, 0]
    order_size = matrix.shape[-1]
    live_cols = (jnp.arange(order_size) < order_here).astype(jnp.float32)
    masked = masked_coarse(matrix, order_here)
    merged = merged_tree(masked, "gx", parallel_sum, "gy")
    compliance = newton_inverse(merged)
    adjoint = jnp.zeros_like(source)
    residual = source
    precond = precondition(residual, inverses, labels, basis, live_cols, compliance)
    direction = precond
    tables = face_tables(faces, diagonal.shape[0], diagonal.shape[1])
    face_count = faces.shape[0]
    faces_now = gather_faces(direction, tables)
    received = exchange_faces(faces_now.reshape(face_count, -1))
    for iteration in range(ITERS):
        local_image, applied, contribution = operate(
            direction, received, diagonal, couples, pattern, labels, tables
        )
        applied = lax.optimization_barrier(applied)
        products = [direction * local_image, contribution * faces_now]
        if iteration == 0:
            products = [residual * precond] + products
        parts = global_sum(jnp.sum(jnp.stack(products), axis=1))
        if iteration == 0:
            precond_dot = parts[0]
        curvature = parts[-2] + parts[-1]
        step_size = precond_dot / curvature
        adjoint = adjoint + step_size * direction
        residual = residual - step_size * applied
        if iteration + 1 < ITERS:
            precond = precondition(residual, inverses, labels, basis, live_cols, compliance)
            faces_precond = gather_faces(precond, tables)
            dot_next, received_precond = sum_and_exchange_faces(
                jnp.sum(residual * precond), faces_precond.reshape(face_count, -1)
            )
            ratio = dot_next / precond_dot
            direction = precond + ratio * direction
            faces_now = faces_precond + ratio * faces_now
            received = received_precond + ratio * received
            precond_dot = dot_next
    return (adjoint[None, None], residual[None, None])


def solution(mesh):
    in_specs = (
        P("gx", "gy", None),
        P("gx", "gy", None, None),
        P("gx", "gy"),
        P("gx", "gy", None, None, None),
        P("gx", "gy", None, None, None, None),
        P("gx", "gy", None, None),
        P("gx", "gy", None),
        P("gx", "gy", None, None, None),
        P("gx", "gy", None, None),
        P("gx", "gy", None, None),
    )
    out_specs = (P("gx", "gy", None), P("gx", "gy", None))
    return jax.shard_map(body, mesh=mesh, in_specs=in_specs, out_specs=out_specs, check_vma=False)
```
